32 devices in a mesh: group: 2 (over y), seq: 8 (over z, x), head: 2 (over core).
Axes of the slice: x: 2, y: 2, z: 4, core: 2. Of those that a mesh axis runs over, the one named last changes fastest.
Arguments:
- x_in: bfloat16 [4096, 4096], P(('group', 'seq'), 'head'), parts along dimension 0, may hold values from -6 to 6
- step_size: float32 [64, 4096], P('head', ('group', 'seq')), parts along dimension 1, may hold values from 0.002 to 0.128
- a_log: float32 [64], P('head'), may hold values from -8.5 to 0.9
- d_skip: float32 [64], P('head'), may hold values from 0.1 to 1.9
- b_in: bfloat16 [4096, 128], P(('group', 'seq')), parts along dimension 0, may hold values from -6 to 6
- c_in: bfloat16 [4096, 128], P(('group', 'seq')), parts along dimension 0, may hold values from -0.52734375 to 0.52734375
- queries: bfloat16 [4096, 2048], P(('group', 'seq'), 'head'), parts along dimension 0, may hold values from -4.5 to 4.5
- key_rows: bfloat16 [4096, 512], P(('group', 'seq'), 'head'), parts along dimension 0, may hold values from -4.5 to 4.5
- values: bfloat16 [4096, 512], P(('group', 'seq'), 'head'), parts along dimension 0, may hold values from -6 to 6
Outputs:
- mamba_out: bfloat16 [4096, 4096], P(('group', 'seq'), 'head'), parts along dimension 0
- attn_out: bfloat16 [4096, 2048], P(('group', 'seq'), 'head'), parts along dimension 0
The draws below stay inside these ranges and needn't reach their ends.
There are 2 independent parts, one for each index of `group`. The reference program is written for one: setup_inputs(seed, part) draws one part's arguments, and reference() takes and returns one part's arrays. A program takes and returns all parts, laid end to end along the dimension named above; an argument that names none is the same for every part. Nothing has to cross between parts.
All inputs are finite; a program needn't handle non-finite values.
Results may differ from the reference program's by a relative error of at most 0.009.
Values may be sent and summed in bfloat16 or wider, within the bound.
No kernel may reach another device: no remote copies, remote signals or barrier semaphores. Data moves between devices by JAX's collectives and lax.ppermute only.
A program may use at most 320 MiB of HBM per device.

```python
import jax
import jax.numpy as jnp
from jax import lax

BLOCK = 128
SLOTS = 2
MHEADS = 64
HEADDIM = 64
STATE = 128
QHEADS = 16
KVHEADS = 4
HD = 128
SEQLEN = 2048
N_SEQ = 8


def draw_step_size(key, part):
    base_log = jax.random.uniform(jax.random.fold_in(key, 41), (MHEADS, SEQLEN), jnp.float32, jnp.log(0.004), jnp.log(0.016))
    block_log = jax.random.uniform(jax.random.fold_in(key, 42), (MHEADS, SEQLEN // BLOCK), jnp.float32, jnp.log(0.5), jnp.log(8.0))
    block_log = jnp.repeat(block_log, BLOCK, axis=1)
    return jnp.exp(base_log + block_log)


def draw_queries(key, part):
    base = jnp.clip(jax.random.normal(jax.random.fold_in(key, 21), (SEQLEN, QHEADS * HD), jnp.float32), -4.5, 4.5)
    return base.astype(jnp.bfloat16)


def draw_key_rows(key, part):
    base = jnp.clip(jax.random.normal(jax.random.fold_in(key, 31), (SEQLEN, KVHEADS * HD), jnp.float32), -4.5, 4.5)
    return base.astype(jnp.bfloat16)


def block_scale(rng, extent, pieces, least, top_value):
    gain, own = 1.0, jax.random.fold_in(rng, 6)
    for axis_at, blocks in pieces:
        steps = jnp.exp(jax.random.uniform(jax.random.fold_in(own, axis_at), (blocks,), jnp.float32, least / len(pieces), top_value / len(pieces)))
        gain = gain * jnp.repeat(steps, extent[axis_at] // blocks).reshape([-1 if axis == axis_at else 1 for axis in range(len(extent))])
    return gain


def scatter_about(own_key, dims, spread, limit, split=(), held_as=jnp.bfloat16):
    entries = spread * jax.random.normal(own_key, dims, jnp.float32)
    if split:
        entries = entries * block_scale(own_key, dims, split, -0.22, 0.18)
    return jnp.clip(entries, -limit, limit).astype(held_as)


def setup_inputs(seed: int = 0, part: int = 0) -> dict:
    streams_of = jax.random.split(jax.random.key(seed), 10)
    own_keys = jax.random.split(jax.random.fold_in(streams_of[9], part), 10)
    x_in = scatter_about(own_keys[0], (SEQLEN, MHEADS * HEADDIM), 1.0, 6.0, ((0, 8), (1, 2)))
    step_size = draw_step_size(jax.random.fold_in(jax.random.fold_in(streams_of[9], part), 71), part)
    a_log = jnp.clip(-8.5 + 9.4 * jax.random.uniform(streams_of[2], (MHEADS,), jnp.float32) ** block_scale(streams_of[2], (MHEADS,), ((0, 2),), -0.2, 0.2), -8.5, 0.9)
    d_skip = jnp.clip(1.0 + 0.18 * jax.random.normal(streams_of[3], (MHEADS,), jnp.float32), 0.1, 1.9)
    b_in = scatter_about(own_keys[4], (SEQLEN, STATE), 1.0, 6.0, ((0, 8),))
    c_in = scatter_about(own_keys[5], (SEQLEN, STATE), (STATE ** -0.5), 0.52734375, ((0, 8),))
    queries = draw_queries(jax.random.fold_in(jax.random.fold_in(streams_of[9], part), 71), part)
    key_rows = draw_key_rows(jax.random.fold_in(jax.random.fold_in(streams_of[9], part), 71), part)
    values = scatter_about(own_keys[8], (SEQLEN, KVHEADS * HD), 1.0, 6.0, ((0, 8), (1, 2)))
    return {"x_in": x_in, "step_size": step_size, "a_log": a_log, "d_skip": d_skip, "b_in": b_in, "c_in": c_in, "queries": queries, "key_rows": key_rows, "values": values}


NEG = -1e30


def to_global(array):
    width = array.shape[1]
    return array.reshape(N_SEQ, SLOTS, BLOCK, width).transpose(1, 0, 2, 3).reshape(N_SEQ * SLOTS * BLOCK, width)


def from_global(array):
    width = array.shape[1]
    return array.reshape(SLOTS, N_SEQ, BLOCK, width).transpose(1, 0, 2, 3).reshape(N_SEQ * SLOTS * BLOCK, width)


def ssd_local(x_blocks, steps, rate, b_blocks, c_blocks):
    cum = jnp.cumsum(steps * rate[None, :, None], axis=2)
    causal = jnp.arange(BLOCK)[:, None] >= jnp.arange(BLOCK)[None, :]
    log_gap = jnp.where(causal, cum[:, :, :, None] - cum[:, :, None, :], -jnp.inf)
    inner = jnp.einsum("cin,cjn->cij", c_blocks.astype(jnp.float32), b_blocks.astype(jnp.float32))
    mixing = (inner[:, None] * jnp.exp(log_gap) * steps[:, :, None, :]).astype(jnp.bfloat16)
    intra = jnp.einsum("chij,cjhp->cihp", mixing.astype(jnp.float32), x_blocks.astype(jnp.float32))
    log_total = cum[:, :, -1]
    factor = (jnp.exp(log_total[:, :, None] - cum) * steps).transpose(0, 2, 1)[..., None]
    scaled = (factor * x_blocks.astype(jnp.float32)).astype(jnp.bfloat16)
    block_state = jnp.einsum("cjhp,cjn->chpn", scaled.astype(jnp.float32), b_blocks.astype(jnp.float32))
    return intra, block_state, log_total, cum


def ssd_finish(intra, cum, c_blocks, incoming, d_skip, x_blocks):
    carried = jnp.einsum("cin,chpn->cihp", c_blocks.astype(jnp.float32), incoming, precision=lax.Precision.HIGHEST)
    carried = carried * jnp.exp(cum).transpose(0, 2, 1)[..., None]
    return (intra + carried + d_skip[None, None, :, None] * x_blocks.astype(jnp.float32)).astype(jnp.bfloat16)


def reference(x_in, step_size, a_log, d_skip, b_in, c_in, queries, key_rows, values):
    count = N_SEQ * SLOTS
    total = count * BLOCK
    rate = -jnp.exp(a_log)
    x_glob = to_global(x_in).reshape(count, 1, BLOCK, MHEADS, HEADDIM)
    step_glob = to_global(step_size.T).reshape(count, 1, BLOCK, MHEADS).transpose(0, 1, 3, 2)
    b_glob = to_global(b_in).reshape(count, 1, BLOCK, STATE)
    c_glob = to_global(c_in).reshape(count, 1, BLOCK, STATE)

    def advance(state, inputs):
        x_blocks, steps, b_blocks, c_blocks = inputs
        intra, block_state, log_total, cum = ssd_local(x_blocks, steps, rate, b_blocks, c_blocks)
        output = ssd_finish(intra, cum, c_blocks, state[None], d_skip, x_blocks)
        state = jnp.exp(log_total[0])[:, None, None] * state + block_state[0]
        return state, output

    start_state = jnp.zeros((MHEADS, HEADDIM, STATE), jnp.float32)
    unused, outputs = lax.scan(advance, start_state, (x_glob, step_glob, b_glob, c_glob))
    mamba_out = from_global(outputs.reshape(total, MHEADS * HEADDIM))

    per_kv = QHEADS // KVHEADS
    q_glob = to_global(queries).reshape(total, KVHEADS, per_kv, HD)
    k_glob = to_global(key_rows).reshape(total, KVHEADS, HD).astype(jnp.float32)
    v_glob = to_global(values).reshape(total, KVHEADS, HD).astype(jnp.float32)
    score_scale = 1.0 / (HD ** 0.5)
    key_pos = jnp.arange(total).astype(jnp.int32)

    def attend(number):
        first = (number * BLOCK).astype(jnp.int32)
        q_block = lax.dynamic_slice_in_dim(q_glob, first, BLOCK, 0).astype(jnp.float32)
        scores = jnp.einsum("ihgd,jhd->hgij", q_block, k_glob) * score_scale
        query_pos = first + jnp.arange(BLOCK).astype(jnp.int32)
        visible = key_pos[None, :] <= query_pos[:, None]
        scores = jnp.where(visible, scores, NEG)
        top = jnp.max(scores, axis=-1, keepdims=True)
        probs = jnp.where(visible, jnp.exp(scores - top), 0.0)
        denom = jnp.sum(probs, axis=-1)
        probs_low = probs.astype(jnp.bfloat16).astype(jnp.float32)
        mixed = jnp.einsum("hgij,jhd->ihgd", probs_low, v_glob)
        mixed = mixed / denom.transpose(2, 0, 1)[..., None]
        return mixed.astype(jnp.bfloat16).reshape(BLOCK, QHEADS * HD)

    attended = lax.map(attend, jnp.arange(count).astype(jnp.int32))
    attn_out = from_global(attended.reshape(total, QHEADS * HD))
    return mamba_out, attn_out
```

```python
import jax
import jax.numpy as jnp
from jax import lax
from jax.sharding import PartitionSpec as P

BLOCK = 128
HEADDIM = 64
STATE = 128
QHEADS = 16
KVHEADS = 4
HD = 128


NEG = -1e30


def combine_if(lower, earlier, later):
    a_e, s_e = earlier
    a_l, s_l = later
    joined_a = a_e * a_l
    joined_s = a_l[..., None, None] * s_e + s_l
    return (jnp.where(lower, joined_a, a_l), jnp.where(lower, joined_s, s_l))


def exchange(value, axis, pairs):
    decay, state = value
    got_decay = lax.ppermute(decay, axis, pairs)
    got_state = lax.ppermute(state.astype(jnp.bfloat16), axis, pairs).astype(jnp.float32)
    return (got_decay, got_state)


def entering_states(decay, block_state, count, mine):
    slots = decay.shape[0]
    excl = (jnp.ones_like(decay), jnp.zeros_like(block_state))
    total = (decay, block_state)
    span = 1
    while span < count:
        lower = (mine // span) % 2 == 1
        last = span * 2 >= count
        pairs = [(i, i ^ span) for i in range(count)]
        if last and slots > 1:
            head = exchange(jax.tree.map(lambda v: v[:-1], total), "seq", pairs)
            up_pairs = [(i, i ^ span) for i in range(count) if (i // span) % 2 == 0]
            tail = exchange(jax.tree.map(lambda v: v[-1:], total), "seq", up_pairs)
            got = jax.tree.map(lambda a, b: jnp.concatenate([a, b], axis=0), head, tail)
        else:
            got = exchange(total, "seq", pairs)
        excl = combine_if(lower, got, excl)
        joined_low = combine_if(lower, got, total)
        joined_high = (total[0] * got[0], got[0][..., None, None] * total[1] + got[1])
        total = (
            jnp.where(lower, joined_low[0], joined_high[0]),
            jnp.where(lower, joined_low[1], joined_high[1]),
        )
        span *= 2
    carry = jnp.zeros_like(block_state[0])
    entering = []
    for slot in range(slots):
        entering.append(excl[0][slot][:, None, None] * carry + excl[1][slot])
        carry = total[0][slot][:, None, None] * carry + total[1][slot]
    return jnp.stack(entering, axis=0)


def ssd_local(x_blocks, steps, rate, b_blocks, c_blocks):
    cum = jnp.cumsum(steps * rate[None, :, None], axis=2)
    causal = jnp.arange(BLOCK)[:, None] >= jnp.arange(BLOCK)[None, :]
    log_gap = jnp.where(causal, cum[:, :, :, None] - cum[:, :, None, :], -jnp.inf)
    inner = jnp.einsum("cin,cjn->cij", c_blocks, b_blocks, preferred_element_type=jnp.float32)
    mixing = (inner[:, None] * jnp.exp(log_gap) * steps[:, :, None, :]).astype(jnp.bfloat16)
    intra = jnp.einsum("chij,cjhp->cihp", mixing, x_blocks, preferred_element_type=jnp.float32)
    log_total = cum[:, :, -1]
    factor = (jnp.exp(log_total[:, :, None] - cum) * steps).transpose(0, 2, 1)[..., None]
    scaled = (factor * x_blocks.astype(jnp.float32)).astype(jnp.bfloat16)
    block_state = jnp.einsum("cjhp,cjn->chpn", scaled, b_blocks, preferred_element_type=jnp.float32)
    return (intra, block_state, log_total, cum)


def ssd_finish(intra, cum, c_blocks, incoming, d_skip, x_blocks):
    carried = jnp.einsum(
        "cin,chpn->cihp", c_blocks.astype(jnp.float32), incoming, precision=lax.Precision.HIGHEST
    )
    carried = carried * jnp.exp(cum).transpose(0, 2, 1)[..., None]
    return (intra + carried + d_skip[None, None, :, None] * x_blocks.astype(jnp.float32)).astype(
        jnp.bfloat16
    )


def local(x_in, step_size, a_log, d_skip, b_in, c_in, queries, key_rows, values):
    my_index = lax.axis_index("seq")
    seq_count = lax.axis_size("seq")
    tok_rows = x_in.shape[0]
    slots = tok_rows // BLOCK
    mamba_local = step_size.shape[0]
    rate = -jnp.exp(a_log)
    x_blocks = x_in.reshape(slots, BLOCK, mamba_local, HEADDIM)
    steps = step_size.reshape(mamba_local, slots, BLOCK).transpose(1, 0, 2)
    b_blocks = b_in.reshape(slots, BLOCK, STATE)
    c_blocks = c_in.reshape(slots, BLOCK, STATE)
    intra, block_state, log_total, cum = ssd_local(x_blocks, steps, rate, b_blocks, c_blocks)
    decay = jnp.exp(log_total)
    incoming = entering_states(decay, block_state, seq_count, my_index)
    mamba_out = ssd_finish(intra, cum, c_blocks, incoming, d_skip, x_blocks).reshape(
        tok_rows, mamba_local * HEADDIM
    )
    per_kv = QHEADS // KVHEADS
    kv_local = key_rows.shape[1] // HD
    score_scale = 1.0 / HD**0.5
    stride = seq_count * BLOCK
    q_flat = queries.reshape(slots, BLOCK, kv_local, per_kv, HD).transpose(2, 0, 3, 1, 4)
    q_flat = q_flat.reshape(kv_local, slots * per_kv * BLOCK, HD)
    q_slot = jnp.arange(slots)[:, None, None]
    q_row = jnp.arange(BLOCK)[None, None, :]
    query_pos = (
        q_slot * stride + my_index * BLOCK + q_row + jnp.zeros((slots, per_kv, BLOCK), jnp.int32)
    ).reshape(-1)
    k_slots = key_rows.reshape(slots, BLOCK, kv_local * HD)
    v_slots = values.reshape(slots, BLOCK, kv_local * HD)
    q_total = slots * per_kv * BLOCK
    start_state = (
        jnp.full((kv_local, q_total), NEG, jnp.float32),
        jnp.zeros((kv_local, q_total), jnp.float32),
        jnp.zeros((kv_local, q_total, HD), jnp.float32),
    )
    running = start_state
    kv_piece = lax.all_gather(jnp.concatenate([k_slots, v_slots], axis=2), "seq", axis=1, tiled=True)
    k_piece = kv_piece[..., : kv_local * HD]
    v_piece = kv_piece[..., kv_local * HD :]
    rows = k_piece.shape[1]
    block_rows = 512
    count = rows // block_rows
    k_blocks = k_piece.reshape(slots, count, block_rows, kv_local, HD).transpose(1, 0, 2, 3, 4)
    v_blocks = v_piece.reshape(slots, count, block_rows, kv_local, HD).transpose(1, 0, 2, 3, 4)
    k_slot = jnp.arange(slots)[:, None]
    k_row = jnp.arange(block_rows)[None, :]

    def per_block(state, inputs):
        k_block, v_block, number = inputs
        run_max, run_sum, run_acc = state
        k_flat = k_block.reshape(slots * block_rows, kv_local, HD)
        v_flat = v_block.reshape(slots * block_rows, kv_local, HD)
        key_pos = (k_slot * stride + number * block_rows + k_row).reshape(-1)
        visible = key_pos[None, None, :] <= query_pos[None, :, None]
        scores = (
            jnp.einsum("gqd,kgd->gqk", q_flat, k_flat, preferred_element_type=jnp.float32)
            * score_scale
        )
        scores = jnp.where(visible, scores, NEG)
        new_max = jnp.maximum(run_max, jnp.max(scores, axis=-1))
        rescale = jnp.exp(run_max - new_max)
        weights = jnp.where(visible, jnp.exp(scores - new_max[..., None]), 0.0)
        new_sum = run_sum * rescale + jnp.sum(weights, axis=-1)
        update = jnp.einsum(
            "gqk,kgd->gqd", weights.astype(jnp.bfloat16), v_flat, preferred_element_type=jnp.float32
        )
        return ((new_max, new_sum, run_acc * rescale[..., None] + update), None)

    numbers = jnp.arange(count)
    running, unused = lax.scan(per_block, running, (k_blocks, v_blocks, numbers))
    run_max, run_sum, run_acc = running
    attended = (run_acc / run_sum[..., None]).astype(jnp.bfloat16)
    attn_out = (
        attended.reshape(kv_local, slots, per_kv, BLOCK, HD)
        .transpose(1, 3, 0, 2, 4)
        .reshape(tok_rows, kv_local * per_kv * HD)
    )
    return (mamba_out, attn_out)


def solution(mesh):
    in_specs = (
        P(("group", "seq"), "head"),
        P("head", ("group", "seq")),
        P("head"),
        P("head"),
        P(("group", "seq"), None),
        P(("group", "seq"), None),
        P(("group", "seq"), "head"),
        P(("group", "seq"), "head"),
        P(("group", "seq"), "head"),
    )
    out_specs = (P(("group", "seq"), "head"), P(("group", "seq"), "head"))
    return jax.shard_map(local, mesh=mesh, in_specs=in_specs, out_specs=out_specs, check_vma=False)
```

```python
import jax
import jax.numpy as jnp
from jax import lax
from jax.sharding import PartitionSpec as P

BLOCK = 128
HEADDIM = 64
STATE = 128
QHEADS = 16
KVHEADS = 4
HD = 128


NEG = -1e30


def combine_if(lower, earlier, later):
    a_e, s_e = earlier
    a_l, s_l = later
    joined_a = a_e * a_l
    joined_s = a_l[..., None, None] * s_e + s_l
    return (jnp.where(lower, joined_a, a_l), jnp.where(lower, joined_s, s_l))


def exchange(value, axis, pairs):
    decay, state = value
    got_decay = lax.ppermute(decay, axis, pairs)
    got_state = lax.ppermute(state.astype(jnp.bfloat16), axis, pairs).astype(jnp.float32)
    return (got_decay, got_state)


def entering_states(decay, block_state, count, mine, inside, inside_args):
    slots = decay.shape[0]
    excl = (jnp.ones_like(decay), jnp.zeros_like(block_state))
    total = (decay, block_state)
    span = 1
    while span < count:
        lower = (mine // span) % 2 == 1
        last = span * 2 >= count
        pairs = [(i, i ^ span) for i in range(count)]
        if last:
            total, inside_args = lax.optimization_barrier((total, inside_args))
        got = exchange(total, "seq", pairs)
        if last:
            covered = inside(*inside_args)
            got, covered = lax.optimization_barrier((got, covered))
        excl = combine_if(lower, got, excl)
        joined_low = combine_if(lower, got, total)
        joined_high = (total[0] * got[0], got[0][..., None, None] * total[1] + got[1])
        total = (
            jnp.where(lower, joined_low[0], joined_high[0]),
            jnp.where(lower, joined_low[1], joined_high[1]),
        )
        span *= 2
    carry = jnp.zeros_like(block_state[0])
    entering = []
    for slot in range(slots):
        entering.append(excl[0][slot][:, None, None] * carry + excl[1][slot])
        carry = total[0][slot][:, None, None] * carry + total[1][slot]
    return (jnp.stack(entering, axis=0), covered)


def ssd_local(x_blocks, steps, rate, b_blocks, c_blocks):
    cum = jnp.cumsum(steps * rate[None, :, None], axis=2)
    causal = jnp.arange(BLOCK)[:, None] >= jnp.arange(BLOCK)[None, :]
    log_gap = jnp.where(causal, cum[:, :, :, None] - cum[:, :, None, :], -jnp.inf)
    inner = jnp.einsum("cin,cjn->cij", c_blocks, b_blocks, preferred_element_type=jnp.float32)
    mixing = (inner[:, None] * jnp.exp(log_gap) * steps[:, :, None, :]).astype(jnp.bfloat16)
    intra = jnp.einsum("chij,cjhp->cihp", mixing, x_blocks, preferred_element_type=jnp.float32)
    log_total = cum[:, :, -1]
    factor = (jnp.exp(log_total[:, :, None] - cum) * steps).transpose(0, 2, 1)[..., None]
    scaled = (factor * x_blocks.astype(jnp.float32)).astype(jnp.bfloat16)
    block_state = jnp.einsum("cjhp,cjn->chpn", scaled, b_blocks, preferred_element_type=jnp.float32)
    return (intra, block_state, log_total, cum)


def ssd_finish(intra, cum, c_blocks, incoming, d_skip, x_blocks):
    carried = jnp.einsum(
        "cin,chpn->cihp", c_blocks.astype(jnp.float32), incoming, precision=lax.Precision.HIGHEST
    )
    carried = carried * jnp.exp(cum).transpose(0, 2, 1)[..., None]
    return (intra + carried + d_skip[None, None, :, None] * x_blocks.astype(jnp.float32)).astype(
        jnp.bfloat16
    )


def attention(queries, kv_piece, my_index):
    seq_count = lax.axis_size("seq")
    tok_rows = queries.shape[0]
    slots = tok_rows // BLOCK
    kv_local = kv_piece.shape[2] // (2 * HD)
    per_kv = QHEADS // KVHEADS
    score_scale = 1.0 / HD**0.5
    stride = seq_count * BLOCK
    q_flat = queries.reshape(slots, BLOCK, kv_local, per_kv, HD).transpose(2, 0, 3, 1, 4)
    q_flat = q_flat.reshape(kv_local, slots * per_kv * BLOCK, HD)
    q_slot = jnp.arange(slots)[:, None, None]
    q_row = jnp.arange(BLOCK)[None, None, :]
    query_pos = (
        q_slot * stride + my_index * BLOCK + q_row + jnp.zeros((slots, per_kv, BLOCK), jnp.int32)
    ).reshape(-1)
    q_total = slots * per_kv * BLOCK
    start_state = (
        jnp.full((kv_local, q_total), NEG, jnp.float32),
        jnp.zeros((kv_local, q_total), jnp.float32),
        jnp.zeros((kv_local, q_total, HD), jnp.float32),
    )
    running = start_state
    k_piece = kv_piece[..., : kv_local * HD]
    v_piece = kv_piece[..., kv_local * HD :]
    rows = k_piece.shape[1]
    block_rows = 512
    count = rows // block_rows
    k_blocks = k_piece.reshape(slots, count, block_rows, kv_local, HD).transpose(1, 0, 2, 3, 4)
    v_blocks = v_piece.reshape(slots, count, block_rows, kv_local, HD).transpose(1, 0, 2, 3, 4)
    k_slot = jnp.arange(slots)[:, None]
    k_row = jnp.arange(block_rows)[None, :]

    def per_block(state, inputs):
        k_block, v_block, number = inputs
        run_max, run_sum, run_acc = state
        k_flat = k_block.reshape(slots * block_rows, kv_local, HD)
        v_flat = v_block.reshape(slots * block_rows, kv_local, HD)
        key_pos = (k_slot * stride + number * block_rows + k_row).reshape(-1)
        visible = key_pos[None, None, :] <= query_pos[None, :, None]
        scores = (
            jnp.einsum("gqd,kgd->gqk", q_flat, k_flat, preferred_element_type=jnp.float32)
            * score_scale
        )
        scores = jnp.where(visible, scores, NEG)
        new_max = jnp.maximum(run_max, jnp.max(scores, axis=-1))
        rescale = jnp.exp(run_max - new_max)
        weights = jnp.where(visible, jnp.exp(scores - new_max[..., None]), 0.0)
        new_sum = run_sum * rescale + jnp.sum(weights, axis=-1)
        update = jnp.einsum(
            "gqk,kgd->gqd", weights.astype(jnp.bfloat16), v_flat, preferred_element_type=jnp.float32
        )
        return ((new_max, new_sum, run_acc * rescale[..., None] + update), None)

    numbers = jnp.arange(count)
    running, unused = lax.scan(per_block, running, (k_blocks, v_blocks, numbers), unroll=True)
    run_max, run_sum, run_acc = running
    attended = (run_acc / run_sum[..., None]).astype(jnp.bfloat16)
    attn_out = (
        attended.reshape(kv_local, slots, per_kv, BLOCK, HD)
        .transpose(1, 3, 0, 2, 4)
        .reshape(tok_rows, kv_local * per_kv * HD)
    )
    return attn_out


def local(x_in, step_size, a_log, d_skip, b_in, c_in, queries, key_rows, values):
    my_index = lax.axis_index("seq")
    seq_count = lax.axis_size("seq")
    slots_kv = key_rows.shape[0] // BLOCK
    width_kv = key_rows.shape[1]
    kv_cat = jnp.concatenate(
        [key_rows.reshape(slots_kv, BLOCK, width_kv), values.reshape(slots_kv, BLOCK, width_kv)], axis=2
    )
    kv_cat, x_in, step_size = lax.optimization_barrier((kv_cat, x_in, step_size))
    kv_piece = lax.all_gather(kv_cat, "seq", axis=1, tiled=True)
    tok_rows = x_in.shape[0]
    slots = tok_rows // BLOCK
    mamba_local = step_size.shape[0]
    rate = -jnp.exp(a_log)
    x_blocks = x_in.reshape(slots, BLOCK, mamba_local, HEADDIM)
    steps = step_size.reshape(mamba_local, slots, BLOCK).transpose(1, 0, 2)
    b_blocks = b_in.reshape(slots, BLOCK, STATE)
    c_blocks = c_in.reshape(slots, BLOCK, STATE)
    intra, block_state, log_total, cum = ssd_local(x_blocks, steps, rate, b_blocks, c_blocks)
    decay = jnp.exp(log_total)
    incoming, attn_out = entering_states(
        decay, block_state, seq_count, my_index, attention, (queries, kv_piece, my_index)
    )
    mamba_out = ssd_finish(intra, cum, c_blocks, incoming, d_skip, x_blocks).reshape(
        tok_rows, mamba_local * HEADDIM
    )
    return (mamba_out, attn_out)


def solution(mesh):
    in_specs = (
        P(("group", "seq"), "head"),
        P("head", ("group", "seq")),
        P("head"),
        P("head"),
        P(("group", "seq"), None),
        P(("group", "seq"), None),
        P(("group", "seq"), "head"),
        P(("group", "seq"), "head"),
        P(("group", "seq"), "head"),
    )
    out_specs = (P(("group", "seq"), "head"), P(("group", "seq"), "head"))
    return jax.shard_map(local, mesh=mesh, in_specs=in_specs, out_specs=out_specs, check_vma=False)
```

```python
import jax
import jax.numpy as jnp
from jax import lax
from jax.experimental import pallas as pl
from jax.experimental.pallas import tpu as pltpu
from jax.sharding import PartitionSpec as P

BLOCK = 128
HEADDIM = 64
STATE = 128
QHEADS = 16
KVHEADS = 4
HD = 128


NEG = -1e30


def spread(a):
    return jnp.repeat(a, HEADDIM, axis=-1)


def combine_if(lower, earlier, later):
    a_e, s_e = earlier
    a_l, s_l = later
    joined_a = a_e * a_l
    joined_s = spread(a_l)[:, None, :] * s_e + s_l
    return (jnp.where(lower, joined_a, a_l), jnp.where(lower, joined_s, s_l))


def exchange(value, axis, pairs):
    decay, state = value
    spread_decay = spread(decay)[:, None, :]
    high = spread_decay.astype(jnp.bfloat16)
    low = (spread_decay - high.astype(jnp.float32)).astype(jnp.bfloat16)
    pad = jnp.zeros((state.shape[0], 6, state.shape[2]), jnp.bfloat16)
    sent = jnp.concatenate([state.astype(jnp.bfloat16), high, low, pad], axis=1)
    got = lax.ppermute(sent, axis, pairs)
    rows = state.shape[1]
    got_decay = got[:, rows, ::HEADDIM].astype(jnp.float32) + got[:, rows + 1, ::HEADDIM].astype(jnp.float32)
    return (got_decay, got[:, :rows].astype(jnp.float32))


def entering_states(decay, block_state, count, mine, hooks):
    slots = decay.shape[0]
    excl = (jnp.ones_like(decay), jnp.zeros_like(block_state))
    total = (decay, block_state)
    results = {}
    span, step = 1, 0
    while span < count:
        lower = (mine // span) % 2 == 1
        pairs = [(i, i ^ span) for i in range(count)]
        hook = hooks.get(step if span * 2 < count else -1)
        if hook is not None:
            total, args = lax.optimization_barrier((total, hook[1]))
        got = exchange(total, "seq", pairs)
        if hook is not None:
            done = hook[0](*args)
            got, done = lax.optimization_barrier((got, done))
            results[hook[0].__name__] = done
        excl = combine_if(lower, got, excl)
        joined_low = combine_if(lower, got, total)
        joined_high = (total[0] * got[0], spread(got[0])[:, None, :] * total[1] + got[1])
        total = (
            jnp.where(lower, joined_low[0], joined_high[0]),
            jnp.where(lower, joined_low[1], joined_high[1]),
        )
        span, step = span * 2, step + 1
    carry = jnp.zeros_like(block_state[0])
    entering = []
    for slot in range(slots):
        entering.append(spread(excl[0][slot])[None, :] * carry + excl[1][slot])
        carry = spread(total[0][slot])[None, :] * carry + total[1][slot]
    return (jnp.stack(entering, axis=0), results)


def mamba_base(x_in, steps, cum, b_blocks, c_blocks, d_skip):
    slots, heads = steps.shape[:2]
    x_blocks = x_in.reshape(slots, BLOCK, heads, HEADDIM)
    causal = jnp.arange(BLOCK)[:, None] >= jnp.arange(BLOCK)[None, :]
    log_gap = jnp.where(causal, cum[:, :, :, None] - cum[:, :, None, :], -jnp.inf)
    inner = jnp.einsum("cin,cjn->cij", c_blocks, b_blocks, preferred_element_type=jnp.float32)
    mixing = (inner[:, None] * jnp.exp(log_gap) * steps[:, :, None, :]).astype(jnp.bfloat16)
    intra = jnp.einsum("chij,cjhp->cihp", mixing, x_blocks, preferred_element_type=jnp.float32)
    base = intra + d_skip[None, None, :, None] * x_blocks.astype(jnp.float32)
    return base.reshape(slots, BLOCK, heads * HEADDIM)


KEY_CHUNK = 256


def attention_prep(queries, kv_piece, my_index):
    tok_rows = queries.shape[0]
    slots = tok_rows // BLOCK
    kv_local = kv_piece.shape[2] // (2 * HD)
    per_kv = QHEADS // KVHEADS
    q_flat = queries.reshape(slots, BLOCK, kv_local, per_kv, HD).transpose(2, 0, 3, 1, 4)
    q_flat = q_flat.reshape(kv_local, slots * per_kv * BLOCK, HD)
    rows = kv_piece.shape[0] * kv_piece.shape[1]
    k_all = kv_piece[..., : kv_local * HD].reshape(rows, kv_local, HD).transpose(1, 0, 2)
    v_all = kv_piece[..., kv_local * HD :].reshape(rows, kv_local, HD).transpose(1, 0, 2)
    return (q_flat, k_all, v_all)


def attention_kernel(q_ref, k_ref, v_ref, o_ref):
    seq_count = lax.axis_size("seq")
    me = lax.axis_index("seq")
    slot = pl.program_id(1)
    rows = q_ref.shape[1]
    first = (slot * seq_count + me) * BLOCK
    chunks = (first + BLOCK + KEY_CHUNK - 1) // KEY_CHUNK
    q = q_ref[0]
    query_pos = first + lax.broadcasted_iota(jnp.int32, (rows, KEY_CHUNK), 0) % BLOCK
    key_col = lax.broadcasted_iota(jnp.int32, (rows, KEY_CHUNK), 1)
    score_scale = 1.0 / HD**0.5

    def scores(c):
        start = pl.multiple_of(c * KEY_CHUNK, KEY_CHUNK)
        k = k_ref[0, pl.ds(start, KEY_CHUNK), :]
        s = lax.dot_general(q, k, (((1,), (1,)), ((), ())), preferred_element_type=jnp.float32)
        visible = start + key_col <= query_pos
        return s * score_scale, visible, start

    def top_of(c, top):
        s, visible, unused = scores(c)
        return jnp.maximum(top, jnp.max(jnp.where(visible, s, NEG), axis=1, keepdims=True))

    top = lax.fori_loop(0, chunks, top_of, jnp.full((rows, 1), NEG, jnp.float32))

    def add_of(c, carry):
        total, acc = carry
        s, visible, start = scores(c)
        probs = jnp.where(visible, jnp.exp(s - top), 0.0)
        v = v_ref[0, pl.ds(start, KEY_CHUNK), :]
        acc = acc + jnp.dot(probs.astype(jnp.bfloat16), v, preferred_element_type=jnp.float32)
        return (total + jnp.sum(probs, axis=1, keepdims=True), acc)

    start_carry = (jnp.zeros((rows, 1), jnp.float32), jnp.zeros((rows, HD), jnp.float32))
    total, acc = lax.fori_loop(0, chunks, add_of, start_carry)
    o_ref[0] = (acc / total).astype(o_ref.dtype)


def attention_core(q_flat, k_all, v_all):
    groups, q_total, unused = q_flat.shape
    keys = k_all.shape[1]
    slots = q_total // ((QHEADS // KVHEADS) * BLOCK)
    block_q = q_total // slots
    cost = pl.CostEstimate(
        flops=4 * groups * q_total * keys * HD,
        transcendentals=groups * q_total * keys,
        bytes_accessed=2 * (2 * q_flat.size + k_all.size + v_all.size),
    )
    attended = pl.pallas_call(
        attention_kernel,
        out_shape=jax.ShapeDtypeStruct(q_flat.shape, jnp.bfloat16),
        grid=(groups, slots),
        in_specs=[
            pl.BlockSpec((1, block_q, HD), lambda g, s: (g, s, 0)),
            pl.BlockSpec((1, keys, HD), lambda g, s: (g, 0, 0)),
            pl.BlockSpec((1, keys, HD), lambda g, s: (g, 0, 0)),
        ],
        out_specs=pl.BlockSpec((1, block_q, HD), lambda g, s: (g, s, 0)),
        cost_estimate=cost,
    )(q_flat, k_all, v_all)
    per_kv = QHEADS // KVHEADS
    return (
        attended.reshape(groups, slots, per_kv, BLOCK, HD)
        .transpose(1, 3, 0, 2, 4)
        .reshape(slots * BLOCK, groups * per_kv * HD)
    )


def local(x_in, step_size, a_log, d_skip, b_in, c_in, queries, key_rows, values):
    my_index = lax.axis_index("seq")
    seq_count = lax.axis_size("seq")
    tok_rows, width = x_in.shape
    slots = tok_rows // BLOCK
    heads = step_size.shape[0]
    kv_cat = jnp.concatenate(
        [key_rows.reshape(slots, BLOCK, -1), values.reshape(slots, BLOCK, -1)], axis=2
    )
    kv_cat, x_in, step_size = lax.optimization_barrier((kv_cat, x_in, step_size))
    kv_piece = lax.all_gather(kv_cat, "seq", axis=1, tiled=True)
    rate = -jnp.exp(a_log)
    steps = step_size.reshape(heads, slots, BLOCK).transpose(1, 0, 2)
    cum = jnp.cumsum(steps * rate[None, :, None], axis=2)
    log_total = cum[:, :, -1]
    factor = (jnp.exp(log_total[:, :, None] - cum) * steps).transpose(0, 2, 1)
    x3 = x_in.reshape(slots, BLOCK, width)
    scaled = (spread(factor) * x3.astype(jnp.float32)).astype(jnp.bfloat16)
    b_blocks = b_in.reshape(slots, BLOCK, STATE)
    c_blocks = c_in.reshape(slots, BLOCK, STATE)
    block_state = jnp.einsum("ctn,ctk->cnk", b_blocks, scaled, preferred_element_type=jnp.float32)
    decay = jnp.exp(log_total)
    prepared = attention_prep(queries, kv_piece, my_index)
    hooks = {
        0: (mamba_base, (x_in, steps, cum, b_blocks, c_blocks, d_skip)),
        -1: (attention_core, prepared),
    }
    incoming, results = entering_states(decay, block_state, seq_count, my_index, hooks)
    carried = jnp.einsum(
        "ctn,cnk->ctk", c_blocks.astype(jnp.float32), incoming, precision=lax.Precision.HIGHEST
    )
    carried = carried * spread(jnp.exp(cum).transpose(0, 2, 1))
    mamba_out = (results["mamba_base"] + carried).astype(jnp.bfloat16).reshape(tok_rows, width)
    return (mamba_out, results["attention_core"])


def solution(mesh):
    in_specs = (
        P(("group", "seq"), "head"),
        P("head", ("group", "seq")),
        P("head"),
        P("head"),
        P(("group", "seq"), None),
        P(("group", "seq"), None),
        P(("group", "seq"), "head"),
        P(("group", "seq"), "head"),
        P(("group", "seq"), "head"),
    )
    out_specs = (P(("group", "seq"), "head"), P(("group", "seq"), "head"))
    return jax.shard_map(local, mesh=mesh, in_specs=in_specs, out_specs=out_specs, check_vma=False)
```

```python
import jax
import jax.numpy as jnp
from jax import lax
from jax.experimental import pallas as pl
from jax.experimental.pallas import tpu as pltpu
from jax.sharding import PartitionSpec as P

BLOCK = 128
HEADDIM = 64
STATE = 128
QHEADS = 16
KVHEADS = 4
HD = 128


NEG = -1e30


def spread(a):
    return jnp.repeat(a, HEADDIM, axis=-1)


def decay_scan(decay, count, mine):
    excl = jnp.ones_like(decay)
    total = decay
    steps = []
    span = 1
    while span < count:
        lower = (mine // span) % 2 == 1
        got = lax.ppermute(total, "seq", [(i, i ^ span) for i in range(count)])
        steps.append((lower, excl, total, got))
        excl = jnp.where(lower, got * excl, excl)
        total = total * got
        span *= 2
    return steps, excl, total


def entering_states(decay, block_state, count, mine, hooks):
    steps, excl_decay, total_decay = decay_scan(decay, count, mine)
    excl = jnp.zeros_like(block_state)
    total = block_state
    results = {}
    span = 1
    for step, (lower, excl_a, own_a, got_a) in enumerate(steps):
        pairs = [(i, i ^ span) for i in range(count)]
        hook = hooks.get(step if step + 1 < len(steps) else -1)
        if hook is not None:
            total, args = lax.optimization_barrier((total, hook[1]))
        got = lax.ppermute(total.astype(jnp.bfloat16), "seq", pairs).astype(jnp.float32)
        if hook is not None:
            done = hook[0](*args)
            got, done = lax.optimization_barrier((got, done))
            results[hook[0].__name__] = done
        excl = jnp.where(lower, spread(excl_a)[:, None, :] * got + excl, excl)
        total = jnp.where(
            lower,
            spread(own_a)[:, None, :] * got + total,
            spread(got_a)[:, None, :] * total + got,
        )
        span *= 2
    carry = jnp.zeros_like(block_state[0])
    entering = []
    for slot in range(decay.shape[0]):
        entering.append(spread(excl_decay[slot])[None, :] * carry + excl[slot])
        carry = spread(total_decay[slot])[None, :] * carry + total[slot]
    return (jnp.stack(entering, axis=0), results)


def mamba_base(x_in, steps, cum, b_blocks, c_blocks, d_skip):
    slots, heads = steps.shape[:2]
    x_blocks = x_in.reshape(slots, BLOCK, heads, HEADDIM)
    causal = jnp.arange(BLOCK)[:, None] >= jnp.arange(BLOCK)[None, :]
    log_gap = jnp.where(causal, cum[:, :, :, None] - cum[:, :, None, :], -jnp.inf)
    inner = jnp.einsum("cin,cjn->cij", c_blocks, b_blocks, preferred_element_type=jnp.float32)
    mixing = (inner[:, None] * jnp.exp(log_gap) * steps[:, :, None, :]).astype(jnp.bfloat16)
    intra = jnp.einsum("chij,cjhp->cihp", mixing, x_blocks, preferred_element_type=jnp.float32)
    base = intra + d_skip[None, None, :, None] * x_blocks.astype(jnp.float32)
    return base.reshape(slots, BLOCK, heads * HEADDIM)


KEY_CHUNK = 256


def attention_prep(queries, kv_piece, my_index):
    tok_rows = queries.shape[0]
    slots = tok_rows // BLOCK
    kv_local = kv_piece.shape[2] // (2 * HD)
    per_kv = QHEADS // KVHEADS
    q_flat = queries.reshape(slots, BLOCK, kv_local, per_kv, HD).transpose(2, 0, 3, 1, 4)
    q_flat = q_flat.reshape(kv_local, slots * per_kv * BLOCK, HD)
    rows = kv_piece.shape[0] * kv_piece.shape[1]
    k_all = kv_piece[..., : kv_local * HD].reshape(rows, kv_local, HD).transpose(1, 0, 2)
    v_all = kv_piece[..., kv_local * HD :].reshape(rows, kv_local, HD).transpose(1, 0, 2)
    return (q_flat, k_all, v_all)


def attention_kernel(q_ref, k_ref, v_ref, o_ref):
    seq_count = lax.axis_size("seq")
    me = lax.axis_index("seq")
    slot = pl.program_id(1)
    rows = q_ref.shape[1]
    first = (slot * seq_count + me) * BLOCK
    chunks = (first + BLOCK + KEY_CHUNK - 1) // KEY_CHUNK
    q = q_ref[0]
    query_pos = first + lax.broadcasted_iota(jnp.int32, (rows, KEY_CHUNK), 0) % BLOCK
    key_col = lax.broadcasted_iota(jnp.int32, (rows, KEY_CHUNK), 1)
    score_scale = 1.0 / HD**0.5

    def scores(c):
        start = pl.multiple_of(c * KEY_CHUNK, KEY_CHUNK)
        k = k_ref[0, pl.ds(start, KEY_CHUNK), :]
        s = lax.dot_general(q, k, (((1,), (1,)), ((), ())), preferred_element_type=jnp.float32)
        visible = start + key_col <= query_pos
        return s * score_scale, visible, start

    def top_of(c, top):
        s, visible, unused = scores(c)
        return jnp.maximum(top, jnp.max(jnp.where(visible, s, NEG), axis=1, keepdims=True))

    top = lax.fori_loop(0, chunks, top_of, jnp.full((rows, 1), NEG, jnp.float32))

    def add_of(c, carry):
        total, acc = carry
        s, visible, start = scores(c)
        probs = jnp.where(visible, jnp.exp(s - top), 0.0)
        v = v_ref[0, pl.ds(start, KEY_CHUNK), :]
        acc = acc + jnp.dot(probs.astype(jnp.bfloat16), v, preferred_element_type=jnp.float32)
        return (total + jnp.sum(probs, axis=1, keepdims=True), acc)

    start_carry = (jnp.zeros((rows, 1), jnp.float32), jnp.zeros((rows, HD), jnp.float32))
    total, acc = lax.fori_loop(0, chunks, add_of, start_carry)
    o_ref[0] = (acc / total).astype(o_ref.dtype)


def attention_core(q_flat, k_all, v_all):
    groups, q_total, unused = q_flat.shape
    keys = k_all.shape[1]
    slots = q_total // ((QHEADS // KVHEADS) * BLOCK)
    block_q = q_total // slots
    cost = pl.CostEstimate(
        flops=4 * groups * q_total * keys * HD,
        transcendentals=groups * q_total * keys,
        bytes_accessed=2 * (2 * q_flat.size + k_all.size + v_all.size),
    )
    attended = pl.pallas_call(
        attention_kernel,
        out_shape=jax.ShapeDtypeStruct(q_flat.shape, jnp.bfloat16),
        grid=(groups, slots),
        in_specs=[
            pl.BlockSpec((1, block_q, HD), lambda g, s: (g, s, 0)),
            pl.BlockSpec((1, keys, HD), lambda g, s: (g, 0, 0)),
            pl.BlockSpec((1, keys, HD), lambda g, s: (g, 0, 0)),
        ],
        out_specs=pl.BlockSpec((1, block_q, HD), lambda g, s: (g, s, 0)),
        cost_estimate=cost,
    )(q_flat, k_all, v_all)
    per_kv = QHEADS // KVHEADS
    return (
        attended.reshape(groups, slots, per_kv, BLOCK, HD)
        .transpose(1, 3, 0, 2, 4)
        .reshape(slots * BLOCK, groups * per_kv * HD)
    )


def local(x_in, step_size, a_log, d_skip, b_in, c_in, queries, key_rows, values):
    my_index = lax.axis_index("seq")
    seq_count = lax.axis_size("seq")
    tok_rows, width = x_in.shape
    slots = tok_rows // BLOCK
    heads = step_size.shape[0]
    kv_cat = jnp.concatenate(
        [key_rows.reshape(slots, BLOCK, -1), values.reshape(slots, BLOCK, -1)], axis=2
    )
    kv_cat, x_in, step_size = lax.optimization_barrier((kv_cat, x_in, step_size))
    kv_piece = lax.all_gather(kv_cat, "seq", axis=1, tiled=True)
    rate = -jnp.exp(a_log)
    steps = step_size.reshape(heads, slots, BLOCK).transpose(1, 0, 2)
    cum = jnp.cumsum(steps * rate[None, :, None], axis=2)
    log_total = cum[:, :, -1]
    factor = (jnp.exp(log_total[:, :, None] - cum) * steps).transpose(0, 2, 1)
    x3 = x_in.reshape(slots, BLOCK, width)
    scaled = (spread(factor) * x3.astype(jnp.float32)).astype(jnp.bfloat16)
    b_blocks = b_in.reshape(slots, BLOCK, STATE)
    c_blocks = c_in.reshape(slots, BLOCK, STATE)
    block_state = jnp.einsum("ctn,ctk->cnk", b_blocks, scaled, preferred_element_type=jnp.float32)
    decay = jnp.exp(log_total)
    prepared = attention_prep(queries, kv_piece, my_index)
    hooks = {
        0: (mamba_base, (x_in, steps, cum, b_blocks, c_blocks, d_skip)),
        -1: (attention_core, prepared),
    }
    incoming, results = entering_states(decay, block_state, seq_count, my_index, hooks)
    carried = jnp.einsum(
        "ctn,cnk->ctk", c_blocks.astype(jnp.float32), incoming, precision=lax.Precision.HIGHEST
    )
    carried = carried * spread(jnp.exp(cum).transpose(0, 2, 1))
    mamba_out = (results["mamba_base"] + carried).astype(jnp.bfloat16).reshape(tok_rows, width)
    return (mamba_out, results["attention_core"])


def solution(mesh):
    in_specs = (
        P(("group", "seq"), "head"),
        P("head", ("group", "seq")),
        P("head"),
        P("head"),
        P(("group", "seq"), None),
        P(("group", "seq"), None),
        P(("group", "seq"), "head"),
        P(("group", "seq"), "head"),
        P(("group", "seq"), "head"),
    )
    out_specs = (P(("group", "seq"), "head"), P(("group", "seq"), "head"))
    return jax.shard_map(local, mesh=mesh, in_specs=in_specs, out_specs=out_specs, check_vma=False)
```

```python
import jax
import jax.numpy as jnp
from jax import lax
from jax.experimental import pallas as pl
from jax.experimental.pallas import tpu as pltpu
from jax.sharding import PartitionSpec as P

BLOCK = 128
HEADDIM = 64
STATE = 128
QHEADS = 16
KVHEADS = 4
HD = 128


NEG = -1e30


def spread(a):
    return jnp.repeat(a, HEADDIM, axis=-1)


def decay_scan(decay, count, mine):
    excl = jnp.ones_like(decay)
    total = decay
    steps = []
    span = 1
    while span < count:
        lower = (mine // span) % 2 == 1
        got = lax.ppermute(total, "seq", [(i, i ^ span) for i in range(count)])
        steps.append((lower, excl, total, got))
        excl = jnp.where(lower, got * excl, excl)
        total = total * got
        span *= 2
    return steps, excl, total


def entering_states(decay, block_state, count, mine, hooks):
    steps, excl_decay, total_decay = decay_scan(decay, count, mine)
    total, steps, excl_decay, total_decay = lax.optimization_barrier(
        (block_state, steps, excl_decay, total_decay)
    )
    excl = jnp.zeros_like(block_state)
    results = {}
    span = 1
    for step, (lower, excl_a, own_a, got_a) in enumerate(steps):
        pairs = [(i, i ^ span) for i in range(count)]
        hook = hooks.get(step if step + 1 < len(steps) else -1)
        if hook is not None:
            total, args = lax.optimization_barrier((total, hook[1]))
        got = lax.ppermute(total.astype(jnp.bfloat16), "seq", pairs).astype(jnp.float32)
        if hook is not None:
            done = hook[0](*args)
            got, done = lax.optimization_barrier((got, done))
            results[hook[0].__name__] = done
        excl = jnp.where(lower, spread(excl_a)[:, None, :] * got + excl, excl)
        total = jnp.where(
            lower,
            spread(own_a)[:, None, :] * got + total,
            spread(got_a)[:, None, :] * total + got,
        )
        span *= 2
    carry = jnp.zeros_like(block_state[0])
    entering = []
    for slot in range(decay.shape[0]):
        entering.append(spread(excl_decay[slot])[None, :] * carry + excl[slot])
        carry = spread(total_decay[slot])[None, :] * carry + total[slot]
    return (jnp.stack(entering, axis=0), results)


def mamba_base(x_in, steps, cum, b_blocks, c_blocks, d_skip):
    slots, heads = steps.shape[:2]
    x_blocks = x_in.reshape(slots, BLOCK, heads, HEADDIM)
    causal = jnp.arange(BLOCK)[:, None] >= jnp.arange(BLOCK)[None, :]
    log_gap = jnp.where(causal, cum[:, :, :, None] - cum[:, :, None, :], -jnp.inf)
    inner = jnp.einsum("cin,cjn->cij", c_blocks, b_blocks, preferred_element_type=jnp.float32)
    mixing = (inner[:, None] * jnp.exp(log_gap) * steps[:, :, None, :]).astype(jnp.bfloat16)
    intra = jnp.einsum("chij,cjhp->cihp", mixing, x_blocks, preferred_element_type=jnp.float32)
    base = intra + d_skip[None, None, :, None] * x_blocks.astype(jnp.float32)
    return base.reshape(slots, BLOCK, heads * HEADDIM)


KEY_CHUNK = 256


def attention_prep(queries, kv_piece, my_index):
    tok_rows = queries.shape[0]
    slots = tok_rows // BLOCK
    kv_local = kv_piece.shape[2] // (2 * HD)
    per_kv = QHEADS // KVHEADS
    q_flat = queries.reshape(slots, BLOCK, kv_local, per_kv, HD).transpose(2, 0, 3, 1, 4)
    q_flat = q_flat.reshape(kv_local, slots * per_kv * BLOCK, HD)
    rows = kv_piece.shape[0] * kv_piece.shape[1]
    k_all = kv_piece[..., : kv_local * HD].reshape(rows, kv_local, HD).transpose(1, 0, 2)
    v_all = kv_piece[..., kv_local * HD :].reshape(rows, kv_local, HD).transpose(1, 0, 2)
    return (q_flat, k_all, v_all)


def attention_kernel(q_ref, k_ref, v_ref, o_ref):
    seq_count = lax.axis_size("seq")
    me = lax.axis_index("seq")
    slot = pl.program_id(1)
    rows = q_ref.shape[1]
    first = (slot * seq_count + me) * BLOCK
    chunks = (first + BLOCK + KEY_CHUNK - 1) // KEY_CHUNK
    q = q_ref[0]
    query_pos = first + lax.broadcasted_iota(jnp.int32, (rows, KEY_CHUNK), 0) % BLOCK
    key_col = lax.broadcasted_iota(jnp.int32, (rows, KEY_CHUNK), 1)
    score_scale = 1.0 / HD**0.5

    def scores(c):
        start = pl.multiple_of(c * KEY_CHUNK, KEY_CHUNK)
        k = k_ref[0, pl.ds(start, KEY_CHUNK), :]
        s = lax.dot_general(q, k, (((1,), (1,)), ((), ())), preferred_element_type=jnp.float32)
        visible = start + key_col <= query_pos
        return s * score_scale, visible, start

    def top_of(c, top):
        s, visible, unused = scores(c)
        return jnp.maximum(top, jnp.max(jnp.where(visible, s, NEG), axis=1, keepdims=True))

    top = lax.fori_loop(0, chunks, top_of, jnp.full((rows, 1), NEG, jnp.float32))

    def add_of(c, carry):
        total, acc = carry
        s, visible, start = scores(c)
        probs = jnp.where(visible, jnp.exp(s - top), 0.0)
        v = v_ref[0, pl.ds(start, KEY_CHUNK), :]
        acc = acc + jnp.dot(probs.astype(jnp.bfloat16), v, preferred_element_type=jnp.float32)
        return (total + jnp.sum(probs, axis=1, keepdims=True), acc)

    start_carry = (jnp.zeros((rows, 1), jnp.float32), jnp.zeros((rows, HD), jnp.float32))
    total, acc = lax.fori_loop(0, chunks, add_of, start_carry)
    o_ref[0] = (acc / total).astype(o_ref.dtype)


def attention_core(q_flat, k_all, v_all):
    groups, q_total, unused = q_flat.shape
    keys = k_all.shape[1]
    slots = q_total // ((QHEADS // KVHEADS) * BLOCK)
    block_q = q_total // slots
    cost = pl.CostEstimate(
        flops=4 * groups * q_total * keys * HD,
        transcendentals=groups * q_total * keys,
        bytes_accessed=2 * (2 * q_flat.size + k_all.size + v_all.size),
    )
    attended = pl.pallas_call(
        attention_kernel,
        out_shape=jax.ShapeDtypeStruct(q_flat.shape, jnp.bfloat16),
        grid=(groups, slots),
        in_specs=[
            pl.BlockSpec((1, block_q, HD), lambda g, s: (g, s, 0)),
            pl.BlockSpec((1, keys, HD), lambda g, s: (g, 0, 0)),
            pl.BlockSpec((1, keys, HD), lambda g, s: (g, 0, 0)),
        ],
        out_specs=pl.BlockSpec((1, block_q, HD), lambda g, s: (g, s, 0)),
        cost_estimate=cost,
    )(q_flat, k_all, v_all)
    per_kv = QHEADS // KVHEADS
    return (
        attended.reshape(groups, slots, per_kv, BLOCK, HD)
        .transpose(1, 3, 0, 2, 4)
        .reshape(slots * BLOCK, groups * per_kv * HD)
    )


def local(x_in, step_size, a_log, d_skip, b_in, c_in, queries, key_rows, values):
    my_index = lax.axis_index("seq")
    seq_count = lax.axis_size("seq")
    tok_rows, width = x_in.shape
    slots = tok_rows // BLOCK
    heads = step_size.shape[0]
    kv_cat = jnp.concatenate(
        [key_rows.reshape(slots, BLOCK, -1), values.reshape(slots, BLOCK, -1)], axis=2
    )
    kv_cat, x_in, step_size = lax.optimization_barrier((kv_cat, x_in, step_size))
    kv_piece = lax.all_gather(kv_cat, "seq", axis=1, tiled=True)
    rate = -jnp.exp(a_log)
    steps = step_size.reshape(heads, slots, BLOCK).transpose(1, 0, 2)
    cum = jnp.cumsum(steps * rate[None, :, None], axis=2)
    log_total = cum[:, :, -1]
    factor = (jnp.exp(log_total[:, :, None] - cum) * steps).transpose(0, 2, 1)
    x3 = x_in.reshape(slots, BLOCK, width)
    scaled = (spread(factor) * x3.astype(jnp.float32)).astype(jnp.bfloat16)
    b_blocks = b_in.reshape(slots, BLOCK, STATE)
    c_blocks = c_in.reshape(slots, BLOCK, STATE)
    block_state = jnp.einsum("ctn,ctk->cnk", b_blocks, scaled, preferred_element_type=jnp.float32)
    decay = jnp.exp(log_total)
    prepared = attention_prep(queries, kv_piece, my_index)
    hooks = {
        0: (mamba_base, (x_in, steps, cum, b_blocks, c_blocks, d_skip)),
        -1: (attention_core, prepared),
    }
    incoming, results = entering_states(decay, block_state, seq_count, my_index, hooks)
    carried = jnp.einsum(
        "ctn,cnk->ctk", c_blocks.astype(jnp.float32), incoming, precision=lax.Precision.HIGHEST
    )
    carried = carried * spread(jnp.exp(cum).transpose(0, 2, 1))
    mamba_out = (results["mamba_base"] + carried).astype(jnp.bfloat16).reshape(tok_rows, width)
    return (mamba_out, results["attention_core"])


def solution(mesh):
    in_specs = (
        P(("group", "seq"), "head"),
        P("head", ("group", "seq")),
        P("head"),
        P("head"),
        P(("group", "seq"), None),
        P(("group", "seq"), None),
        P(("group", "seq"), "head"),
        P(("group", "seq"), "head"),
        P(("group", "seq"), "head"),
    )
    out_specs = (P(("group", "seq"), "head"), P(("group", "seq"), "head"))
    return jax.shard_map(local, mesh=mesh, in_specs=in_specs, out_specs=out_specs, check_vma=False)
```

```python
import jax
import jax.numpy as jnp
from jax import lax
from jax.experimental import pallas as pl
from jax.experimental.pallas import tpu as pltpu
from jax.sharding import PartitionSpec as P

BLOCK = 128
HEADDIM = 64
STATE = 128
QHEADS = 16
KVHEADS = 4
HD = 128


NEG = -1e30


def spread(a):
    return jnp.repeat(a, HEADDIM, axis=-1)


def decay_scan(decay, count, mine):
    excl = jnp.ones_like(decay)
    total = decay
    steps = []
    span = 1
    while span < count:
        lower = (mine // span) % 2 == 1
        got = lax.ppermute(total, "seq", [(i, i ^ span) for i in range(count)])
        steps.append((lower, excl, total, got))
        excl = jnp.where(lower, got * excl, excl)
        total = total * got
        span *= 2
    return steps, excl, total


def entering_states(decay, block_state, count, mine, hooks):
    steps, excl_decay, total_decay = decay_scan(decay, count, mine)
    total = block_state
    excl = jnp.zeros_like(block_state)
    results = {}
    span = 1
    for step, known in enumerate(steps):
        pairs = [(i, i ^ span) for i in range(count)]
        hook = hooks.get(step if step + 1 < len(steps) else -1)
        total, known, args = lax.optimization_barrier((total, known, hook[1] if hook else ()))
        lower, excl_a, own_a, got_a = known
        got = lax.ppermute(total.astype(jnp.bfloat16), "seq", pairs).astype(jnp.float32)
        if hook is not None:
            done = hook[0](*args)
            got, done = lax.optimization_barrier((got, done))
            results[hook[0].__name__] = done
        excl = jnp.where(lower, spread(excl_a)[:, None, :] * got + excl, excl)
        total = jnp.where(
            lower,
            spread(own_a)[:, None, :] * got + total,
            spread(got_a)[:, None, :] * total + got,
        )
        span *= 2
    carry = jnp.zeros_like(block_state[0])
    entering = []
    for slot in range(decay.shape[0]):
        entering.append(spread(excl_decay[slot])[None, :] * carry + excl[slot])
        carry = spread(total_decay[slot])[None, :] * carry + total[slot]
    return (jnp.stack(entering, axis=0), results)


def mamba_base(x_in, steps, cum, b_blocks, c_blocks, d_skip):
    slots, heads = steps.shape[:2]
    x_blocks = x_in.reshape(slots, BLOCK, heads, HEADDIM)
    causal = jnp.arange(BLOCK)[:, None] >= jnp.arange(BLOCK)[None, :]
    log_gap = jnp.where(causal, cum[:, :, :, None] - cum[:, :, None, :], -jnp.inf)
    inner = jnp.einsum("cin,cjn->cij", c_blocks, b_blocks, preferred_element_type=jnp.float32)
    mixing = (inner[:, None] * jnp.exp(log_gap) * steps[:, :, None, :]).astype(jnp.bfloat16)
    intra = jnp.einsum("chij,cjhp->cihp", mixing, x_blocks, preferred_element_type=jnp.float32)
    base = intra + d_skip[None, None, :, None] * x_blocks.astype(jnp.float32)
    return base.reshape(slots, BLOCK, heads * HEADDIM)


KEY_CHUNK = 256


def attention_kernel(q_ref, k_ref, v_ref, o_ref):
    seq_count = lax.axis_size("seq")
    me = lax.axis_index("seq")
    slot = pl.program_id(1)
    per_kv = q_ref.shape[1] // HD
    rows = per_kv * BLOCK
    held = k_ref.shape[1]
    first = (slot * seq_count + me) * BLOCK
    chunks = (first + BLOCK + KEY_CHUNK - 1) // KEY_CHUNK
    q = jnp.concatenate([q_ref[:, j * HD : (j + 1) * HD] for j in range(per_kv)], axis=0)
    query_pos = first + lax.broadcasted_iota(jnp.int32, (rows, KEY_CHUNK), 0) % BLOCK
    key_col = lax.broadcasted_iota(jnp.int32, (rows, KEY_CHUNK), 1)
    score_scale = 1.0 / HD**0.5

    def place(c):
        start = c * KEY_CHUNK
        return start, start // held, pl.multiple_of(start % held, KEY_CHUNK)

    def scores(c):
        start, at_slot, at_row = place(c)
        k = k_ref[at_slot, pl.ds(at_row, KEY_CHUNK), :]
        s = lax.dot_general(q, k, (((1,), (1,)), ((), ())), preferred_element_type=jnp.float32)
        return s * score_scale, start + key_col <= query_pos

    def top_of(c, top):
        s, visible = scores(c)
        return jnp.maximum(top, jnp.max(jnp.where(visible, s, NEG), axis=1, keepdims=True))

    top = lax.fori_loop(0, chunks, top_of, jnp.full((rows, 1), NEG, jnp.float32))

    def add_of(c, carry):
        total, acc = carry
        s, visible = scores(c)
        probs = jnp.where(visible, jnp.exp(s - top), 0.0)
        unused, at_slot, at_row = place(c)
        v = v_ref[at_slot, pl.ds(at_row, KEY_CHUNK), :]
        acc = acc + jnp.dot(probs.astype(jnp.bfloat16), v, preferred_element_type=jnp.float32)
        return (total + jnp.sum(probs, axis=1, keepdims=True), acc)

    start_carry = (jnp.zeros((rows, 1), jnp.float32), jnp.zeros((rows, HD), jnp.float32))
    total, acc = lax.fori_loop(0, chunks, add_of, start_carry)
    out = (acc / total).astype(o_ref.dtype)
    for j in range(per_kv):
        o_ref[:, j * HD : (j + 1) * HD] = out[j * BLOCK : (j + 1) * BLOCK]


def attention_core(queries, kv_piece):
    tok_rows, width = queries.shape
    slots, held, unused = kv_piece.shape
    kv_local = kv_piece.shape[2] // (2 * HD)
    group_width = width // kv_local
    keys = slots * held
    cost = pl.CostEstimate(
        flops=4 * tok_rows * width * keys,
        transcendentals=tok_rows * width * keys // HD,
        bytes_accessed=2 * (2 * queries.size + kv_piece.size),
    )
    return pl.pallas_call(
        attention_kernel,
        out_shape=jax.ShapeDtypeStruct(queries.shape, jnp.bfloat16),
        grid=(kv_local, slots),
        in_specs=[
            pl.BlockSpec((BLOCK, group_width), lambda g, s: (s, g)),
            pl.BlockSpec((slots, held, HD), lambda g, s: (0, 0, g)),
            pl.BlockSpec((slots, held, HD), lambda g, s: (0, 0, kv_local + g)),
        ],
        out_specs=pl.BlockSpec((BLOCK, group_width), lambda g, s: (s, g)),
        cost_estimate=cost,
    )(queries, kv_piece, kv_piece)


def local(x_in, step_size, a_log, d_skip, b_in, c_in, queries, key_rows, values):
    my_index = lax.axis_index("seq")
    seq_count = lax.axis_size("seq")
    tok_rows, width = x_in.shape
    slots = tok_rows // BLOCK
    heads = step_size.shape[0]
    kv_cat = jnp.concatenate(
        [key_rows.reshape(slots, BLOCK, -1), values.reshape(slots, BLOCK, -1)], axis=2
    )
    kv_cat, x_in, step_size = lax.optimization_barrier((kv_cat, x_in, step_size))
    kv_piece = lax.all_gather(kv_cat, "seq", axis=1, tiled=True)
    rate = -jnp.exp(a_log)
    steps = step_size.reshape(heads, slots, BLOCK).transpose(1, 0, 2)
    cum = jnp.cumsum(steps * rate[None, :, None], axis=2)
    log_total = cum[:, :, -1]
    factor = (jnp.exp(log_total[:, :, None] - cum) * steps).transpose(0, 2, 1)
    x3 = x_in.reshape(slots, BLOCK, width)
    scaled = (spread(factor) * x3.astype(jnp.float32)).astype(jnp.bfloat16)
    b_blocks = b_in.reshape(slots, BLOCK, STATE)
    c_blocks = c_in.reshape(slots, BLOCK, STATE)
    block_state = jnp.einsum("ctn,ctk->cnk", b_blocks, scaled, preferred_element_type=jnp.float32)
    decay = jnp.exp(log_total)
    hooks = {
        0: (mamba_base, (x_in, steps, cum, b_blocks, c_blocks, d_skip)),
        -1: (attention_core, (queries, kv_piece)),
    }
    incoming, results = entering_states(decay, block_state, seq_count, my_index, hooks)
    carried = jnp.einsum(
        "ctn,cnk->ctk", c_blocks.astype(jnp.float32), incoming, precision=lax.Precision.HIGHEST
    )
    carried = carried * spread(jnp.exp(cum).transpose(0, 2, 1))
    mamba_out = (results["mamba_base"] + carried).astype(jnp.bfloat16).reshape(tok_rows, width)
    return (mamba_out, results["attention_core"])


def solution(mesh):
    in_specs = (
        P(("group", "seq"), "head"),
        P("head", ("group", "seq")),
        P("head"),
        P("head"),
        P(("group", "seq"), None),
        P(("group", "seq"), None),
        P(("group", "seq"), "head"),
        P(("group", "seq"), "head"),
        P(("group", "seq"), "head"),
    )
    out_specs = (P(("group", "seq"), "head"), P(("group", "seq"), "head"))
    return jax.shard_map(local, mesh=mesh, in_specs=in_specs, out_specs=out_specs, check_vma=False)
```

```python
import jax
import jax.numpy as jnp
from jax import lax
from jax.experimental import pallas as pl
from jax.experimental.pallas import tpu as pltpu
from jax.sharding import PartitionSpec as P

BLOCK = 128
HEADDIM = 64
STATE = 128
QHEADS = 16
KVHEADS = 4
HD = 128


NEG = -1e30


def spread(a):
    return jnp.repeat(a, HEADDIM, axis=-1)


def decay_scan(decay, count, mine):
    excl = jnp.ones_like(decay)
    total = decay
    steps = []
    span = 1
    while span < count:
        lower = (mine // span) % 2 == 1
        got = lax.ppermute(total, "seq", [(i, i ^ span) for i in range(count)])
        steps.append((lower, excl, total, got))
        excl = jnp.where(lower, got * excl, excl)
        total = total * got
        span *= 2
    return steps, excl, total


def entering_states(decay, block_state, count, mine, hooks, parts):
    steps, excl_decay, total_decay = decay_scan(decay, count, mine)
    heads, width = decay.shape[1], block_state.shape[2]
    head_cut, width_cut = heads // parts, width // parts
    totals = [block_state[:, :, j * width_cut : (j + 1) * width_cut] for j in range(parts)]
    excls = [jnp.zeros_like(t) for t in totals]
    results = {}
    span = 1
    for step, known_all in enumerate(steps):
        pairs = [(i, i ^ span) for i in range(count)]
        before = ()
        for j in range(parts):
            hook = hooks.get((j, step if step + 1 < len(steps) else -1))
            totals[j], known, args, unused = lax.optimization_barrier(
                (totals[j], known_all, hook[1] if hook else (), before)
            )
            lower, excl_a, own_a, got_a = [
                v if v.ndim == 0 else v[:, j * head_cut : (j + 1) * head_cut] for v in known
            ]
            got = lax.ppermute(totals[j].astype(jnp.bfloat16), "seq", pairs).astype(jnp.float32)
            if hook is not None:
                done = hook[0](*args)
                got, done = lax.optimization_barrier((got, done))
                results[hook[0].__name__] = done
            excls[j] = jnp.where(lower, spread(excl_a)[:, None, :] * got + excls[j], excls[j])
            totals[j] = jnp.where(
                lower,
                spread(own_a)[:, None, :] * got + totals[j],
                spread(got_a)[:, None, :] * totals[j] + got,
            )
            before = got
        span *= 2
    entering = []
    for j in range(parts):
        carry = jnp.zeros_like(totals[j][0])
        rows = []
        for slot in range(decay.shape[0]):
            a_excl = excl_decay[slot, j * head_cut : (j + 1) * head_cut]
            a_total = total_decay[slot, j * head_cut : (j + 1) * head_cut]
            rows.append(spread(a_excl)[None, :] * carry + excls[j][slot])
            carry = spread(a_total)[None, :] * carry + totals[j][slot]
        entering.append(jnp.stack(rows, axis=0))
    return (entering, results)


def mamba_base(x_in, steps, cum, b_blocks, c_blocks, d_skip):
    slots, heads = steps.shape[:2]
    x_blocks = x_in.reshape(slots, BLOCK, heads, HEADDIM)
    causal = jnp.arange(BLOCK)[:, None] >= jnp.arange(BLOCK)[None, :]
    log_gap = jnp.where(causal, cum[:, :, :, None] - cum[:, :, None, :], -jnp.inf)
    inner = jnp.einsum("cin,cjn->cij", c_blocks, b_blocks, preferred_element_type=jnp.float32)
    mixing = (inner[:, None] * jnp.exp(log_gap) * steps[:, :, None, :]).astype(jnp.bfloat16)
    intra = jnp.einsum("chij,cjhp->cihp", mixing, x_blocks, preferred_element_type=jnp.float32)
    base = intra + d_skip[None, None, :, None] * x_blocks.astype(jnp.float32)
    return base.reshape(slots, BLOCK, heads * HEADDIM)


KEY_CHUNK = 256


def attention_kernel(q_ref, k_ref, v_ref, o_ref):
    seq_count = lax.axis_size("seq")
    me = lax.axis_index("seq")
    slot = pl.program_id(1)
    per_kv = q_ref.shape[1] // HD
    rows = per_kv * BLOCK
    held = k_ref.shape[1]
    first = (slot * seq_count + me) * BLOCK
    chunks = (first + BLOCK + KEY_CHUNK - 1) // KEY_CHUNK
    q = jnp.concatenate([q_ref[:, j * HD : (j + 1) * HD] for j in range(per_kv)], axis=0)
    query_pos = first + lax.broadcasted_iota(jnp.int32, (rows, KEY_CHUNK), 0) % BLOCK
    key_col = lax.broadcasted_iota(jnp.int32, (rows, KEY_CHUNK), 1)
    score_scale = 1.0 / HD**0.5

    def place(c):
        start = c * KEY_CHUNK
        return start, start // held, pl.multiple_of(start % held, KEY_CHUNK)

    def scores(c):
        start, at_slot, at_row = place(c)
        k = k_ref[at_slot, pl.ds(at_row, KEY_CHUNK), :]
        s = lax.dot_general(q, k, (((1,), (1,)), ((), ())), preferred_element_type=jnp.float32)
        return s * score_scale, start + key_col <= query_pos

    def top_of(c, top):
        s, visible = scores(c)
        return jnp.maximum(top, jnp.max(jnp.where(visible, s, NEG), axis=1, keepdims=True))

    top = lax.fori_loop(0, chunks, top_of, jnp.full((rows, 1), NEG, jnp.float32))

    def add_of(c, carry):
        total, acc = carry
        s, visible = scores(c)
        probs = jnp.where(visible, jnp.exp(s - top), 0.0)
        unused, at_slot, at_row = place(c)
        v = v_ref[at_slot, pl.ds(at_row, KEY_CHUNK), :]
        acc = acc + jnp.dot(probs.astype(jnp.bfloat16), v, preferred_element_type=jnp.float32)
        return (total + jnp.sum(probs, axis=1, keepdims=True), acc)

    start_carry = (jnp.zeros((rows, 1), jnp.float32), jnp.zeros((rows, HD), jnp.float32))
    total, acc = lax.fori_loop(0, chunks, add_of, start_carry)
    out = (acc / total).astype(o_ref.dtype)
    for j in range(per_kv):
        o_ref[:, j * HD : (j + 1) * HD] = out[j * BLOCK : (j + 1) * BLOCK]


def attention_core(queries, kv_piece):
    tok_rows, width = queries.shape
    slots, held, unused = kv_piece.shape
    kv_local = kv_piece.shape[2] // (2 * HD)
    group_width = width // kv_local
    keys = slots * held
    cost = pl.CostEstimate(
        flops=4 * tok_rows * width * keys,
        transcendentals=tok_rows * width * keys // HD,
        bytes_accessed=2 * (2 * queries.size + kv_piece.size),
    )
    return pl.pallas_call(
        attention_kernel,
        out_shape=jax.ShapeDtypeStruct(queries.shape, jnp.bfloat16),
        grid=(kv_local, slots),
        in_specs=[
            pl.BlockSpec((BLOCK, group_width), lambda g, s: (s, g)),
            pl.BlockSpec((slots, held, HD), lambda g, s: (0, 0, g)),
            pl.BlockSpec((slots, held, HD), lambda g, s: (0, 0, kv_local + g)),
        ],
        out_specs=pl.BlockSpec((BLOCK, group_width), lambda g, s: (s, g)),
        cost_estimate=cost,
    )(queries, kv_piece, kv_piece)


def local(x_in, step_size, a_log, d_skip, b_in, c_in, queries, key_rows, values):
    my_index = lax.axis_index("seq")
    seq_count = lax.axis_size("seq")
    tok_rows, width = x_in.shape
    slots = tok_rows // BLOCK
    heads = step_size.shape[0]
    kv_cat = jnp.concatenate(
        [key_rows.reshape(slots, BLOCK, -1), values.reshape(slots, BLOCK, -1)], axis=2
    )
    kv_cat, x_in, step_size = lax.optimization_barrier((kv_cat, x_in, step_size))
    kv_piece = lax.all_gather(kv_cat, "seq", axis=1, tiled=True)
    rate = -jnp.exp(a_log)
    steps = step_size.reshape(heads, slots, BLOCK).transpose(1, 0, 2)
    cum = jnp.cumsum(steps * rate[None, :, None], axis=2)
    log_total = cum[:, :, -1]
    factor = (jnp.exp(log_total[:, :, None] - cum) * steps).transpose(0, 2, 1)
    x3 = x_in.reshape(slots, BLOCK, width)
    scaled = (spread(factor) * x3.astype(jnp.float32)).astype(jnp.bfloat16)
    b_blocks = b_in.reshape(slots, BLOCK, STATE)
    c_blocks = c_in.reshape(slots, BLOCK, STATE)
    block_state = jnp.einsum("ctn,ctk->cnk", b_blocks, scaled, preferred_element_type=jnp.float32)
    decay = jnp.exp(log_total)
    parts = 2 if heads % 2 == 0 else 1
    hooks = {
        (0, 0): (mamba_base, (x_in, steps, cum, b_blocks, c_blocks, d_skip)),
        (0, -1): (attention_core, (queries, kv_piece)),
    }
    incoming, results = entering_states(decay, block_state, seq_count, my_index, hooks, parts)
    c_wide = c_blocks.astype(jnp.float32)
    carried = jnp.concatenate(
        [
            jnp.einsum("ctn,cnk->ctk", c_wide, part, precision=lax.Precision.HIGHEST)
            for part in incoming
        ],
        axis=2,
    )
    carried = carried * spread(jnp.exp(cum).transpose(0, 2, 1))
    mamba_out = (results["mamba_base"] + carried).astype(jnp.bfloat16).reshape(tok_rows, width)
    return (mamba_out, results["attention_core"])


def solution(mesh):
    in_specs = (
        P(("group", "seq"), "head"),
        P("head", ("group", "seq")),
        P("head"),
        P("head"),
        P(("group", "seq"), None),
        P(("group", "seq"), None),
        P(("group", "seq"), "head"),
        P(("group", "seq"), "head"),
        P(("group", "seq"), "head"),
    )
    out_specs = (P(("group", "seq"), "head"), P(("group", "seq"), "head"))
    return jax.shard_map(local, mesh=mesh, in_specs=in_specs, out_specs=out_specs, check_vma=False)
```

```python
import jax
import jax.numpy as jnp
from jax import lax
from jax.experimental import pallas as pl
from jax.experimental.pallas import tpu as pltpu
from jax.sharding import PartitionSpec as P

BLOCK = 128
HEADDIM = 64
STATE = 128
QHEADS = 16
KVHEADS = 4
HD = 128


NEG = -1e30


def spread(a):
    return jnp.repeat(a, HEADDIM, axis=-1)


def decay_scan(decay, count, mine):
    excl = jnp.ones_like(decay)
    total = decay
    steps = []
    span = 1
    while span < count:
        lower = (mine // span) % 2 == 1
        got = lax.ppermute(total, "seq", [(i, i ^ span) for i in range(count)])
        steps.append((lower, excl, total, got))
        excl = jnp.where(lower, got * excl, excl)
        total = total * got
        span *= 2
    return steps, excl, total


def entering_states(decay, block_state, count, mine, hooks, parts):
    steps, excl_decay, total_decay = decay_scan(decay, count, mine)
    heads, width = decay.shape[1], block_state.shape[2]
    head_cut, width_cut = heads // parts, width // parts
    totals = [block_state[:, :, j * width_cut : (j + 1) * width_cut] for j in range(parts)]
    excls = [jnp.zeros_like(t) for t in totals]
    results = {}
    span = 1
    for step, known_all in enumerate(steps):
        pairs = [(i, i ^ span) for i in range(count)]
        before = ()
        for j in range(parts):
            hook = hooks.get((j, step if step + 1 < len(steps) else -1))
            totals[j], known, args, unused = lax.optimization_barrier(
                (totals[j], known_all, hook[1] if hook else (), before)
            )
            lower, excl_a, own_a, got_a = [
                v if v.ndim == 0 else v[:, j * head_cut : (j + 1) * head_cut] for v in known
            ]
            got = lax.ppermute(totals[j].astype(jnp.bfloat16), "seq", pairs).astype(jnp.float32)
            if hook is not None:
                done = hook[0](*args)
                got, done = lax.optimization_barrier((got, done))
                results[hook[0].__name__] = done
            excls[j] = jnp.where(lower, spread(excl_a)[:, None, :] * got + excls[j], excls[j])
            totals[j] = jnp.where(
                lower,
                spread(own_a)[:, None, :] * got + totals[j],
                spread(got_a)[:, None, :] * totals[j] + got,
            )
            before = got
        span *= 2
    entering = []
    for j in range(parts):
        carry = jnp.zeros_like(totals[j][0])
        rows = []
        for slot in range(decay.shape[0]):
            a_excl = excl_decay[slot, j * head_cut : (j + 1) * head_cut]
            a_total = total_decay[slot, j * head_cut : (j + 1) * head_cut]
            rows.append(spread(a_excl)[None, :] * carry + excls[j][slot])
            carry = spread(a_total)[None, :] * carry + totals[j][slot]
        entering.append(jnp.stack(rows, axis=0))
    return (entering, results)


def mamba_base_kernel(x_ref, inner_ref, cum_row_ref, cum_col_ref, step_ref, skip_ref, o_ref):
    causal = lax.broadcasted_iota(jnp.int32, (BLOCK, BLOCK), 0) >= lax.broadcasted_iota(
        jnp.int32, (BLOCK, BLOCK), 1
    )
    inner = inner_ref[0]
    for e in range(cum_row_ref.shape[1]):
        log_gap = jnp.where(causal, cum_col_ref[0, e] - cum_row_ref[0, e], -jnp.inf)
        mixing = (inner * jnp.exp(log_gap) * step_ref[0, e]).astype(jnp.bfloat16)
        x_head = x_ref[:, e * HEADDIM : (e + 1) * HEADDIM]
        intra = jnp.dot(mixing, x_head, preferred_element_type=jnp.float32)
        skip = skip_ref[:, e * HEADDIM : (e + 1) * HEADDIM] * x_head.astype(jnp.float32)
        o_ref[0, :, e * HEADDIM : (e + 1) * HEADDIM] = intra + skip


def mamba_base(x_in, steps, cum, b_blocks, c_blocks, d_skip):
    slots, heads = steps.shape[:2]
    width = x_in.shape[1]
    pair = 128 // HEADDIM
    inner = jnp.einsum("cin,cjn->cij", c_blocks, b_blocks, preferred_element_type=jnp.float32)
    cum_row = cum[:, :, None, :]
    cum_col = cum[:, :, :, None]
    step_row = steps[:, :, None, :]
    skip_row = spread(d_skip)[None, :]
    cost = pl.CostEstimate(
        flops=2 * slots * heads * BLOCK * BLOCK * (HEADDIM + 3),
        transcendentals=slots * heads * BLOCK * BLOCK,
        bytes_accessed=x_in.size * 2 + slots * BLOCK * width * 4,
    )
    return pl.pallas_call(
        mamba_base_kernel,
        out_shape=jax.ShapeDtypeStruct((slots, BLOCK, width), jnp.float32),
        grid=(slots, heads // pair),
        in_specs=[
            pl.BlockSpec((BLOCK, pair * HEADDIM), lambda c, g: (c, g)),
            pl.BlockSpec((1, BLOCK, BLOCK), lambda c, g: (c, 0, 0)),
            pl.BlockSpec((1, pair, 1, BLOCK), lambda c, g: (c, g, 0, 0)),
            pl.BlockSpec((1, pair, BLOCK, 1), lambda c, g: (c, g, 0, 0)),
            pl.BlockSpec((1, pair, 1, BLOCK), lambda c, g: (c, g, 0, 0)),
            pl.BlockSpec((1, pair * HEADDIM), lambda c, g: (0, g)),
        ],
        out_specs=pl.BlockSpec((1, BLOCK, pair * HEADDIM), lambda c, g: (c, 0, g)),
        cost_estimate=cost,
    )(x_in, inner, cum_row, cum_col, step_row, skip_row)


KEY_CHUNK = 256


def attention_kernel(q_ref, k_ref, v_ref, o_ref):
    seq_count = lax.axis_size("seq")
    me = lax.axis_index("seq")
    slot = pl.program_id(1)
    per_kv = q_ref.shape[1] // HD
    rows = per_kv * BLOCK
    held = k_ref.shape[1]
    first = (slot * seq_count + me) * BLOCK
    chunks = (first + BLOCK + KEY_CHUNK - 1) // KEY_CHUNK
    q = jnp.concatenate([q_ref[:, j * HD : (j + 1) * HD] for j in range(per_kv)], axis=0)
    query_pos = first + lax.broadcasted_iota(jnp.int32, (rows, KEY_CHUNK), 0) % BLOCK
    key_col = lax.broadcasted_iota(jnp.int32, (rows, KEY_CHUNK), 1)
    score_scale = 1.0 / HD**0.5

    def place(c):
        start = c * KEY_CHUNK
        return start, start // held, pl.multiple_of(start % held, KEY_CHUNK)

    def scores(c):
        start, at_slot, at_row = place(c)
        k = k_ref[at_slot, pl.ds(at_row, KEY_CHUNK), :]
        s = lax.dot_general(q, k, (((1,), (1,)), ((), ())), preferred_element_type=jnp.float32)
        return s * score_scale, start + key_col <= query_pos

    def top_of(c, top):
        s, visible = scores(c)
        return jnp.maximum(top, jnp.max(jnp.where(visible, s, NEG), axis=1, keepdims=True))

    top = lax.fori_loop(0, chunks, top_of, jnp.full((rows, 1), NEG, jnp.float32))

    def add_of(c, carry):
        total, acc = carry
        s, visible = scores(c)
        probs = jnp.where(visible, jnp.exp(s - top), 0.0)
        unused, at_slot, at_row = place(c)
        v = v_ref[at_slot, pl.ds(at_row, KEY_CHUNK), :]
        acc = acc + jnp.dot(probs.astype(jnp.bfloat16), v, preferred_element_type=jnp.float32)
        return (total + jnp.sum(probs, axis=1, keepdims=True), acc)

    start_carry = (jnp.zeros((rows, 1), jnp.float32), jnp.zeros((rows, HD), jnp.float32))
    total, acc = lax.fori_loop(0, chunks, add_of, start_carry)
    out = (acc / total).astype(o_ref.dtype)
    for j in range(per_kv):
        o_ref[:, j * HD : (j + 1) * HD] = out[j * BLOCK : (j + 1) * BLOCK]


def attention_core(queries, kv_piece):
    tok_rows, width = queries.shape
    slots, held, unused = kv_piece.shape
    kv_local = kv_piece.shape[2] // (2 * HD)
    group_width = width // kv_local
    keys = slots * held
    cost = pl.CostEstimate(
        flops=4 * tok_rows * width * keys,
        transcendentals=tok_rows * width * keys // HD,
        bytes_accessed=2 * (2 * queries.size + kv_piece.size),
    )
    return pl.pallas_call(
        attention_kernel,
        out_shape=jax.ShapeDtypeStruct(queries.shape, jnp.bfloat16),
        grid=(kv_local, slots),
        in_specs=[
            pl.BlockSpec((BLOCK, group_width), lambda g, s: (s, g)),
            pl.BlockSpec((slots, held, HD), lambda g, s: (0, 0, g)),
            pl.BlockSpec((slots, held, HD), lambda g, s: (0, 0, kv_local + g)),
        ],
        out_specs=pl.BlockSpec((BLOCK, group_width), lambda g, s: (s, g)),
        cost_estimate=cost,
    )(queries, kv_piece, kv_piece)


def local(x_in, step_size, a_log, d_skip, b_in, c_in, queries, key_rows, values):
    my_index = lax.axis_index("seq")
    seq_count = lax.axis_size("seq")
    tok_rows, width = x_in.shape
    slots = tok_rows // BLOCK
    heads = step_size.shape[0]
    kv_cat = jnp.concatenate(
        [key_rows.reshape(slots, BLOCK, -1), values.reshape(slots, BLOCK, -1)], axis=2
    )
    kv_cat, x_in, step_size = lax.optimization_barrier((kv_cat, x_in, step_size))
    kv_piece = lax.all_gather(kv_cat, "seq", axis=1, tiled=True)
    rate = -jnp.exp(a_log)
    steps = step_size.reshape(heads, slots, BLOCK).transpose(1, 0, 2)
    cum = jnp.cumsum(steps * rate[None, :, None], axis=2)
    log_total = cum[:, :, -1]
    factor = (jnp.exp(log_total[:, :, None] - cum) * steps).transpose(0, 2, 1)
    x3 = x_in.reshape(slots, BLOCK, width)
    scaled = (spread(factor) * x3.astype(jnp.float32)).astype(jnp.bfloat16)
    b_blocks = b_in.reshape(slots, BLOCK, STATE)
    c_blocks = c_in.reshape(slots, BLOCK, STATE)
    block_state = jnp.einsum("ctn,ctk->cnk", b_blocks, scaled, preferred_element_type=jnp.float32)
    decay = jnp.exp(log_total)
    parts = 2 if heads % 2 == 0 else 1
    hooks = {
        (0, 0): (mamba_base, (x_in, steps, cum, b_blocks, c_blocks, d_skip)),
        (0, -1): (attention_core, (queries, kv_piece)),
    }
    incoming, results = entering_states(decay, block_state, seq_count, my_index, hooks, parts)
    c_wide = c_blocks.astype(jnp.float32)
    carried = jnp.concatenate(
        [
            jnp.einsum("ctn,cnk->ctk", c_wide, part, precision=lax.Precision.HIGHEST)
            for part in incoming
        ],
        axis=2,
    )
    carried = carried * spread(jnp.exp(cum).transpose(0, 2, 1))
    mamba_out = (results["mamba_base"] + carried).astype(jnp.bfloat16).reshape(tok_rows, width)
    return (mamba_out, results["attention_core"])


def solution(mesh):
    in_specs = (
        P(("group", "seq"), "head"),
        P("head", ("group", "seq")),
        P("head"),
        P("head"),
        P(("group", "seq"), None),
        P(("group", "seq"), None),
        P(("group", "seq"), "head"),
        P(("group", "seq"), "head"),
        P(("group", "seq"), "head"),
    )
    out_specs = (P(("group", "seq"), "head"), P(("group", "seq"), "head"))
    return jax.shard_map(local, mesh=mesh, in_specs=in_specs, out_specs=out_specs, check_vma=False)
```

```python
import jax
import jax.numpy as jnp
from jax import lax
from jax.experimental import pallas as pl
from jax.experimental.pallas import tpu as pltpu
from jax.sharding import PartitionSpec as P

BLOCK = 128
HEADDIM = 64
STATE = 128
QHEADS = 16
KVHEADS = 4
HD = 128


NEG = -1e30


def spread(a):
    return jnp.repeat(a, HEADDIM, axis=-1)


def decay_scan(decay, count, mine):
    excl = jnp.ones_like(decay)
    total = decay
    steps = []
    span = 1
    while span < count:
        lower = (mine // span) % 2 == 1
        got = lax.ppermute(total, "seq", [(i, i ^ span) for i in range(count)])
        steps.append((lower, excl, total, got))
        excl = jnp.where(lower, got * excl, excl)
        total = total * got
        span *= 2
    return steps, excl, total


def entering_states(decay, block_state, count, mine, hooks, parts):
    steps, excl_decay, total_decay = decay_scan(decay, count, mine)
    heads, width = decay.shape[1], block_state.shape[2]
    head_cut, width_cut = heads // parts, width // parts
    totals = [block_state[:, :, j * width_cut : (j + 1) * width_cut] for j in range(parts)]
    excls = [jnp.zeros_like(t) for t in totals]
    results = {}
    span = 1
    for step, known_all in enumerate(steps):
        pairs = [(i, i ^ span) for i in range(count)]
        gots = []
        for j in range(parts):
            hook = hooks.get((j, step if step + 1 < len(steps) else -1))
            tie = gots[-1] if gots else ()
            totals[j], known, args, tie = lax.optimization_barrier(
                (totals[j], known_all, hook[1] if hook else (), tie)
            )
            if gots:
                gots[-1] = tie
            got = lax.ppermute(totals[j].astype(jnp.bfloat16), "seq", pairs).astype(jnp.float32)
            if hook is not None:
                done = hook[0](*args)
                got, done = lax.optimization_barrier((got, done))
                results[hook[0].__name__] = done
            gots.append(got)
        lower = known_all[0]
        for j in range(parts):
            unused, excl_a, own_a, got_a = [
                v if v.ndim == 0 else v[:, j * head_cut : (j + 1) * head_cut] for v in known_all
            ]
            got = gots[j]
            excls[j] = jnp.where(lower, spread(excl_a)[:, None, :] * got + excls[j], excls[j])
            totals[j] = jnp.where(
                lower,
                spread(own_a)[:, None, :] * got + totals[j],
                spread(got_a)[:, None, :] * totals[j] + got,
            )
        span *= 2
    entering = []
    for j in range(parts):
        carry = jnp.zeros_like(totals[j][0])
        rows = []
        for slot in range(decay.shape[0]):
            a_excl = excl_decay[slot, j * head_cut : (j + 1) * head_cut]
            a_total = total_decay[slot, j * head_cut : (j + 1) * head_cut]
            rows.append(spread(a_excl)[None, :] * carry + excls[j][slot])
            carry = spread(a_total)[None, :] * carry + totals[j][slot]
        entering.append(jnp.stack(rows, axis=0))
    return (entering, results)


def mamba_base_kernel(x_ref, inner_ref, cum_row_ref, cum_col_ref, step_ref, skip_ref, o_ref):
    causal = lax.broadcasted_iota(jnp.int32, (BLOCK, BLOCK), 0) >= lax.broadcasted_iota(
        jnp.int32, (BLOCK, BLOCK), 1
    )
    inner = inner_ref[0]
    for e in range(cum_row_ref.shape[1]):
        log_gap = jnp.where(causal, cum_col_ref[0, e] - cum_row_ref[0, e], -jnp.inf)
        mixing = (inner * jnp.exp(log_gap) * step_ref[0, e]).astype(jnp.bfloat16)
        x_head = x_ref[:, e * HEADDIM : (e + 1) * HEADDIM]
        intra = jnp.dot(mixing, x_head, preferred_element_type=jnp.float32)
        skip = skip_ref[:, e * HEADDIM : (e + 1) * HEADDIM] * x_head.astype(jnp.float32)
        o_ref[0, :, e * HEADDIM : (e + 1) * HEADDIM] = intra + skip


def mamba_base(x_in, steps, cum, b_blocks, c_blocks, d_skip):
    slots, heads = steps.shape[:2]
    width = x_in.shape[1]
    pair = 128 // HEADDIM
    inner = jnp.einsum("cin,cjn->cij", c_blocks, b_blocks, preferred_element_type=jnp.float32)
    cum_row = cum[:, :, None, :]
    cum_col = cum[:, :, :, None]
    step_row = steps[:, :, None, :]
    skip_row = spread(d_skip)[None, :]
    cost = pl.CostEstimate(
        flops=2 * slots * heads * BLOCK * BLOCK * (HEADDIM + 3),
        transcendentals=slots * heads * BLOCK * BLOCK,
        bytes_accessed=x_in.size * 2 + slots * BLOCK * width * 4,
    )
    return pl.pallas_call(
        mamba_base_kernel,
        out_shape=jax.ShapeDtypeStruct((slots, BLOCK, width), jnp.float32),
        grid=(slots, heads // pair),
        in_specs=[
            pl.BlockSpec((BLOCK, pair * HEADDIM), lambda c, g: (c, g)),
            pl.BlockSpec((1, BLOCK, BLOCK), lambda c, g: (c, 0, 0)),
            pl.BlockSpec((1, pair, 1, BLOCK), lambda c, g: (c, g, 0, 0)),
            pl.BlockSpec((1, pair, BLOCK, 1), lambda c, g: (c, g, 0, 0)),
            pl.BlockSpec((1, pair, 1, BLOCK), lambda c, g: (c, g, 0, 0)),
            pl.BlockSpec((1, pair * HEADDIM), lambda c, g: (0, g)),
        ],
        out_specs=pl.BlockSpec((1, BLOCK, pair * HEADDIM), lambda c, g: (c, 0, g)),
        cost_estimate=cost,
    )(x_in, inner, cum_row, cum_col, step_row, skip_row)


KEY_CHUNK = 256


def attention_kernel(q_ref, k_ref, v_ref, o_ref):
    seq_count = lax.axis_size("seq")
    me = lax.axis_index("seq")
    slot = pl.program_id(1)
    per_kv = q_ref.shape[1] // HD
    rows = per_kv * BLOCK
    held = k_ref.shape[1]
    first = (slot * seq_count + me) * BLOCK
    chunks = (first + BLOCK + KEY_CHUNK - 1) // KEY_CHUNK
    q = jnp.concatenate([q_ref[:, j * HD : (j + 1) * HD] for j in range(per_kv)], axis=0)
    query_pos = first + lax.broadcasted_iota(jnp.int32, (rows, KEY_CHUNK), 0) % BLOCK
    key_col = lax.broadcasted_iota(jnp.int32, (rows, KEY_CHUNK), 1)
    score_scale = 1.0 / HD**0.5

    def place(c):
        start = c * KEY_CHUNK
        return start, start // held, pl.multiple_of(start % held, KEY_CHUNK)

    def scores(c):
        start, at_slot, at_row = place(c)
        k = k_ref[at_slot, pl.ds(at_row, KEY_CHUNK), :]
        s = lax.dot_general(q, k, (((1,), (1,)), ((), ())), preferred_element_type=jnp.float32)
        return s * score_scale, start + key_col <= query_pos

    def top_of(c, top):
        s, visible = scores(c)
        return jnp.maximum(top, jnp.max(jnp.where(visible, s, NEG), axis=1, keepdims=True))

    top = lax.fori_loop(0, chunks, top_of, jnp.full((rows, 1), NEG, jnp.float32))

    def add_of(c, carry):
        total, acc = carry
        s, visible = scores(c)
        probs = jnp.where(visible, jnp.exp(s - top), 0.0)
        unused, at_slot, at_row = place(c)
        v = v_ref[at_slot, pl.ds(at_row, KEY_CHUNK), :]
        acc = acc + jnp.dot(probs.astype(jnp.bfloat16), v, preferred_element_type=jnp.float32)
        return (total + jnp.sum(probs, axis=1, keepdims=True), acc)

    start_carry = (jnp.zeros((rows, 1), jnp.float32), jnp.zeros((rows, HD), jnp.float32))
    total, acc = lax.fori_loop(0, chunks, add_of, start_carry)
    out = (acc / total).astype(o_ref.dtype)
    for j in range(per_kv):
        o_ref[:, j * HD : (j + 1) * HD] = out[j * BLOCK : (j + 1) * BLOCK]


def attention_core(queries, kv_piece):
    tok_rows, width = queries.shape
    slots, held, unused = kv_piece.shape
    kv_local = kv_piece.shape[2] // (2 * HD)
    group_width = width // kv_local
    keys = slots * held
    cost = pl.CostEstimate(
        flops=4 * tok_rows * width * keys,
        transcendentals=tok_rows * width * keys // HD,
        bytes_accessed=2 * (2 * queries.size + kv_piece.size),
    )
    return pl.pallas_call(
        attention_kernel,
        out_shape=jax.ShapeDtypeStruct(queries.shape, jnp.bfloat16),
        grid=(kv_local, slots),
        in_specs=[
            pl.BlockSpec((BLOCK, group_width), lambda g, s: (s, g)),
            pl.BlockSpec((slots, held, HD), lambda g, s: (0, 0, g)),
            pl.BlockSpec((slots, held, HD), lambda g, s: (0, 0, kv_local + g)),
        ],
        out_specs=pl.BlockSpec((BLOCK, group_width), lambda g, s: (s, g)),
        cost_estimate=cost,
    )(queries, kv_piece, kv_piece)


def local(x_in, step_size, a_log, d_skip, b_in, c_in, queries, key_rows, values):
    my_index = lax.axis_index("seq")
    seq_count = lax.axis_size("seq")
    tok_rows, width = x_in.shape
    slots = tok_rows // BLOCK
    heads = step_size.shape[0]
    kv_cat = jnp.concatenate(
        [key_rows.reshape(slots, BLOCK, -1), values.reshape(slots, BLOCK, -1)], axis=2
    )
    kv_cat, x_in, step_size = lax.optimization_barrier((kv_cat, x_in, step_size))
    kv_piece = lax.all_gather(kv_cat, "seq", axis=1, tiled=True)
    rate = -jnp.exp(a_log)
    steps = step_size.reshape(heads, slots, BLOCK).transpose(1, 0, 2)
    cum = jnp.cumsum(steps * rate[None, :, None], axis=2)
    log_total = cum[:, :, -1]
    factor = (jnp.exp(log_total[:, :, None] - cum) * steps).transpose(0, 2, 1)
    x3 = x_in.reshape(slots, BLOCK, width)
    scaled = (spread(factor) * x3.astype(jnp.float32)).astype(jnp.bfloat16)
    b_blocks = b_in.reshape(slots, BLOCK, STATE)
    c_blocks = c_in.reshape(slots, BLOCK, STATE)
    block_state = jnp.einsum("ctn,ctk->cnk", b_blocks, scaled, preferred_element_type=jnp.float32)
    decay = jnp.exp(log_total)
    parts = 2 if heads % 2 == 0 else 1
    hooks = {
        (1, 0): (mamba_base, (x_in, steps, cum, b_blocks, c_blocks, d_skip)),
        (0, -1): (attention_core, (queries, kv_piece)),
    }
    incoming, results = entering_states(decay, block_state, seq_count, my_index, hooks, parts)
    c_wide = c_blocks.astype(jnp.float32)
    carried = jnp.concatenate(
        [
            jnp.einsum("ctn,cnk->ctk", c_wide, part, precision=lax.Precision.HIGHEST)
            for part in incoming
        ],
        axis=2,
    )
    carried = carried * spread(jnp.exp(cum).transpose(0, 2, 1))
    mamba_out = (results["mamba_base"] + carried).astype(jnp.bfloat16).reshape(tok_rows, width)
    return (mamba_out, results["attention_core"])


def solution(mesh):
    in_specs = (
        P(("group", "seq"), "head"),
        P("head", ("group", "seq")),
        P("head"),
        P("head"),
        P(("group", "seq"), None),
        P(("group", "seq"), None),
        P(("group", "seq"), "head"),
        P(("group", "seq"), "head"),
        P(("group", "seq"), "head"),
    )
    out_specs = (P(("group", "seq"), "head"), P(("group", "seq"), "head"))
    return jax.shard_map(local, mesh=mesh, in_specs=in_specs, out_specs=out_specs, check_vma=False)
```

```python
import jax
import jax.numpy as jnp
from jax import lax
from jax.experimental import pallas as pl
from jax.experimental.pallas import tpu as pltpu
from jax.sharding import PartitionSpec as P

BLOCK = 128
HEADDIM = 64
STATE = 128
QHEADS = 16
KVHEADS = 4
HD = 128


NEG = -1e30


def spread(a):
    return jnp.repeat(a, HEADDIM, axis=-1)


def decay_scan(decay, count, mine):
    excl = jnp.ones_like(decay)
    total = decay
    steps = []
    span = 1
    while span < count:
        lower = (mine // span) % 2 == 1
        got = lax.ppermute(total, "seq", [(i, i ^ span) for i in range(count)])
        steps.append((lower, excl, total, got))
        excl = jnp.where(lower, got * excl, excl)
        total = total * got
        span *= 2
    return steps, excl, total


def entering_states(decay, block_state, count, mine, hooks, parts):
    steps, excl_decay, total_decay = decay_scan(decay, count, mine)
    heads, width = decay.shape[1], block_state.shape[2]
    head_cut, width_cut = heads // parts, width // parts
    totals = [block_state[:, :, j * width_cut : (j + 1) * width_cut] for j in range(parts)]
    excls = [jnp.zeros_like(t) for t in totals]
    results = {}
    span = 1
    for step, known_all in enumerate(steps):
        pairs = [(i, i ^ span) for i in range(count)]
        gots = []
        for j in range(parts):
            hook = hooks.get((j, step if step + 1 < len(steps) else -1))
            tie = gots[-1] if gots else ()
            totals[j], known, args, tie = lax.optimization_barrier(
                (totals[j], known_all, hook[1] if hook else (), tie)
            )
            if gots:
                gots[-1] = tie
            got = lax.ppermute(totals[j].astype(jnp.bfloat16), "seq", pairs).astype(jnp.float32)
            if hook is not None:
                done = hook[0](*args)
                got, done = lax.optimization_barrier((got, done))
                results[hook[0].__name__] = done
            gots.append(got)
        lower = known_all[0]
        for j in range(parts):
            unused, excl_a, own_a, got_a = [
                v if v.ndim == 0 else v[:, j * head_cut : (j + 1) * head_cut] for v in known_all
            ]
            got = gots[j]
            excls[j] = jnp.where(lower, spread(excl_a)[:, None, :] * got + excls[j], excls[j])
            totals[j] = jnp.where(
                lower,
                spread(own_a)[:, None, :] * got + totals[j],
                spread(got_a)[:, None, :] * totals[j] + got,
            )
        span *= 2
    entering = []
    for j in range(parts):
        carry = jnp.zeros_like(totals[j][0])
        rows = []
        for slot in range(decay.shape[0]):
            a_excl = excl_decay[slot, j * head_cut : (j + 1) * head_cut]
            a_total = total_decay[slot, j * head_cut : (j + 1) * head_cut]
            rows.append(spread(a_excl)[None, :] * carry + excls[j][slot])
            carry = spread(a_total)[None, :] * carry + totals[j][slot]
        entering.append(jnp.stack(rows, axis=0))
    return (entering, results)


def mamba_base_kernel(x_ref, inner_ref, cum_ref, step_ref, skip_ref, o_ref):
    rows = lax.broadcasted_iota(jnp.int32, (BLOCK, BLOCK), 0)
    cols = lax.broadcasted_iota(jnp.int32, (BLOCK, BLOCK), 1)
    causal = rows >= cols
    inner = inner_ref[0]
    for e in range(cum_ref.shape[1]):
        cum_row = cum_ref[0, e]
        cum_col = jnp.sum(jnp.where(rows == cols, cum_row, 0.0), axis=1, keepdims=True)
        log_gap = jnp.where(causal, cum_col - cum_row, -jnp.inf)
        mixing = (inner * jnp.exp(log_gap) * step_ref[0, e]).astype(jnp.bfloat16)
        x_head = x_ref[:, e * HEADDIM : (e + 1) * HEADDIM]
        intra = jnp.dot(mixing, x_head, preferred_element_type=jnp.float32)
        skip = skip_ref[:, e * HEADDIM : (e + 1) * HEADDIM] * x_head.astype(jnp.float32)
        o_ref[0, :, e * HEADDIM : (e + 1) * HEADDIM] = intra + skip


def mamba_base(x_in, steps, cum, b_blocks, c_blocks, d_skip):
    slots, heads = steps.shape[:2]
    width = x_in.shape[1]
    group = 8 if heads % 8 == 0 else 128 // HEADDIM
    inner = jnp.einsum("cin,cjn->cij", c_blocks, b_blocks, preferred_element_type=jnp.float32)
    cum_row = cum[:, :, None, :]
    step_row = steps[:, :, None, :]
    skip_row = spread(d_skip)[None, :]
    cost = pl.CostEstimate(
        flops=2 * slots * heads * BLOCK * BLOCK * (HEADDIM + 3),
        transcendentals=slots * heads * BLOCK * BLOCK,
        bytes_accessed=x_in.size * 2 + slots * BLOCK * width * 4,
    )
    return pl.pallas_call(
        mamba_base_kernel,
        out_shape=jax.ShapeDtypeStruct((slots, BLOCK, width), jnp.float32),
        grid=(slots, heads // group),
        in_specs=[
            pl.BlockSpec((BLOCK, group * HEADDIM), lambda c, g: (c, g)),
            pl.BlockSpec((1, BLOCK, BLOCK), lambda c, g: (c, 0, 0)),
            pl.BlockSpec((1, group, 1, BLOCK), lambda c, g: (c, g, 0, 0)),
            pl.BlockSpec((1, group, 1, BLOCK), lambda c, g: (c, g, 0, 0)),
            pl.BlockSpec((1, group * HEADDIM), lambda c, g: (0, g)),
        ],
        out_specs=pl.BlockSpec((1, BLOCK, group * HEADDIM), lambda c, g: (c, 0, g)),
        cost_estimate=cost,
    )(x_in, inner, cum_row, step_row, skip_row)


KEY_CHUNK = 256


def attention_kernel(q_ref, k_ref, v_ref, o_ref):
    seq_count = lax.axis_size("seq")
    me = lax.axis_index("seq")
    slot = pl.program_id(1)
    per_kv = q_ref.shape[1] // HD
    rows = per_kv * BLOCK
    held = k_ref.shape[1]
    first = (slot * seq_count + me) * BLOCK
    chunks = (first + BLOCK + KEY_CHUNK - 1) // KEY_CHUNK
    q = jnp.concatenate([q_ref[:, j * HD : (j + 1) * HD] for j in range(per_kv)], axis=0)
    query_pos = first + lax.broadcasted_iota(jnp.int32, (rows, KEY_CHUNK), 0) % BLOCK
    key_col = lax.broadcasted_iota(jnp.int32, (rows, KEY_CHUNK), 1)
    score_scale = 1.0 / HD**0.5

    def place(c):
        start = c * KEY_CHUNK
        return start, start // held, pl.multiple_of(start % held, KEY_CHUNK)

    def scores(c):
        start, at_slot, at_row = place(c)
        k = k_ref[at_slot, pl.ds(at_row, KEY_CHUNK), :]
        s = lax.dot_general(q, k, (((1,), (1,)), ((), ())), preferred_element_type=jnp.float32)
        return s * score_scale, start + key_col <= query_pos

    def top_of(c, top):
        s, visible = scores(c)
        return jnp.maximum(top, jnp.max(jnp.where(visible, s, NEG), axis=1, keepdims=True))

    top = lax.fori_loop(0, chunks, top_of, jnp.full((rows, 1), NEG, jnp.float32))

    def add_of(c, carry):
        total, acc = carry
        s, visible = scores(c)
        probs = jnp.where(visible, jnp.exp(s - top), 0.0)
        unused, at_slot, at_row = place(c)
        v = v_ref[at_slot, pl.ds(at_row, KEY_CHUNK), :]
        acc = acc + jnp.dot(probs.astype(jnp.bfloat16), v, preferred_element_type=jnp.float32)
        return (total + jnp.sum(probs, axis=1, keepdims=True), acc)

    start_carry = (jnp.zeros((rows, 1), jnp.float32), jnp.zeros((rows, HD), jnp.float32))
    total, acc = lax.fori_loop(0, chunks, add_of, start_carry)
    out = (acc / total).astype(o_ref.dtype)
    for j in range(per_kv):
        o_ref[:, j * HD : (j + 1) * HD] = out[j * BLOCK : (j + 1) * BLOCK]


def attention_core(queries, kv_piece):
    tok_rows, width = queries.shape
    slots, held, unused = kv_piece.shape
    kv_local = kv_piece.shape[2] // (2 * HD)
    group_width = width // kv_local
    keys = slots * held
    cost = pl.CostEstimate(
        flops=4 * tok_rows * width * keys,
        transcendentals=tok_rows * width * keys // HD,
        bytes_accessed=2 * (2 * queries.size + kv_piece.size),
    )
    return pl.pallas_call(
        attention_kernel,
        out_shape=jax.ShapeDtypeStruct(queries.shape, jnp.bfloat16),
        grid=(kv_local, slots),
        in_specs=[
            pl.BlockSpec((BLOCK, group_width), lambda g, s: (s, g)),
            pl.BlockSpec((slots, held, HD), lambda g, s: (0, 0, g)),
            pl.BlockSpec((slots, held, HD), lambda g, s: (0, 0, kv_local + g)),
        ],
        out_specs=pl.BlockSpec((BLOCK, group_width), lambda g, s: (s, g)),
        cost_estimate=cost,
    )(queries, kv_piece, kv_piece)


def local(x_in, step_size, a_log, d_skip, b_in, c_in, queries, key_rows, values):
    my_index = lax.axis_index("seq")
    seq_count = lax.axis_size("seq")
    tok_rows, width = x_in.shape
    slots = tok_rows // BLOCK
    heads = step_size.shape[0]
    kv_cat = jnp.concatenate(
        [key_rows.reshape(slots, BLOCK, -1), values.reshape(slots, BLOCK, -1)], axis=2
    )
    kv_cat, x_in, step_size = lax.optimization_barrier((kv_cat, x_in, step_size))
    kv_piece = lax.all_gather(kv_cat, "seq", axis=1, tiled=True)
    rate = -jnp.exp(a_log)
    steps = step_size.reshape(heads, slots, BLOCK).transpose(1, 0, 2)
    cum = jnp.cumsum(steps * rate[None, :, None], axis=2)
    log_total = cum[:, :, -1]
    factor = (jnp.exp(log_total[:, :, None] - cum) * steps).transpose(0, 2, 1)
    x3 = x_in.reshape(slots, BLOCK, width)
    scaled = (spread(factor) * x3.astype(jnp.float32)).astype(jnp.bfloat16)
    b_blocks = b_in.reshape(slots, BLOCK, STATE)
    c_blocks = c_in.reshape(slots, BLOCK, STATE)
    block_state = jnp.einsum("ctn,ctk->cnk", b_blocks, scaled, preferred_element_type=jnp.float32)
    decay = jnp.exp(log_total)
    parts = 2 if heads % 2 == 0 else 1
    hooks = {
        (1, 0): (mamba_base, (x_in, steps, cum, b_blocks, c_blocks, d_skip)),
        (0, -1): (attention_core, (queries, kv_piece)),
    }
    incoming, results = entering_states(decay, block_state, seq_count, my_index, hooks, parts)
    c_wide = c_blocks.astype(jnp.float32)
    carried = jnp.concatenate(
        [
            jnp.einsum("ctn,cnk->ctk", c_wide, part, precision=lax.Precision.HIGHEST)
            for part in incoming
        ],
        axis=2,
    )
    carried = carried * spread(jnp.exp(cum).transpose(0, 2, 1))
    mamba_out = (results["mamba_base"] + carried).astype(jnp.bfloat16).reshape(tok_rows, width)
    return (mamba_out, results["attention_core"])


def solution(mesh):
    in_specs = (
        P(("group", "seq"), "head"),
        P("head", ("group", "seq")),
        P("head"),
        P("head"),
        P(("group", "seq"), None),
        P(("group", "seq"), None),
        P(("group", "seq"), "head"),
        P(("group", "seq"), "head"),
        P(("group", "seq"), "head"),
    )
    out_specs = (P(("group", "seq"), "head"), P(("group", "seq"), "head"))
    return jax.shard_map(local, mesh=mesh, in_specs=in_specs, out_specs=out_specs, check_vma=False)
```

```python
import jax
import jax.numpy as jnp
from jax import lax
from jax.experimental import pallas as pl
from jax.experimental.pallas import tpu as pltpu
from jax.sharding import PartitionSpec as P

BLOCK = 128
HEADDIM = 64
STATE = 128
QHEADS = 16
KVHEADS = 4
HD = 128


NEG = -1e30


def spread(a):
    return jnp.repeat(a, HEADDIM, axis=-1)


def decay_scan(decay, count, mine):
    excl = jnp.ones_like(decay)
    total = decay
    steps = []
    span = 1
    while span < count:
        lower = (mine // span) % 2 == 1
        got = lax.ppermute(total, "seq", [(i, i ^ span) for i in range(count)])
        steps.append((lower, excl, total, got))
        excl = jnp.where(lower, got * excl, excl)
        total = total * got
        span *= 2
    return steps, excl, total


def entering_states(decay, block_state, count, mine, hooks, parts):
    steps, excl_decay, total_decay = decay_scan(decay, count, mine)
    heads, width = decay.shape[1], block_state.shape[2]
    head_cut, width_cut = heads // parts, width // parts
    totals = [block_state[:, :, j * width_cut : (j + 1) * width_cut] for j in range(parts)]
    excls = [jnp.zeros_like(t) for t in totals]
    results = {}
    span = 1
    for step, known_all in enumerate(steps):
        pairs = [(i, i ^ span) for i in range(count)]
        gots = []
        for j in range(parts):
            hook = hooks.get((j, step if step + 1 < len(steps) else -1))
            tie = gots[-1] if gots else ()
            totals[j], known, args, tie = lax.optimization_barrier(
                (totals[j], known_all, hook[1] if hook else (), tie)
            )
            if gots:
                gots[-1] = tie
            got = lax.ppermute(totals[j].astype(jnp.bfloat16), "seq", pairs).astype(jnp.float32)
            if hook is not None:
                done = hook[0](*args)
                got, done = lax.optimization_barrier((got, done))
                results[hook[0].__name__] = done
            gots.append(got)
        lower = known_all[0]
        for j in range(parts):
            unused, excl_a, own_a, got_a = [
                v if v.ndim == 0 else v[:, j * head_cut : (j + 1) * head_cut] for v in known_all
            ]
            got = gots[j]
            excls[j] = jnp.where(lower, spread(excl_a)[:, None, :] * got + excls[j], excls[j])
            totals[j] = jnp.where(
                lower,
                spread(own_a)[:, None, :] * got + totals[j],
                spread(got_a)[:, None, :] * totals[j] + got,
            )
        span *= 2
    entering = []
    for j in range(parts):
        carry = jnp.zeros_like(totals[j][0])
        rows = []
        for slot in range(decay.shape[0]):
            a_excl = excl_decay[slot, j * head_cut : (j + 1) * head_cut]
            a_total = total_decay[slot, j * head_cut : (j + 1) * head_cut]
            rows.append(spread(a_excl)[None, :] * carry + excls[j][slot])
            carry = spread(a_total)[None, :] * carry + totals[j][slot]
        entering.append(jnp.stack(rows, axis=0))
    return (entering, results)


def mamba_base_kernel(x_ref, inner_ref, cum_ref, step_ref, skip_ref, o_ref):
    rows = lax.broadcasted_iota(jnp.int32, (BLOCK, BLOCK), 0)
    cols = lax.broadcasted_iota(jnp.int32, (BLOCK, BLOCK), 1)
    causal = rows >= cols
    inner = inner_ref[0]
    for e in range(cum_ref.shape[1]):
        cum_row = cum_ref[0, e]
        cum_col = jnp.sum(jnp.where(rows == cols, cum_row, 0.0), axis=1, keepdims=True)
        log_gap = jnp.where(causal, cum_col - cum_row, -jnp.inf)
        mixing = (inner * jnp.exp(log_gap) * step_ref[0, e]).astype(jnp.bfloat16)
        x_head = x_ref[:, e * HEADDIM : (e + 1) * HEADDIM]
        intra = jnp.dot(mixing, x_head, preferred_element_type=jnp.float32)
        skip = skip_ref[:, e * HEADDIM : (e + 1) * HEADDIM] * x_head.astype(jnp.float32)
        o_ref[0, :, e * HEADDIM : (e + 1) * HEADDIM] = intra + skip


def mamba_base(x_in, steps, cum, b_blocks, c_blocks, d_skip):
    slots, heads = steps.shape[:2]
    width = x_in.shape[1]
    group = 8 if heads % 8 == 0 else 128 // HEADDIM
    inner = jnp.einsum("cin,cjn->cij", c_blocks, b_blocks, preferred_element_type=jnp.float32)
    cum_row = cum[:, :, None, :]
    step_row = steps[:, :, None, :]
    skip_row = spread(d_skip)[None, :]
    cost = pl.CostEstimate(
        flops=2 * slots * heads * BLOCK * BLOCK * (HEADDIM + 3),
        transcendentals=slots * heads * BLOCK * BLOCK,
        bytes_accessed=x_in.size * 2 + slots * BLOCK * width * 4,
    )
    return pl.pallas_call(
        mamba_base_kernel,
        out_shape=jax.ShapeDtypeStruct((slots, BLOCK, width), jnp.float32),
        grid=(slots, heads // group),
        in_specs=[
            pl.BlockSpec((BLOCK, group * HEADDIM), lambda c, g: (c, g)),
            pl.BlockSpec((1, BLOCK, BLOCK), lambda c, g: (c, 0, 0)),
            pl.BlockSpec((1, group, 1, BLOCK), lambda c, g: (c, g, 0, 0)),
            pl.BlockSpec((1, group, 1, BLOCK), lambda c, g: (c, g, 0, 0)),
            pl.BlockSpec((1, group * HEADDIM), lambda c, g: (0, g)),
        ],
        out_specs=pl.BlockSpec((1, BLOCK, group * HEADDIM), lambda c, g: (c, 0, g)),
        cost_estimate=cost,
    )(x_in, inner, cum_row, step_row, skip_row)


KEY_CHUNK = 256


def attention_kernel(q_ref, k_ref, v_ref, o_ref):
    seq_count = lax.axis_size("seq")
    me = lax.axis_index("seq")
    slot = pl.program_id(1)
    per_kv = q_ref.shape[1] // HD
    rows = per_kv * BLOCK
    held = k_ref.shape[1]
    first = (slot * seq_count + me) * BLOCK
    chunks = (first + BLOCK + KEY_CHUNK - 1) // KEY_CHUNK
    q = jnp.concatenate([q_ref[:, j * HD : (j + 1) * HD] for j in range(per_kv)], axis=0)
    query_pos = first + lax.broadcasted_iota(jnp.int32, (rows, KEY_CHUNK), 0) % BLOCK
    key_col = lax.broadcasted_iota(jnp.int32, (rows, KEY_CHUNK), 1)
    score_scale = 1.0 / HD**0.5

    def place(c):
        start = c * KEY_CHUNK
        return start, start // held, pl.multiple_of(start % held, KEY_CHUNK)

    def scores(c):
        start, at_slot, at_row = place(c)
        k = k_ref[at_slot, pl.ds(at_row, KEY_CHUNK), :]
        s = lax.dot_general(q, k, (((1,), (1,)), ((), ())), preferred_element_type=jnp.float32)
        return s * score_scale, start + key_col <= query_pos

    def top_of(c, top):
        s, visible = scores(c)
        return jnp.maximum(top, jnp.max(jnp.where(visible, s, NEG), axis=1, keepdims=True))

    top = lax.fori_loop(0, chunks, top_of, jnp.full((rows, 1), NEG, jnp.float32))

    def add_of(c, carry):
        total, acc = carry
        s, visible = scores(c)
        probs = jnp.where(visible, jnp.exp(s - top), 0.0)
        unused, at_slot, at_row = place(c)
        v = v_ref[at_slot, pl.ds(at_row, KEY_CHUNK), :]
        acc = acc + jnp.dot(probs.astype(jnp.bfloat16), v, preferred_element_type=jnp.float32)
        return (total + jnp.sum(probs, axis=1, keepdims=True), acc)

    start_carry = (jnp.zeros((rows, 1), jnp.float32), jnp.zeros((rows, HD), jnp.float32))
    total, acc = lax.fori_loop(0, chunks, add_of, start_carry)
    out = (acc / total).astype(o_ref.dtype)
    for j in range(per_kv):
        o_ref[:, j * HD : (j + 1) * HD] = out[j * BLOCK : (j + 1) * BLOCK]


def attention_core(queries, kv_piece):
    tok_rows, width = queries.shape
    slots, held, unused = kv_piece.shape
    kv_local = kv_piece.shape[2] // (2 * HD)
    group_width = width // kv_local
    keys = slots * held
    cost = pl.CostEstimate(
        flops=4 * tok_rows * width * keys,
        transcendentals=tok_rows * width * keys // HD,
        bytes_accessed=2 * (2 * queries.size + kv_piece.size),
    )
    return pl.pallas_call(
        attention_kernel,
        out_shape=jax.ShapeDtypeStruct(queries.shape, jnp.bfloat16),
        grid=(kv_local, slots),
        in_specs=[
            pl.BlockSpec((BLOCK, group_width), lambda g, s: (s, g)),
            pl.BlockSpec((slots, held, HD), lambda g, s: (0, 0, g)),
            pl.BlockSpec((slots, held, HD), lambda g, s: (0, 0, kv_local + g)),
        ],
        out_specs=pl.BlockSpec((BLOCK, group_width), lambda g, s: (s, g)),
        cost_estimate=cost,
    )(queries, kv_piece, kv_piece)


def local(x_in, step_size, a_log, d_skip, b_in, c_in, queries, key_rows, values):
    my_index = lax.axis_index("seq")
    seq_count = lax.axis_size("seq")
    tok_rows, width = x_in.shape
    slots = tok_rows // BLOCK
    heads = step_size.shape[0]
    kv_cat = jnp.concatenate(
        [key_rows.reshape(slots, BLOCK, -1), values.reshape(slots, BLOCK, -1)], axis=2
    )
    kv_cat, x_in, step_size = lax.optimization_barrier((kv_cat, x_in, step_size))
    kv_piece = lax.all_gather(kv_cat, "seq", axis=1, tiled=True)
    rate = -jnp.exp(a_log)
    steps = step_size.reshape(heads, slots, BLOCK).transpose(1, 0, 2)
    cum = jnp.cumsum(steps * rate[None, :, None], axis=2)
    log_total = cum[:, :, -1]
    factor = (jnp.exp(log_total[:, :, None] - cum) * steps).transpose(0, 2, 1)
    x3 = x_in.reshape(slots, BLOCK, width)
    scaled = (spread(factor) * x3.astype(jnp.float32)).astype(jnp.bfloat16)
    b_blocks = b_in.reshape(slots, BLOCK, STATE)
    c_blocks = c_in.reshape(slots, BLOCK, STATE)
    block_state = jnp.einsum("ctn,ctk->cnk", b_blocks, scaled, preferred_element_type=jnp.float32)
    decay = jnp.exp(log_total)
    parts = 2 if heads % 2 == 0 else 1
    hooks = {
        (0, 0): (mamba_base, (x_in, steps, cum, b_blocks, c_blocks, d_skip)),
        (0, -1): (attention_core, (queries, kv_piece)),
    }
    incoming, results = entering_states(decay, block_state, seq_count, my_index, hooks, parts)
    c_wide = c_blocks.astype(jnp.float32)
    carried = jnp.concatenate(
        [
            jnp.einsum("ctn,cnk->ctk", c_wide, part, precision=lax.Precision.HIGHEST)
            for part in incoming
        ],
        axis=2,
    )
    carried = carried * spread(jnp.exp(cum).transpose(0, 2, 1))
    mamba_out = (results["mamba_base"] + carried).astype(jnp.bfloat16).reshape(tok_rows, width)
    return (mamba_out, results["attention_core"])


def solution(mesh):
    in_specs = (
        P(("group", "seq"), "head"),
        P("head", ("group", "seq")),
        P("head"),
        P("head"),
        P(("group", "seq"), None),
        P(("group", "seq"), None),
        P(("group", "seq"), "head"),
        P(("group", "seq"), "head"),
        P(("group", "seq"), "head"),
    )
    out_specs = (P(("group", "seq"), "head"), P(("group", "seq"), "head"))
    return jax.shard_map(local, mesh=mesh, in_specs=in_specs, out_specs=out_specs, check_vma=False)
```

```python
import jax
import jax.numpy as jnp
from jax import lax
from jax.experimental import pallas as pl
from jax.experimental.pallas import tpu as pltpu
from jax.sharding import PartitionSpec as P

BLOCK = 128
HEADDIM = 64
STATE = 128
QHEADS = 16
KVHEADS = 4
HD = 128


NEG = -1e30


def spread(a):
    return jnp.repeat(a, HEADDIM, axis=-1)


def decay_scan(decay, count, mine):
    excl = jnp.ones_like(decay)
    total = decay
    steps = []
    span = 1
    while span < count:
        lower = (mine // span) % 2 == 1
        got = lax.ppermute(total, "seq", [(i, i ^ span) for i in range(count)])
        steps.append((lower, excl, total, got))
        excl = jnp.where(lower, got * excl, excl)
        total = total * got
        span *= 2
    return steps, excl, total


def entering_states(decay, block_state, count, mine, hooks, parts):
    steps, excl_decay, total_decay = decay_scan(decay, count, mine)
    heads, width = decay.shape[1], block_state.shape[2]
    head_cut, width_cut = heads // parts, width // parts
    totals = [block_state[:, :, j * width_cut : (j + 1) * width_cut] for j in range(parts)]
    excls = [jnp.zeros_like(t) for t in totals]
    results = {}
    span = 1
    for step, known_all in enumerate(steps):
        pairs = [(i, i ^ span) for i in range(count)]
        gots = []
        for j in range(parts):
            hook = hooks.get((j, step if step + 1 < len(steps) else -1))
            tie = gots[-1] if gots and step + 1 < len(steps) else ()
            totals[j], known, args, tie = lax.optimization_barrier(
                (totals[j], known_all, hook[1] if hook else (), tie)
            )
            if gots and step + 1 < len(steps):
                gots[-1] = tie
            got = lax.ppermute(totals[j].astype(jnp.bfloat16), "seq", pairs).astype(jnp.float32)
            if hook is not None:
                done = hook[0](*args)
                got, done = lax.optimization_barrier((got, done))
                results[hook[0].__name__] = done
            gots.append(got)
        lower = known_all[0]
        for j in range(parts):
            unused, excl_a, own_a, got_a = [
                v if v.ndim == 0 else v[:, j * head_cut : (j + 1) * head_cut] for v in known_all
            ]
            got = gots[j]
            excls[j] = jnp.where(lower, spread(excl_a)[:, None, :] * got + excls[j], excls[j])
            totals[j] = jnp.where(
                lower,
                spread(own_a)[:, None, :] * got + totals[j],
                spread(got_a)[:, None, :] * totals[j] + got,
            )
        span *= 2
    entering = []
    for j in range(parts):
        carry = jnp.zeros_like(totals[j][0])
        rows = []
        for slot in range(decay.shape[0]):
            a_excl = excl_decay[slot, j * head_cut : (j + 1) * head_cut]
            a_total = total_decay[slot, j * head_cut : (j + 1) * head_cut]
            rows.append(spread(a_excl)[None, :] * carry + excls[j][slot])
            carry = spread(a_total)[None, :] * carry + totals[j][slot]
        entering.append(jnp.stack(rows, axis=0))
    return (entering, results)


def mamba_base_kernel(x_ref, inner_ref, cum_ref, step_ref, skip_ref, o_ref):
    rows = lax.broadcasted_iota(jnp.int32, (BLOCK, BLOCK), 0)
    cols = lax.broadcasted_iota(jnp.int32, (BLOCK, BLOCK), 1)
    causal = rows >= cols
    inner = inner_ref[0]
    for e in range(cum_ref.shape[1]):
        cum_row = cum_ref[0, e]
        cum_col = jnp.sum(jnp.where(rows == cols, cum_row, 0.0), axis=1, keepdims=True)
        log_gap = jnp.where(causal, cum_col - cum_row, -jnp.inf)
        mixing = (inner * jnp.exp(log_gap) * step_ref[0, e]).astype(jnp.bfloat16)
        x_head = x_ref[:, e * HEADDIM : (e + 1) * HEADDIM]
        intra = jnp.dot(mixing, x_head, preferred_element_type=jnp.float32)
        skip = skip_ref[:, e * HEADDIM : (e + 1) * HEADDIM] * x_head.astype(jnp.float32)
        o_ref[0, :, e * HEADDIM : (e + 1) * HEADDIM] = intra + skip


def mamba_base(x_in, steps, cum, b_blocks, c_blocks, d_skip):
    slots, heads = steps.shape[:2]
    width = x_in.shape[1]
    group = 8 if heads % 8 == 0 else 128 // HEADDIM
    inner = jnp.einsum("cin,cjn->cij", c_blocks, b_blocks, preferred_element_type=jnp.float32)
    cum_row = cum[:, :, None, :]
    step_row = steps[:, :, None, :]
    skip_row = spread(d_skip)[None, :]
    cost = pl.CostEstimate(
        flops=2 * slots * heads * BLOCK * BLOCK * (HEADDIM + 3),
        transcendentals=slots * heads * BLOCK * BLOCK,
        bytes_accessed=x_in.size * 2 + slots * BLOCK * width * 4,
    )
    return pl.pallas_call(
        mamba_base_kernel,
        out_shape=jax.ShapeDtypeStruct((slots, BLOCK, width), jnp.float32),
        grid=(slots, heads // group),
        in_specs=[
            pl.BlockSpec((BLOCK, group * HEADDIM), lambda c, g: (c, g)),
            pl.BlockSpec((1, BLOCK, BLOCK), lambda c, g: (c, 0, 0)),
            pl.BlockSpec((1, group, 1, BLOCK), lambda c, g: (c, g, 0, 0)),
            pl.BlockSpec((1, group, 1, BLOCK), lambda c, g: (c, g, 0, 0)),
            pl.BlockSpec((1, group * HEADDIM), lambda c, g: (0, g)),
        ],
        out_specs=pl.BlockSpec((1, BLOCK, group * HEADDIM), lambda c, g: (c, 0, g)),
        cost_estimate=cost,
    )(x_in, inner, cum_row, step_row, skip_row)


KEY_CHUNK = 256


def attention_kernel(q_ref, k_ref, v_ref, o_ref):
    seq_count = lax.axis_size("seq")
    me = lax.axis_index("seq")
    slot = pl.program_id(1)
    per_kv = q_ref.shape[1] // HD
    rows = per_kv * BLOCK
    held = k_ref.shape[1]
    first = (slot * seq_count + me) * BLOCK
    chunks = (first + BLOCK + KEY_CHUNK - 1) // KEY_CHUNK
    q = jnp.concatenate([q_ref[:, j * HD : (j + 1) * HD] for j in range(per_kv)], axis=0)
    query_pos = first + lax.broadcasted_iota(jnp.int32, (rows, KEY_CHUNK), 0) % BLOCK
    key_col = lax.broadcasted_iota(jnp.int32, (rows, KEY_CHUNK), 1)
    score_scale = 1.0 / HD**0.5

    def place(c):
        start = c * KEY_CHUNK
        return start, start // held, pl.multiple_of(start % held, KEY_CHUNK)

    def scores(c):
        start, at_slot, at_row = place(c)
        k = k_ref[at_slot, pl.ds(at_row, KEY_CHUNK), :]
        s = lax.dot_general(q, k, (((1,), (1,)), ((), ())), preferred_element_type=jnp.float32)
        return s * score_scale, start + key_col <= query_pos

    def top_of(c, top):
        s, visible = scores(c)
        return jnp.maximum(top, jnp.max(jnp.where(visible, s, NEG), axis=1, keepdims=True))

    top = lax.fori_loop(0, chunks, top_of, jnp.full((rows, 1), NEG, jnp.float32))

    def add_of(c, carry):
        total, acc = carry
        s, visible = scores(c)
        probs = jnp.where(visible, jnp.exp(s - top), 0.0)
        unused, at_slot, at_row = place(c)
        v = v_ref[at_slot, pl.ds(at_row, KEY_CHUNK), :]
        acc = acc + jnp.dot(probs.astype(jnp.bfloat16), v, preferred_element_type=jnp.float32)
        return (total + jnp.sum(probs, axis=1, keepdims=True), acc)

    start_carry = (jnp.zeros((rows, 1), jnp.float32), jnp.zeros((rows, HD), jnp.float32))
    total, acc = lax.fori_loop(0, chunks, add_of, start_carry)
    out = (acc / total).astype(o_ref.dtype)
    for j in range(per_kv):
        o_ref[:, j * HD : (j + 1) * HD] = out[j * BLOCK : (j + 1) * BLOCK]


def attention_core(queries, kv_piece):
    tok_rows, width = queries.shape
    slots, held, unused = kv_piece.shape
    kv_local = kv_piece.shape[2] // (2 * HD)
    group_width = width // kv_local
    keys = slots * held
    cost = pl.CostEstimate(
        flops=4 * tok_rows * width * keys,
        transcendentals=tok_rows * width * keys // HD,
        bytes_accessed=2 * (2 * queries.size + kv_piece.size),
    )
    return pl.pallas_call(
        attention_kernel,
        out_shape=jax.ShapeDtypeStruct(queries.shape, jnp.bfloat16),
        grid=(kv_local, slots),
        in_specs=[
            pl.BlockSpec((BLOCK, group_width), lambda g, s: (s, g)),
            pl.BlockSpec((slots, held, HD), lambda g, s: (0, 0, g)),
            pl.BlockSpec((slots, held, HD), lambda g, s: (0, 0, kv_local + g)),
        ],
        out_specs=pl.BlockSpec((BLOCK, group_width), lambda g, s: (s, g)),
        cost_estimate=cost,
    )(queries, kv_piece, kv_piece)


def local(x_in, step_size, a_log, d_skip, b_in, c_in, queries, key_rows, values):
    my_index = lax.axis_index("seq")
    seq_count = lax.axis_size("seq")
    tok_rows, width = x_in.shape
    slots = tok_rows // BLOCK
    heads = step_size.shape[0]
    kv_cat = jnp.concatenate(
        [key_rows.reshape(slots, BLOCK, -1), values.reshape(slots, BLOCK, -1)], axis=2
    )
    kv_cat, x_in, step_size = lax.optimization_barrier((kv_cat, x_in, step_size))
    kv_piece = lax.all_gather(kv_cat, "seq", axis=1, tiled=True)
    rate = -jnp.exp(a_log)
    steps = step_size.reshape(heads, slots, BLOCK).transpose(1, 0, 2)
    cum = jnp.cumsum(steps * rate[None, :, None], axis=2)
    log_total = cum[:, :, -1]
    factor = (jnp.exp(log_total[:, :, None] - cum) * steps).transpose(0, 2, 1)
    x3 = x_in.reshape(slots, BLOCK, width)
    scaled = (spread(factor) * x3.astype(jnp.float32)).astype(jnp.bfloat16)
    b_blocks = b_in.reshape(slots, BLOCK, STATE)
    c_blocks = c_in.reshape(slots, BLOCK, STATE)
    block_state = jnp.einsum("ctn,ctk->cnk", b_blocks, scaled, preferred_element_type=jnp.float32)
    decay = jnp.exp(log_total)
    parts = 2 if heads % 2 == 0 else 1
    hooks = {
        (1, 0): (mamba_base, (x_in, steps, cum, b_blocks, c_blocks, d_skip)),
        (1, 1): (attention_core, (queries, kv_piece)),
    }
    incoming, results = entering_states(decay, block_state, seq_count, my_index, hooks, parts)
    c_wide = c_blocks.astype(jnp.float32)
    carried = jnp.concatenate(
        [
            jnp.einsum("ctn,cnk->ctk", c_wide, part, precision=lax.Precision.HIGHEST)
            for part in incoming
        ],
        axis=2,
    )
    carried = carried * spread(jnp.exp(cum).transpose(0, 2, 1))
    mamba_out = (results["mamba_base"] + carried).astype(jnp.bfloat16).reshape(tok_rows, width)
    return (mamba_out, results["attention_core"])


def solution(mesh):
    in_specs = (
        P(("group", "seq"), "head"),
        P("head", ("group", "seq")),
        P("head"),
        P("head"),
        P(("group", "seq"), None),
        P(("group", "seq"), None),
        P(("group", "seq"), "head"),
        P(("group", "seq"), "head"),
        P(("group", "seq"), "head"),
    )
    out_specs = (P(("group", "seq"), "head"), P(("group", "seq"), "head"))
    return jax.shard_map(local, mesh=mesh, in_specs=in_specs, out_specs=out_specs, check_vma=False)
```

```python
import jax
import jax.numpy as jnp
from jax import lax
from jax.experimental import pallas as pl
from jax.experimental.pallas import tpu as pltpu
from jax.sharding import PartitionSpec as P

BLOCK = 128
HEADDIM = 64
STATE = 128
QHEADS = 16
KVHEADS = 4
HD = 128


NEG = -1e30


def spread(a):
    return jnp.repeat(a, HEADDIM, axis=-1)


def decay_scan(decay, count, mine):
    excl = jnp.ones_like(decay)
    total = decay
    steps = []
    span = 1
    while span < count:
        lower = (mine // span) % 2 == 1
        got = lax.ppermute(total, "seq", [(i, i ^ span) for i in range(count)])
        steps.append((lower, excl, total, got))
        excl = jnp.where(lower, got * excl, excl)
        total = total * got
        span *= 2
    return steps, excl, total


def entering_states(decay, block_state, count, mine, hooks, parts):
    steps, excl_decay, total_decay = decay_scan(decay, count, mine)
    heads, width = decay.shape[1], block_state.shape[2]
    head_cut, width_cut = heads // parts, width // parts
    totals = [block_state[:, :, j * width_cut : (j + 1) * width_cut] for j in range(parts)]
    excls = [jnp.zeros_like(t) for t in totals]
    results = {}
    span = 1
    for step, known_all in enumerate(steps):
        pairs = [(i, i ^ span) for i in range(count)]
        gots = []
        for j in range(parts):
            hook = hooks.get((j, step if step + 1 < len(steps) else -1))
            tie = gots[-1] if gots and step + 1 < len(steps) else ()
            totals[j], known, args, tie = lax.optimization_barrier(
                (totals[j], known_all, hook[1] if hook else (), tie)
            )
            if gots and step + 1 < len(steps):
                gots[-1] = tie
            got = lax.ppermute(totals[j].astype(jnp.bfloat16), "seq", pairs).astype(jnp.float32)
            if hook is not None:
                done = hook[0](*args)
                got, done = lax.optimization_barrier((got, done))
                results[hook[0].__name__] = done
            gots.append(got)
        lower = known_all[0]
        for j in range(parts):
            unused, excl_a, own_a, got_a = [
                v if v.ndim == 0 else v[:, j * head_cut : (j + 1) * head_cut] for v in known_all
            ]
            got = gots[j]
            excls[j] = jnp.where(lower, spread(excl_a)[:, None, :] * got + excls[j], excls[j])
            totals[j] = jnp.where(
                lower,
                spread(own_a)[:, None, :] * got + totals[j],
                spread(got_a)[:, None, :] * totals[j] + got,
            )
        span *= 2
    entering = []
    for j in range(parts):
        carry = jnp.zeros_like(totals[j][0])
        rows = []
        for slot in range(decay.shape[0]):
            a_excl = excl_decay[slot, j * head_cut : (j + 1) * head_cut]
            a_total = total_decay[slot, j * head_cut : (j + 1) * head_cut]
            rows.append(spread(a_excl)[None, :] * carry + excls[j][slot])
            carry = spread(a_total)[None, :] * carry + totals[j][slot]
        entering.append(jnp.stack(rows, axis=0))
    return (entering, results)


def mamba_base_kernel(x_ref, inner_ref, cum_ref, step_ref, skip_ref, o_ref):
    rows = lax.broadcasted_iota(jnp.int32, (BLOCK, BLOCK), 0)
    cols = lax.broadcasted_iota(jnp.int32, (BLOCK, BLOCK), 1)
    causal = rows >= cols
    inner = inner_ref[0]
    for e in range(cum_ref.shape[1]):
        cum_row = cum_ref[0, e]
        cum_col = jnp.sum(jnp.where(rows == cols, cum_row, 0.0), axis=1, keepdims=True)
        log_gap = jnp.where(causal, cum_col - cum_row, -jnp.inf)
        mixing = (inner * jnp.exp(log_gap) * step_ref[0, e]).astype(jnp.bfloat16)
        x_head = x_ref[:, e * HEADDIM : (e + 1) * HEADDIM]
        intra = jnp.dot(mixing, x_head, preferred_element_type=jnp.float32)
        skip = skip_ref[:, e * HEADDIM : (e + 1) * HEADDIM] * x_head.astype(jnp.float32)
        o_ref[0, :, e * HEADDIM : (e + 1) * HEADDIM] = intra + skip


def mamba_base(x_in, steps, cum, b_blocks, c_blocks, d_skip):
    slots, heads = steps.shape[:2]
    width = x_in.shape[1]
    group = 8 if heads % 8 == 0 else 128 // HEADDIM
    inner = jnp.einsum("cin,cjn->cij", c_blocks, b_blocks, preferred_element_type=jnp.float32)
    cum_row = cum[:, :, None, :]
    step_row = steps[:, :, None, :]
    skip_row = spread(d_skip)[None, :]
    cost = pl.CostEstimate(
        flops=2 * slots * heads * BLOCK * BLOCK * (HEADDIM + 3),
        transcendentals=slots * heads * BLOCK * BLOCK,
        bytes_accessed=x_in.size * 2 + slots * BLOCK * width * 4,
    )
    return pl.pallas_call(
        mamba_base_kernel,
        out_shape=jax.ShapeDtypeStruct((slots, BLOCK, width), jnp.float32),
        grid=(slots, heads // group),
        in_specs=[
            pl.BlockSpec((BLOCK, group * HEADDIM), lambda c, g: (c, g)),
            pl.BlockSpec((1, BLOCK, BLOCK), lambda c, g: (c, 0, 0)),
            pl.BlockSpec((1, group, 1, BLOCK), lambda c, g: (c, g, 0, 0)),
            pl.BlockSpec((1, group, 1, BLOCK), lambda c, g: (c, g, 0, 0)),
            pl.BlockSpec((1, group * HEADDIM), lambda c, g: (0, g)),
        ],
        out_specs=pl.BlockSpec((1, BLOCK, group * HEADDIM), lambda c, g: (c, 0, g)),
        cost_estimate=cost,
    )(x_in, inner, cum_row, step_row, skip_row)


def block_state_kernel(b_ref, f_ref, x_ref, o_ref):
    scaled = (f_ref[0] * x_ref[...].astype(jnp.float32)).astype(jnp.bfloat16)
    o_ref[0] = jnp.dot(b_ref[0], scaled, preferred_element_type=jnp.float32)


def block_states(b_blocks, factor, x_in):
    slots, tokens, state = b_blocks.shape
    width = x_in.shape[1]
    cut = 512 if width % 512 == 0 else width
    b_t = b_blocks.transpose(0, 2, 1)
    spread_factor = spread(factor)
    cost = pl.CostEstimate(
        flops=2 * slots * state * tokens * width,
        transcendentals=0,
        bytes_accessed=x_in.size * 2 + spread_factor.size * 4 + slots * state * width * 4,
    )
    return pl.pallas_call(
        block_state_kernel,
        out_shape=jax.ShapeDtypeStruct((slots, state, width), jnp.float32),
        grid=(slots, width // cut),
        in_specs=[
            pl.BlockSpec((1, state, tokens), lambda c, k: (c, 0, 0)),
            pl.BlockSpec((1, tokens, cut), lambda c, k: (c, 0, k)),
            pl.BlockSpec((tokens, cut), lambda c, k: (c, k)),
        ],
        out_specs=pl.BlockSpec((1, state, cut), lambda c, k: (c, 0, k)),
        cost_estimate=cost,
    )(b_t, spread_factor, x_in)


KEY_CHUNK = 256


def attention_kernel(q_ref, k_ref, v_ref, o_ref):
    seq_count = lax.axis_size("seq")
    me = lax.axis_index("seq")
    slot = pl.program_id(1)
    per_kv = q_ref.shape[1] // HD
    rows = per_kv * BLOCK
    held = k_ref.shape[1]
    first = (slot * seq_count + me) * BLOCK
    chunks = (first + BLOCK + KEY_CHUNK - 1) // KEY_CHUNK
    q = jnp.concatenate([q_ref[:, j * HD : (j + 1) * HD] for j in range(per_kv)], axis=0)
    query_pos = first + lax.broadcasted_iota(jnp.int32, (rows, KEY_CHUNK), 0) % BLOCK
    key_col = lax.broadcasted_iota(jnp.int32, (rows, KEY_CHUNK), 1)
    score_scale = 1.0 / HD**0.5

    def place(c):
        start = c * KEY_CHUNK
        return start, start // held, pl.multiple_of(start % held, KEY_CHUNK)

    def scores(c):
        start, at_slot, at_row = place(c)
        k = k_ref[at_slot, pl.ds(at_row, KEY_CHUNK), :]
        s = lax.dot_general(q, k, (((1,), (1,)), ((), ())), preferred_element_type=jnp.float32)
        return s * score_scale, start + key_col <= query_pos

    def top_of(c, top):
        s, visible = scores(c)
        return jnp.maximum(top, jnp.max(jnp.where(visible, s, NEG), axis=1, keepdims=True))

    top = lax.fori_loop(0, chunks, top_of, jnp.full((rows, 1), NEG, jnp.float32))

    def add_of(c, carry):
        total, acc = carry
        s, visible = scores(c)
        probs = jnp.where(visible, jnp.exp(s - top), 0.0)
        unused, at_slot, at_row = place(c)
        v = v_ref[at_slot, pl.ds(at_row, KEY_CHUNK), :]
        acc = acc + jnp.dot(probs.astype(jnp.bfloat16), v, preferred_element_type=jnp.float32)
        return (total + jnp.sum(probs, axis=1, keepdims=True), acc)

    start_carry = (jnp.zeros((rows, 1), jnp.float32), jnp.zeros((rows, HD), jnp.float32))
    total, acc = lax.fori_loop(0, chunks, add_of, start_carry)
    out = (acc / total).astype(o_ref.dtype)
    for j in range(per_kv):
        o_ref[:, j * HD : (j + 1) * HD] = out[j * BLOCK : (j + 1) * BLOCK]


def attention_core(queries, kv_piece):
    tok_rows, width = queries.shape
    slots, held, unused = kv_piece.shape
    kv_local = kv_piece.shape[2] // (2 * HD)
    group_width = width // kv_local
    keys = slots * held
    cost = pl.CostEstimate(
        flops=4 * tok_rows * width * keys,
        transcendentals=tok_rows * width * keys // HD,
        bytes_accessed=2 * (2 * queries.size + kv_piece.size),
    )
    return pl.pallas_call(
        attention_kernel,
        out_shape=jax.ShapeDtypeStruct(queries.shape, jnp.bfloat16),
        grid=(kv_local, slots),
        in_specs=[
            pl.BlockSpec((BLOCK, group_width), lambda g, s: (s, g)),
            pl.BlockSpec((slots, held, HD), lambda g, s: (0, 0, g)),
            pl.BlockSpec((slots, held, HD), lambda g, s: (0, 0, kv_local + g)),
        ],
        out_specs=pl.BlockSpec((BLOCK, group_width), lambda g, s: (s, g)),
        cost_estimate=cost,
    )(queries, kv_piece, kv_piece)


def local(x_in, step_size, a_log, d_skip, b_in, c_in, queries, key_rows, values):
    my_index = lax.axis_index("seq")
    seq_count = lax.axis_size("seq")
    tok_rows, width = x_in.shape
    slots = tok_rows // BLOCK
    heads = step_size.shape[0]
    kv_cat = jnp.concatenate(
        [key_rows.reshape(slots, BLOCK, -1), values.reshape(slots, BLOCK, -1)], axis=2
    )
    kv_cat, x_in, step_size = lax.optimization_barrier((kv_cat, x_in, step_size))
    kv_piece = lax.all_gather(kv_cat, "seq", axis=1, tiled=True)
    rate = -jnp.exp(a_log)
    steps = step_size.reshape(heads, slots, BLOCK).transpose(1, 0, 2)
    cum = jnp.cumsum(steps * rate[None, :, None], axis=2)
    log_total = cum[:, :, -1]
    factor = (jnp.exp(log_total[:, :, None] - cum) * steps).transpose(0, 2, 1)
    b_blocks = b_in.reshape(slots, BLOCK, STATE)
    c_blocks = c_in.reshape(slots, BLOCK, STATE)
    block_state = block_states(b_blocks, factor, x_in)
    decay = jnp.exp(log_total)
    parts = 2 if heads % 2 == 0 else 1
    hooks = {
        (1, 0): (mamba_base, (x_in, steps, cum, b_blocks, c_blocks, d_skip)),
        (1, 1): (attention_core, (queries, kv_piece)),
    }
    incoming, results = entering_states(decay, block_state, seq_count, my_index, hooks, parts)
    c_wide = c_blocks.astype(jnp.float32)
    carried = jnp.concatenate(
        [
            jnp.einsum("ctn,cnk->ctk", c_wide, part, precision=lax.Precision.HIGHEST)
            for part in incoming
        ],
        axis=2,
    )
    carried = carried * spread(jnp.exp(cum).transpose(0, 2, 1))
    mamba_out = (results["mamba_base"] + carried).astype(jnp.bfloat16).reshape(tok_rows, width)
    return (mamba_out, results["attention_core"])


def solution(mesh):
    in_specs = (
        P(("group", "seq"), "head"),
        P("head", ("group", "seq")),
        P("head"),
        P("head"),
        P(("group", "seq"), None),
        P(("group", "seq"), None),
        P(("group", "seq"), "head"),
        P(("group", "seq"), "head"),
        P(("group", "seq"), "head"),
    )
    out_specs = (P(("group", "seq"), "head"), P(("group", "seq"), "head"))
    return jax.shard_map(local, mesh=mesh, in_specs=in_specs, out_specs=out_specs, check_vma=False)
```

```python
import jax
import jax.numpy as jnp
from jax import lax
from jax.experimental import pallas as pl
from jax.experimental.pallas import tpu as pltpu
from jax.sharding import PartitionSpec as P

BLOCK = 128
HEADDIM = 64
STATE = 128
QHEADS = 16
KVHEADS = 4
HD = 128


NEG = -1e30


def spread(a):
    return jnp.repeat(a, HEADDIM, axis=-1)


def decay_scan(decay, count, mine):
    excl = jnp.ones_like(decay)
    total = decay
    steps = []
    span = 1
    while span < count:
        lower = (mine // span) % 2 == 1
        got = lax.ppermute(total, "seq", [(i, i ^ span) for i in range(count)])
        steps.append((lower, excl, total, got))
        excl = jnp.where(lower, got * excl, excl)
        total = total * got
        span *= 2
    return steps, excl, total


def entering_states(decay, block_state, count, mine, hooks, parts):
    steps, excl_decay, total_decay = decay_scan(decay, count, mine)
    heads, width = decay.shape[1], block_state.shape[2]
    head_cut, width_cut = heads // parts, width // parts
    totals = [block_state[:, :, j * width_cut : (j + 1) * width_cut] for j in range(parts)]
    excls = [jnp.zeros_like(t) for t in totals]
    results = {}
    span = 1
    for step, known_all in enumerate(steps):
        pairs = [(i, i ^ span) for i in range(count)]
        gots = []
        for j in range(parts):
            hook = hooks.get((j, step if step + 1 < len(steps) else -1))
            tie = gots[-1] if gots and step + 1 < len(steps) else ()
            totals[j], known, args, tie = lax.optimization_barrier(
                (totals[j], known_all, hook[1] if hook else (), tie)
            )
            if gots and step + 1 < len(steps):
                gots[-1] = tie
            got = lax.ppermute(totals[j].astype(jnp.bfloat16), "seq", pairs).astype(jnp.float32)
            if hook is not None:
                done = hook[0](*args)
                got, done = lax.optimization_barrier((got, done))
                results[hook[0].__name__] = done
            gots.append(got)
        lower = known_all[0]
        for j in range(parts):
            unused, excl_a, own_a, got_a = [
                v if v.ndim == 0 else v[:, j * head_cut : (j + 1) * head_cut] for v in known_all
            ]
            got = gots[j]
            excls[j] = jnp.where(lower, spread(excl_a)[:, None, :] * got + excls[j], excls[j])
            totals[j] = jnp.where(
                lower,
                spread(own_a)[:, None, :] * got + totals[j],
                spread(got_a)[:, None, :] * totals[j] + got,
            )
        span *= 2
    entering = []
    for j in range(parts):
        carry = jnp.zeros_like(totals[j][0])
        rows = []
        for slot in range(decay.shape[0]):
            a_excl = excl_decay[slot, j * head_cut : (j + 1) * head_cut]
            a_total = total_decay[slot, j * head_cut : (j + 1) * head_cut]
            rows.append(spread(a_excl)[None, :] * carry + excls[j][slot])
            carry = spread(a_total)[None, :] * carry + totals[j][slot]
        entering.append(jnp.stack(rows, axis=0))
    return (entering, results)


def mamba_base_kernel(x_ref, inner_ref, cum_ref, step_ref, skip_ref, o_ref):
    rows = lax.broadcasted_iota(jnp.int32, (BLOCK, BLOCK), 0)
    cols = lax.broadcasted_iota(jnp.int32, (BLOCK, BLOCK), 1)
    causal = rows >= cols
    inner = inner_ref[0]
    for e in range(cum_ref.shape[1]):
        cum_row = cum_ref[0, e]
        cum_col = jnp.sum(jnp.where(rows == cols, cum_row, 0.0), axis=1, keepdims=True)
        log_gap = jnp.where(causal, cum_col - cum_row, -jnp.inf)
        mixing = (inner * jnp.exp(log_gap) * step_ref[0, e]).astype(jnp.bfloat16)
        x_head = x_ref[:, e * HEADDIM : (e + 1) * HEADDIM]
        intra = jnp.dot(mixing, x_head, preferred_element_type=jnp.float32)
        skip = skip_ref[:, e * HEADDIM : (e + 1) * HEADDIM] * x_head.astype(jnp.float32)
        o_ref[0, :, e * HEADDIM : (e + 1) * HEADDIM] = intra + skip


def mamba_base(x_in, steps, cum, b_blocks, c_blocks, d_skip):
    slots, heads = steps.shape[:2]
    width = x_in.shape[1]
    group = 8 if heads % 8 == 0 else 128 // HEADDIM
    inner = jnp.einsum("cin,cjn->cij", c_blocks, b_blocks, preferred_element_type=jnp.float32)
    cum_row = cum[:, :, None, :]
    step_row = steps[:, :, None, :]
    skip_row = spread(d_skip)[None, :]
    cost = pl.CostEstimate(
        flops=2 * slots * heads * BLOCK * BLOCK * (HEADDIM + 3),
        transcendentals=slots * heads * BLOCK * BLOCK,
        bytes_accessed=x_in.size * 2 + slots * BLOCK * width * 4,
    )
    carried_scale = spread(jnp.exp(cum).transpose(0, 2, 1))
    return carried_scale, pl.pallas_call(
        mamba_base_kernel,
        out_shape=jax.ShapeDtypeStruct((slots, BLOCK, width), jnp.float32),
        grid=(slots, heads // group),
        in_specs=[
            pl.BlockSpec((BLOCK, group * HEADDIM), lambda c, g: (c, g)),
            pl.BlockSpec((1, BLOCK, BLOCK), lambda c, g: (c, 0, 0)),
            pl.BlockSpec((1, group, 1, BLOCK), lambda c, g: (c, g, 0, 0)),
            pl.BlockSpec((1, group, 1, BLOCK), lambda c, g: (c, g, 0, 0)),
            pl.BlockSpec((1, group * HEADDIM), lambda c, g: (0, g)),
        ],
        out_specs=pl.BlockSpec((1, BLOCK, group * HEADDIM), lambda c, g: (c, 0, g)),
        cost_estimate=cost,
    )(x_in, inner, cum_row, step_row, skip_row)


def block_state_kernel(b_ref, f_ref, x_ref, o_ref):
    scaled = (f_ref[0] * x_ref[...].astype(jnp.float32)).astype(jnp.bfloat16)
    o_ref[0] = jnp.dot(b_ref[0], scaled, preferred_element_type=jnp.float32)


def block_states(b_blocks, factor, x_in):
    slots, tokens, state = b_blocks.shape
    width = x_in.shape[1]
    cut = 512 if width % 512 == 0 else width
    b_t = b_blocks.transpose(0, 2, 1)
    spread_factor = spread(factor)
    cost = pl.CostEstimate(
        flops=2 * slots * state * tokens * width,
        transcendentals=0,
        bytes_accessed=x_in.size * 2 + spread_factor.size * 4 + slots * state * width * 4,
    )
    return pl.pallas_call(
        block_state_kernel,
        out_shape=jax.ShapeDtypeStruct((slots, state, width), jnp.float32),
        grid=(slots, width // cut),
        in_specs=[
            pl.BlockSpec((1, state, tokens), lambda c, k: (c, 0, 0)),
            pl.BlockSpec((1, tokens, cut), lambda c, k: (c, 0, k)),
            pl.BlockSpec((tokens, cut), lambda c, k: (c, k)),
        ],
        out_specs=pl.BlockSpec((1, state, cut), lambda c, k: (c, 0, k)),
        cost_estimate=cost,
    )(b_t, spread_factor, x_in)


KEY_CHUNK = 256


def attention_kernel(q_ref, k_ref, v_ref, o_ref):
    seq_count = lax.axis_size("seq")
    me = lax.axis_index("seq")
    slot = pl.program_id(1)
    per_kv = q_ref.shape[1] // HD
    rows = per_kv * BLOCK
    held = k_ref.shape[1]
    first = (slot * seq_count + me) * BLOCK
    chunks = (first + BLOCK + KEY_CHUNK - 1) // KEY_CHUNK
    q = jnp.concatenate([q_ref[:, j * HD : (j + 1) * HD] for j in range(per_kv)], axis=0)
    query_pos = first + lax.broadcasted_iota(jnp.int32, (rows, KEY_CHUNK), 0) % BLOCK
    key_col = lax.broadcasted_iota(jnp.int32, (rows, KEY_CHUNK), 1)
    score_scale = 1.0 / HD**0.5

    def place(c):
        start = c * KEY_CHUNK
        return start, start // held, pl.multiple_of(start % held, KEY_CHUNK)

    def scores(c):
        start, at_slot, at_row = place(c)
        k = k_ref[at_slot, pl.ds(at_row, KEY_CHUNK), :]
        s = lax.dot_general(q, k, (((1,), (1,)), ((), ())), preferred_element_type=jnp.float32)
        return s * score_scale, start + key_col <= query_pos

    def top_of(c, top):
        s, visible = scores(c)
        return jnp.maximum(top, jnp.max(jnp.where(visible, s, NEG), axis=1, keepdims=True))

    top = lax.fori_loop(0, chunks, top_of, jnp.full((rows, 1), NEG, jnp.float32))

    def add_of(c, carry):
        total, acc = carry
        s, visible = scores(c)
        probs = jnp.where(visible, jnp.exp(s - top), 0.0)
        unused, at_slot, at_row = place(c)
        v = v_ref[at_slot, pl.ds(at_row, KEY_CHUNK), :]
        acc = acc + jnp.dot(probs.astype(jnp.bfloat16), v, preferred_element_type=jnp.float32)
        return (total + jnp.sum(probs, axis=1, keepdims=True), acc)

    start_carry = (jnp.zeros((rows, 1), jnp.float32), jnp.zeros((rows, HD), jnp.float32))
    total, acc = lax.fori_loop(0, chunks, add_of, start_carry)
    out = (acc / total).astype(o_ref.dtype)
    for j in range(per_kv):
        o_ref[:, j * HD : (j + 1) * HD] = out[j * BLOCK : (j + 1) * BLOCK]


def attention_core(queries, kv_piece):
    tok_rows, width = queries.shape
    slots, held, unused = kv_piece.shape
    kv_local = kv_piece.shape[2] // (2 * HD)
    group_width = width // kv_local
    keys = slots * held
    cost = pl.CostEstimate(
        flops=4 * tok_rows * width * keys,
        transcendentals=tok_rows * width * keys // HD,
        bytes_accessed=2 * (2 * queries.size + kv_piece.size),
    )
    return pl.pallas_call(
        attention_kernel,
        out_shape=jax.ShapeDtypeStruct(queries.shape, jnp.bfloat16),
        grid=(kv_local, slots),
        in_specs=[
            pl.BlockSpec((BLOCK, group_width), lambda g, s: (s, g)),
            pl.BlockSpec((slots, held, HD), lambda g, s: (0, 0, g)),
            pl.BlockSpec((slots, held, HD), lambda g, s: (0, 0, kv_local + g)),
        ],
        out_specs=pl.BlockSpec((BLOCK, group_width), lambda g, s: (s, g)),
        cost_estimate=cost,
    )(queries, kv_piece, kv_piece)


def local(x_in, step_size, a_log, d_skip, b_in, c_in, queries, key_rows, values):
    my_index = lax.axis_index("seq")
    seq_count = lax.axis_size("seq")
    tok_rows, width = x_in.shape
    slots = tok_rows // BLOCK
    heads = step_size.shape[0]
    kv_cat = jnp.concatenate(
        [key_rows.reshape(slots, BLOCK, -1), values.reshape(slots, BLOCK, -1)], axis=2
    )
    kv_cat, x_in, step_size = lax.optimization_barrier((kv_cat, x_in, step_size))
    kv_piece = lax.all_gather(kv_cat, "seq", axis=1, tiled=True)
    rate = -jnp.exp(a_log)
    steps = step_size.reshape(heads, slots, BLOCK).transpose(1, 0, 2)
    cum = jnp.cumsum(steps * rate[None, :, None], axis=2)
    log_total = cum[:, :, -1]
    factor = (jnp.exp(log_total[:, :, None] - cum) * steps).transpose(0, 2, 1)
    b_blocks = b_in.reshape(slots, BLOCK, STATE)
    c_blocks = c_in.reshape(slots, BLOCK, STATE)
    block_state = block_states(b_blocks, factor, x_in)
    decay = jnp.exp(log_total)
    parts = 2 if heads % 2 == 0 else 1
    hooks = {
        (1, 0): (mamba_base, (x_in, steps, cum, b_blocks, c_blocks, d_skip)),
        (1, 1): (attention_core, (queries, kv_piece)),
    }
    incoming, results = entering_states(decay, block_state, seq_count, my_index, hooks, parts)
    c_wide = c_blocks.astype(jnp.float32)
    carried = jnp.concatenate(
        [
            jnp.einsum("ctn,cnk->ctk", c_wide, part, precision=lax.Precision.HIGHEST)
            for part in incoming
        ],
        axis=2,
    )
    carried_scale, base = results["mamba_base"]
    carried = carried * carried_scale
    mamba_out = (base + carried).astype(jnp.bfloat16).reshape(tok_rows, width)
    return (mamba_out, results["attention_core"])


def solution(mesh):
    in_specs = (
        P(("group", "seq"), "head"),
        P("head", ("group", "seq")),
        P("head"),
        P("head"),
        P(("group", "seq"), None),
        P(("group", "seq"), None),
        P(("group", "seq"), "head"),
        P(("group", "seq"), "head"),
        P(("group", "seq"), "head"),
    )
    out_specs = (P(("group", "seq"), "head"), P(("group", "seq"), "head"))
    return jax.shard_map(local, mesh=mesh, in_specs=in_specs, out_specs=out_specs, check_vma=False)
```

```python
import jax
import jax.numpy as jnp
from jax import lax
from jax.experimental import pallas as pl
from jax.experimental.pallas import tpu as pltpu
from jax.sharding import PartitionSpec as P

BLOCK = 128
HEADDIM = 64
STATE = 128
QHEADS = 16
KVHEADS = 4
HD = 128


NEG = -1e30


def spread(a):
    return jnp.repeat(a, HEADDIM, axis=-1)


def decay_scan(decay, count, mine):
    excl = jnp.ones_like(decay)
    total = decay
    steps = []
    span = 1
    while span < count:
        lower = (mine // span) % 2 == 1
        got = lax.ppermute(total, "seq", [(i, i ^ span) for i in range(count)])
        steps.append((lower, excl, total, got))
        excl = jnp.where(lower, got * excl, excl)
        total = total * got
        span *= 2
    return steps, excl, total


def entering_states(decay, block_state, count, mine, hooks, parts):
    steps, excl_decay, total_decay = decay_scan(decay, count, mine)
    heads = decay.shape[1]
    head_cut = heads // parts
    totals = [block_state[j] for j in range(parts)]
    excls = [jnp.zeros_like(t) for t in totals]
    results = {}
    span = 1
    for step, known_all in enumerate(steps):
        pairs = [(i, i ^ span) for i in range(count)]
        gots = []
        for j in range(parts):
            hook = hooks.get((j, step if step + 1 < len(steps) else -1))
            tie = gots[-1] if gots and step + 1 < len(steps) else ()
            totals[j], known, args, tie = lax.optimization_barrier(
                (totals[j], known_all, hook[1] if hook else (), tie)
            )
            if gots and step + 1 < len(steps):
                gots[-1] = tie
            got = lax.ppermute(totals[j].astype(jnp.bfloat16), "seq", pairs).astype(jnp.float32)
            if hook is not None:
                done = hook[0](*args)
                got, done = lax.optimization_barrier((got, done))
                results[hook[0].__name__] = done
            gots.append(got)
        lower = known_all[0]
        for j in range(parts):
            unused, excl_a, own_a, got_a = [
                v if v.ndim == 0 else v[:, j * head_cut : (j + 1) * head_cut] for v in known_all
            ]
            got = gots[j]
            excls[j] = jnp.where(lower, spread(excl_a)[:, None, :] * got + excls[j], excls[j])
            totals[j] = jnp.where(
                lower,
                spread(own_a)[:, None, :] * got + totals[j],
                spread(got_a)[:, None, :] * totals[j] + got,
            )
        span *= 2
    entering = []
    for j in range(parts):
        carry = jnp.zeros_like(totals[j][0])
        rows = []
        for slot in range(decay.shape[0]):
            a_excl = excl_decay[slot, j * head_cut : (j + 1) * head_cut]
            a_total = total_decay[slot, j * head_cut : (j + 1) * head_cut]
            rows.append(spread(a_excl)[None, :] * carry + excls[j][slot])
            carry = spread(a_total)[None, :] * carry + totals[j][slot]
        entering.append(jnp.stack(rows, axis=0))
    return (entering, results)


def mamba_base_kernel(x_ref, inner_ref, cum_ref, step_ref, skip_ref, o_ref):
    rows = lax.broadcasted_iota(jnp.int32, (BLOCK, BLOCK), 0)
    cols = lax.broadcasted_iota(jnp.int32, (BLOCK, BLOCK), 1)
    causal = rows >= cols
    inner = inner_ref[0]
    for e in range(cum_ref.shape[1]):
        cum_row = cum_ref[0, e]
        cum_col = jnp.sum(jnp.where(rows == cols, cum_row, 0.0), axis=1, keepdims=True)
        log_gap = jnp.where(causal, cum_col - cum_row, -jnp.inf)
        mixing = (inner * jnp.exp(log_gap) * step_ref[0, e]).astype(jnp.bfloat16)
        x_head = x_ref[:, e * HEADDIM : (e + 1) * HEADDIM]
        intra = jnp.dot(mixing, x_head, preferred_element_type=jnp.float32)
        skip = skip_ref[:, e * HEADDIM : (e + 1) * HEADDIM] * x_head.astype(jnp.float32)
        o_ref[0, :, e * HEADDIM : (e + 1) * HEADDIM] = intra + skip


def mamba_base(x_in, steps, cum, b_blocks, c_blocks, d_skip):
    slots, heads = steps.shape[:2]
    width = x_in.shape[1]
    group = 8 if heads % 8 == 0 else 128 // HEADDIM
    inner = jnp.einsum("cin,cjn->cij", c_blocks, b_blocks, preferred_element_type=jnp.float32)
    cum_row = cum[:, :, None, :]
    step_row = steps[:, :, None, :]
    skip_row = spread(d_skip)[None, :]
    cost = pl.CostEstimate(
        flops=2 * slots * heads * BLOCK * BLOCK * (HEADDIM + 3),
        transcendentals=slots * heads * BLOCK * BLOCK,
        bytes_accessed=x_in.size * 2 + slots * BLOCK * width * 4,
    )
    carried_scale = spread(jnp.exp(cum).transpose(0, 2, 1))
    return carried_scale, pl.pallas_call(
        mamba_base_kernel,
        out_shape=jax.ShapeDtypeStruct((slots, BLOCK, width), jnp.float32),
        grid=(slots, heads // group),
        in_specs=[
            pl.BlockSpec((BLOCK, group * HEADDIM), lambda c, g: (c, g)),
            pl.BlockSpec((1, BLOCK, BLOCK), lambda c, g: (c, 0, 0)),
            pl.BlockSpec((1, group, 1, BLOCK), lambda c, g: (c, g, 0, 0)),
            pl.BlockSpec((1, group, 1, BLOCK), lambda c, g: (c, g, 0, 0)),
            pl.BlockSpec((1, group * HEADDIM), lambda c, g: (0, g)),
        ],
        out_specs=pl.BlockSpec((1, BLOCK, group * HEADDIM), lambda c, g: (c, 0, g)),
        cost_estimate=cost,
    )(x_in, inner, cum_row, step_row, skip_row)


def block_state_kernel(b_ref, f_ref, x_ref, o_ref):
    scaled = (f_ref[0] * x_ref[...].astype(jnp.float32)).astype(jnp.bfloat16)
    o_ref[0, 0] = jnp.dot(b_ref[0], scaled, preferred_element_type=jnp.float32)


def block_states(b_blocks, factor, x_in, parts):
    slots, tokens, state = b_blocks.shape
    width = x_in.shape[1]
    cut = width // parts
    b_t = b_blocks.transpose(0, 2, 1)
    spread_factor = spread(factor)
    cost = pl.CostEstimate(
        flops=2 * slots * state * tokens * width,
        transcendentals=0,
        bytes_accessed=x_in.size * 2 + spread_factor.size * 4 + slots * state * width * 4,
    )
    return pl.pallas_call(
        block_state_kernel,
        out_shape=jax.ShapeDtypeStruct((parts, slots, state, cut), jnp.float32),
        grid=(slots, parts),
        in_specs=[
            pl.BlockSpec((1, state, tokens), lambda c, k: (c, 0, 0)),
            pl.BlockSpec((1, tokens, cut), lambda c, k: (c, 0, k)),
            pl.BlockSpec((tokens, cut), lambda c, k: (c, k)),
        ],
        out_specs=pl.BlockSpec((1, 1, state, cut), lambda c, k: (k, c, 0, 0)),
        cost_estimate=cost,
    )(b_t, spread_factor, x_in)


KEY_CHUNK = 256


def attention_kernel(q_ref, k_ref, v_ref, o_ref):
    seq_count = lax.axis_size("seq")
    me = lax.axis_index("seq")
    slot = pl.program_id(1)
    per_kv = q_ref.shape[1] // HD
    rows = per_kv * BLOCK
    held = k_ref.shape[1]
    first = (slot * seq_count + me) * BLOCK
    chunks = (first + BLOCK + KEY_CHUNK - 1) // KEY_CHUNK
    q = jnp.concatenate([q_ref[:, j * HD : (j + 1) * HD] for j in range(per_kv)], axis=0)
    query_pos = first + lax.broadcasted_iota(jnp.int32, (rows, KEY_CHUNK), 0) % BLOCK
    key_col = lax.broadcasted_iota(jnp.int32, (rows, KEY_CHUNK), 1)
    score_scale = 1.0 / HD**0.5

    def place(c):
        start = c * KEY_CHUNK
        return start, start // held, pl.multiple_of(start % held, KEY_CHUNK)

    def scores(c):
        start, at_slot, at_row = place(c)
        k = k_ref[at_slot, pl.ds(at_row, KEY_CHUNK), :]
        s = lax.dot_general(q, k, (((1,), (1,)), ((), ())), preferred_element_type=jnp.float32)
        return s * score_scale, start + key_col <= query_pos

    def top_of(c, top):
        s, visible = scores(c)
        return jnp.maximum(top, jnp.max(jnp.where(visible, s, NEG), axis=1, keepdims=True))

    top = lax.fori_loop(0, chunks, top_of, jnp.full((rows, 1), NEG, jnp.float32))

    def add_of(c, carry):
        total, acc = carry
        s, visible = scores(c)
        probs = jnp.where(visible, jnp.exp(s - top), 0.0)
        unused, at_slot, at_row = place(c)
        v = v_ref[at_slot, pl.ds(at_row, KEY_CHUNK), :]
        acc = acc + jnp.dot(probs.astype(jnp.bfloat16), v, preferred_element_type=jnp.float32)
        return (total + jnp.sum(probs, axis=1, keepdims=True), acc)

    start_carry = (jnp.zeros((rows, 1), jnp.float32), jnp.zeros((rows, HD), jnp.float32))
    total, acc = lax.fori_loop(0, chunks, add_of, start_carry)
    out = (acc / total).astype(o_ref.dtype)
    for j in range(per_kv):
        o_ref[:, j * HD : (j + 1) * HD] = out[j * BLOCK : (j + 1) * BLOCK]


def attention_core(queries, kv_piece):
    tok_rows, width = queries.shape
    slots, held, unused = kv_piece.shape
    kv_local = kv_piece.shape[2] // (2 * HD)
    group_width = width // kv_local
    keys = slots * held
    cost = pl.CostEstimate(
        flops=4 * tok_rows * width * keys,
        transcendentals=tok_rows * width * keys // HD,
        bytes_accessed=2 * (2 * queries.size + kv_piece.size),
    )
    return pl.pallas_call(
        attention_kernel,
        out_shape=jax.ShapeDtypeStruct(queries.shape, jnp.bfloat16),
        grid=(kv_local, slots),
        in_specs=[
            pl.BlockSpec((BLOCK, group_width), lambda g, s: (s, g)),
            pl.BlockSpec((slots, held, HD), lambda g, s: (0, 0, g)),
            pl.BlockSpec((slots, held, HD), lambda g, s: (0, 0, kv_local + g)),
        ],
        out_specs=pl.BlockSpec((BLOCK, group_width), lambda g, s: (s, g)),
        cost_estimate=cost,
    )(queries, kv_piece, kv_piece)


def local(x_in, step_size, a_log, d_skip, b_in, c_in, queries, key_rows, values):
    my_index = lax.axis_index("seq")
    seq_count = lax.axis_size("seq")
    tok_rows, width = x_in.shape
    slots = tok_rows // BLOCK
    heads = step_size.shape[0]
    kv_cat = jnp.concatenate(
        [key_rows.reshape(slots, BLOCK, -1), values.reshape(slots, BLOCK, -1)], axis=2
    )
    kv_cat, x_in, step_size = lax.optimization_barrier((kv_cat, x_in, step_size))
    kv_piece = lax.all_gather(kv_cat, "seq", axis=1, tiled=True)
    rate = -jnp.exp(a_log)
    steps = step_size.reshape(heads, slots, BLOCK).transpose(1, 0, 2)
    cum = jnp.cumsum(steps * rate[None, :, None], axis=2)
    log_total = cum[:, :, -1]
    factor = (jnp.exp(log_total[:, :, None] - cum) * steps).transpose(0, 2, 1)
    b_blocks = b_in.reshape(slots, BLOCK, STATE)
    c_blocks = c_in.reshape(slots, BLOCK, STATE)
    parts = 2 if heads % 2 == 0 else 1
    block_state = block_states(b_blocks, factor, x_in, parts)
    decay = jnp.exp(log_total)
    hooks = {
        (1, 0): (mamba_base, (x_in, steps, cum, b_blocks, c_blocks, d_skip)),
        (1, 1): (attention_core, (queries, kv_piece)),
    }
    incoming, results = entering_states(decay, block_state, seq_count, my_index, hooks, parts)
    c_wide = c_blocks.astype(jnp.float32)
    carried = jnp.concatenate(
        [
            jnp.einsum("ctn,cnk->ctk", c_wide, part, precision=lax.Precision.HIGHEST)
            for part in incoming
        ],
        axis=2,
    )
    carried_scale, base = results["mamba_base"]
    carried = carried * carried_scale
    mamba_out = (base + carried).astype(jnp.bfloat16).reshape(tok_rows, width)
    return (mamba_out, results["attention_core"])


def solution(mesh):
    in_specs = (
        P(("group", "seq"), "head"),
        P("head", ("group", "seq")),
        P("head"),
        P("head"),
        P(("group", "seq"), None),
        P(("group", "seq"), None),
        P(("group", "seq"), "head"),
        P(("group", "seq"), "head"),
        P(("group", "seq"), "head"),
    )
    out_specs = (P(("group", "seq"), "head"), P(("group", "seq"), "head"))
    return jax.shard_map(local, mesh=mesh, in_specs=in_specs, out_specs=out_specs, check_vma=False)
```

```python
import jax
import jax.numpy as jnp
from jax import lax
from jax.experimental import pallas as pl
from jax.experimental.pallas import tpu as pltpu
from jax.sharding import PartitionSpec as P

BLOCK = 128
HEADDIM = 64
STATE = 128
QHEADS = 16
KVHEADS = 4
HD = 128


NEG = -1e30


def spread(a):
    return jnp.repeat(a, HEADDIM, axis=-1)


def decay_scan(decay, count, mine):
    excl = jnp.ones_like(decay)
    total = decay
    steps = []
    span = 1
    while span < count:
        lower = (mine // span) % 2 == 1
        got = lax.ppermute(total, "seq", [(i, i ^ span) for i in range(count)])
        steps.append((lower, excl, total, got))
        excl = jnp.where(lower, got * excl, excl)
        total = total * got
        span *= 2
    return steps, excl, total


def entering_states(decay, block_state, count, mine, hooks, parts):
    steps, excl_decay, total_decay = decay_scan(decay, count, mine)
    heads, width = decay.shape[1], block_state.shape[2]
    head_cut, width_cut = heads // parts, width // parts
    totals = [block_state[:, :, j * width_cut : (j + 1) * width_cut] for j in range(parts)]
    excls = [jnp.zeros_like(t) for t in totals]
    results = {}
    span = 1
    for step, known_all in enumerate(steps):
        pairs = [(i, i ^ span) for i in range(count)]
        gots = []
        for j in range(parts):
            hook = hooks.get((j, step if step + 1 < len(steps) else -1))
            tie = gots[-1] if gots and step + 1 < len(steps) else ()
            totals[j], known, args, tie = lax.optimization_barrier(
                (totals[j], known_all, hook[1] if hook else (), tie)
            )
            if gots and step + 1 < len(steps):
                gots[-1] = tie
            got = lax.ppermute(totals[j].astype(jnp.bfloat16), "seq", pairs).astype(jnp.float32)
            if hook is not None:
                done = hook[0](*args)
                got, done = lax.optimization_barrier((got, done))
                results[hook[0].__name__] = done
            gots.append(got)
        lower = known_all[0]
        for j in range(parts):
            unused, excl_a, own_a, got_a = [
                v if v.ndim == 0 else v[:, j * head_cut : (j + 1) * head_cut] for v in known_all
            ]
            got = gots[j]
            excls[j] = jnp.where(lower, spread(excl_a)[:, None, :] * got + excls[j], excls[j])
            totals[j] = jnp.where(
                lower,
                spread(own_a)[:, None, :] * got + totals[j],
                spread(got_a)[:, None, :] * totals[j] + got,
            )
        span *= 2
    entering = []
    for j in range(parts):
        carry = jnp.zeros_like(totals[j][0])
        rows = []
        for slot in range(decay.shape[0]):
            a_excl = excl_decay[slot, j * head_cut : (j + 1) * head_cut]
            a_total = total_decay[slot, j * head_cut : (j + 1) * head_cut]
            rows.append(spread(a_excl)[None, :] * carry + excls[j][slot])
            carry = spread(a_total)[None, :] * carry + totals[j][slot]
        entering.append(jnp.stack(rows, axis=0))
    return (entering, results)


def mamba_base_kernel(x_ref, inner_ref, cum_ref, step_ref, skip_ref, o_ref):
    rows = lax.broadcasted_iota(jnp.int32, (BLOCK, BLOCK), 0)
    cols = lax.broadcasted_iota(jnp.int32, (BLOCK, BLOCK), 1)
    causal = rows >= cols
    inner = inner_ref[0]
    for e in range(cum_ref.shape[1]):
        cum_row = cum_ref[0, e]
        cum_col = jnp.sum(jnp.where(rows == cols, cum_row, 0.0), axis=1, keepdims=True)
        log_gap = jnp.where(causal, cum_col - cum_row, -jnp.inf)
        mixing = (inner * jnp.exp(log_gap) * step_ref[0, e]).astype(jnp.bfloat16)
        x_head = x_ref[:, e * HEADDIM : (e + 1) * HEADDIM]
        intra = jnp.dot(mixing, x_head, preferred_element_type=jnp.float32)
        skip = skip_ref[:, e * HEADDIM : (e + 1) * HEADDIM] * x_head.astype(jnp.float32)
        o_ref[0, :, e * HEADDIM : (e + 1) * HEADDIM] = intra + skip


def mamba_base(x_in, steps, cum, b_blocks, c_blocks, d_skip):
    slots, heads = steps.shape[:2]
    width = x_in.shape[1]
    group = 8 if heads % 8 == 0 else 128 // HEADDIM
    inner = jnp.einsum("cin,cjn->cij", c_blocks, b_blocks, preferred_element_type=jnp.float32)
    cum_row = cum[:, :, None, :]
    step_row = steps[:, :, None, :]
    skip_row = spread(d_skip)[None, :]
    cost = pl.CostEstimate(
        flops=2 * slots * heads * BLOCK * BLOCK * (HEADDIM + 3),
        transcendentals=slots * heads * BLOCK * BLOCK,
        bytes_accessed=x_in.size * 2 + slots * BLOCK * width * 4,
    )
    carried_scale = spread(jnp.exp(cum).transpose(0, 2, 1))
    return carried_scale, pl.pallas_call(
        mamba_base_kernel,
        out_shape=jax.ShapeDtypeStruct((slots, BLOCK, width), jnp.float32),
        grid=(slots, heads // group),
        in_specs=[
            pl.BlockSpec((BLOCK, group * HEADDIM), lambda c, g: (c, g)),
            pl.BlockSpec((1, BLOCK, BLOCK), lambda c, g: (c, 0, 0)),
            pl.BlockSpec((1, group, 1, BLOCK), lambda c, g: (c, g, 0, 0)),
            pl.BlockSpec((1, group, 1, BLOCK), lambda c, g: (c, g, 0, 0)),
            pl.BlockSpec((1, group * HEADDIM), lambda c, g: (0, g)),
        ],
        out_specs=pl.BlockSpec((1, BLOCK, group * HEADDIM), lambda c, g: (c, 0, g)),
        cost_estimate=cost,
    )(x_in, inner, cum_row, step_row, skip_row)


def block_state_kernel(b_ref, f_ref, x_ref, o_ref):
    scaled = (f_ref[0] * x_ref[...].astype(jnp.float32)).astype(jnp.bfloat16)
    o_ref[0] = jnp.dot(b_ref[0], scaled, preferred_element_type=jnp.float32)


def block_states(b_blocks, factor, x_in):
    slots, tokens, state = b_blocks.shape
    width = x_in.shape[1]
    cut = 512 if width % 512 == 0 else width
    b_t = b_blocks.transpose(0, 2, 1)
    spread_factor = spread(factor)
    cost = pl.CostEstimate(
        flops=2 * slots * state * tokens * width,
        transcendentals=0,
        bytes_accessed=x_in.size * 2 + spread_factor.size * 4 + slots * state * width * 4,
    )
    return pl.pallas_call(
        block_state_kernel,
        out_shape=jax.ShapeDtypeStruct((slots, state, width), jnp.float32),
        grid=(slots, width // cut),
        in_specs=[
            pl.BlockSpec((1, state, tokens), lambda c, k: (c, 0, 0)),
            pl.BlockSpec((1, tokens, cut), lambda c, k: (c, 0, k)),
            pl.BlockSpec((tokens, cut), lambda c, k: (c, k)),
        ],
        out_specs=pl.BlockSpec((1, state, cut), lambda c, k: (c, 0, k)),
        cost_estimate=cost,
    )(b_t, spread_factor, x_in)


KEY_CHUNK = 256


def attention_kernel(q_ref, k_ref, v_ref, o_ref):
    seq_count = lax.axis_size("seq")
    me = lax.axis_index("seq")
    slot = pl.program_id(1)
    per_kv = q_ref.shape[1] // HD
    rows = per_kv * BLOCK
    held = k_ref.shape[1]
    first = (slot * seq_count + me) * BLOCK
    chunks = (first + BLOCK + KEY_CHUNK - 1) // KEY_CHUNK
    q = jnp.concatenate([q_ref[:, j * HD : (j + 1) * HD] for j in range(per_kv)], axis=0)
    query_pos = first + lax.broadcasted_iota(jnp.int32, (rows, KEY_CHUNK), 0) % BLOCK
    key_col = lax.broadcasted_iota(jnp.int32, (rows, KEY_CHUNK), 1)
    score_scale = 1.0 / HD**0.5

    def place(c):
        start = c * KEY_CHUNK
        return start, start // held, pl.multiple_of(start % held, KEY_CHUNK)

    def scores(c):
        start, at_slot, at_row = place(c)
        k = k_ref[at_slot, pl.ds(at_row, KEY_CHUNK), :]
        s = lax.dot_general(q, k, (((1,), (1,)), ((), ())), preferred_element_type=jnp.float32)
        return s * score_scale, start + key_col <= query_pos

    def top_of(c, top):
        s, visible = scores(c)
        return jnp.maximum(top, jnp.max(jnp.where(visible, s, NEG), axis=1, keepdims=True))

    top = lax.fori_loop(0, chunks, top_of, jnp.full((rows, 1), NEG, jnp.float32))

    def add_of(c, carry):
        total, acc = carry
        s, visible = scores(c)
        probs = jnp.where(visible, jnp.exp(s - top), 0.0)
        unused, at_slot, at_row = place(c)
        v = v_ref[at_slot, pl.ds(at_row, KEY_CHUNK), :]
        acc = acc + jnp.dot(probs.astype(jnp.bfloat16), v, preferred_element_type=jnp.float32)
        return (total + jnp.sum(probs, axis=1, keepdims=True), acc)

    start_carry = (jnp.zeros((rows, 1), jnp.float32), jnp.zeros((rows, HD), jnp.float32))
    total, acc = lax.fori_loop(0, chunks, add_of, start_carry)
    out = (acc / total).astype(o_ref.dtype)
    for j in range(per_kv):
        o_ref[:, j * HD : (j + 1) * HD] = out[j * BLOCK : (j + 1) * BLOCK]


def attention_core(queries, kv_piece):
    tok_rows, width = queries.shape
    slots, held, unused = kv_piece.shape
    kv_local = kv_piece.shape[2] // (2 * HD)
    group_width = width // kv_local
    keys = slots * held
    cost = pl.CostEstimate(
        flops=4 * tok_rows * width * keys,
        transcendentals=tok_rows * width * keys // HD,
        bytes_accessed=2 * (2 * queries.size + kv_piece.size),
    )
    return pl.pallas_call(
        attention_kernel,
        out_shape=jax.ShapeDtypeStruct(queries.shape, jnp.bfloat16),
        grid=(kv_local, slots),
        in_specs=[
            pl.BlockSpec((BLOCK, group_width), lambda g, s: (s, g)),
            pl.BlockSpec((slots, held, HD), lambda g, s: (0, 0, g)),
            pl.BlockSpec((slots, held, HD), lambda g, s: (0, 0, kv_local + g)),
        ],
        out_specs=pl.BlockSpec((BLOCK, group_width), lambda g, s: (s, g)),
        cost_estimate=cost,
    )(queries, kv_piece, kv_piece)


def local(x_in, step_size, a_log, d_skip, b_in, c_in, queries, key_rows, values):
    my_index = lax.axis_index("seq")
    seq_count = lax.axis_size("seq")
    tok_rows, width = x_in.shape
    slots = tok_rows // BLOCK
    heads = step_size.shape[0]
    kv_cat = jnp.concatenate(
        [key_rows.reshape(slots, BLOCK, -1), values.reshape(slots, BLOCK, -1)], axis=2
    )
    kv_piece = lax.all_gather(kv_cat, "seq", axis=1, tiled=True)
    rate = -jnp.exp(a_log)
    steps = step_size.reshape(heads, slots, BLOCK).transpose(1, 0, 2)
    cum = jnp.cumsum(steps * rate[None, :, None], axis=2)
    log_total = cum[:, :, -1]
    factor = (jnp.exp(log_total[:, :, None] - cum) * steps).transpose(0, 2, 1)
    b_blocks = b_in.reshape(slots, BLOCK, STATE)
    c_blocks = c_in.reshape(slots, BLOCK, STATE)
    block_state = block_states(b_blocks, factor, x_in)
    decay = jnp.exp(log_total)
    parts = 2 if heads % 2 == 0 else 1
    hooks = {
        (1, 0): (mamba_base, (x_in, steps, cum, b_blocks, c_blocks, d_skip)),
        (1, 1): (attention_core, (queries, kv_piece)),
    }
    incoming, results = entering_states(decay, block_state, seq_count, my_index, hooks, parts)
    c_wide = c_blocks.astype(jnp.float32)
    carried = jnp.concatenate(
        [
            jnp.einsum("ctn,cnk->ctk", c_wide, part, precision=lax.Precision.HIGHEST)
            for part in incoming
        ],
        axis=2,
    )
    carried_scale, base = results["mamba_base"]
    carried = carried * carried_scale
    mamba_out = (base + carried).astype(jnp.bfloat16).reshape(tok_rows, width)
    return (mamba_out, results["attention_core"])


def solution(mesh):
    in_specs = (
        P(("group", "seq"), "head"),
        P("head", ("group", "seq")),
        P("head"),
        P("head"),
        P(("group", "seq"), None),
        P(("group", "seq"), None),
        P(("group", "seq"), "head"),
        P(("group", "seq"), "head"),
        P(("group", "seq"), "head"),
    )
    out_specs = (P(("group", "seq"), "head"), P(("group", "seq"), "head"))
    return jax.shard_map(local, mesh=mesh, in_specs=in_specs, out_specs=out_specs, check_vma=False)
```

```python
import jax
import jax.numpy as jnp
from jax import lax
from jax.experimental import pallas as pl
from jax.experimental.pallas import tpu as pltpu
from jax.sharding import PartitionSpec as P

BLOCK = 128
HEADDIM = 64
STATE = 128
QHEADS = 16
KVHEADS = 4
HD = 128


NEG = -1e30


def spread(a):
    return jnp.repeat(a, HEADDIM, axis=-1)


def decay_scan(decay, count, mine):
    excl = jnp.ones_like(decay)
    total = decay
    steps = []
    span = 1
    while span < count:
        lower = (mine // span) % 2 == 1
        got = lax.ppermute(total, "seq", [(i, i ^ span) for i in range(count)])
        steps.append((lower, excl, total, got))
        excl = jnp.where(lower, got * excl, excl)
        total = total * got
        span *= 2
    return steps, excl, total


def entering_states(decay, block_state, count, mine, hooks, parts):
    steps, excl_decay, total_decay = decay_scan(decay, count, mine)
    heads, width = decay.shape[1], block_state.shape[2]
    head_cut, width_cut = heads // parts, width // parts
    totals = [block_state[:, :, j * width_cut : (j + 1) * width_cut] for j in range(parts)]
    excls = [jnp.zeros_like(t) for t in totals]
    results = {}
    span = 1
    for step, known_all in enumerate(steps):
        pairs = [(i, i ^ span) for i in range(count)]
        gots = []
        for j in range(parts):
            hook = hooks.get((j, step if step + 1 < len(steps) else -1))
            tie = gots[-1] if gots and step + 1 < len(steps) else ()
            totals[j], known, args, tie = lax.optimization_barrier(
                (totals[j], known_all, hook[1] if hook else (), tie)
            )
            if gots and step + 1 < len(steps):
                gots[-1] = tie
            got = lax.ppermute(totals[j].astype(jnp.bfloat16), "seq", pairs).astype(jnp.float32)
            if hook is not None:
                done = hook[0](*args)
                got, done = lax.optimization_barrier((got, done))
                results[hook[0].__name__] = done
            gots.append(got)
        lower = known_all[0]
        for j in range(parts):
            unused, excl_a, own_a, got_a = [
                v if v.ndim == 0 else v[:, j * head_cut : (j + 1) * head_cut] for v in known_all
            ]
            got = gots[j]
            excls[j] = jnp.where(lower, spread(excl_a)[:, None, :] * got + excls[j], excls[j])
            totals[j] = jnp.where(
                lower,
                spread(own_a)[:, None, :] * got + totals[j],
                spread(got_a)[:, None, :] * totals[j] + got,
            )
        span *= 2
    entering = []
    for j in range(parts):
        carry = jnp.zeros_like(totals[j][0])
        rows = []
        for slot in range(decay.shape[0]):
            a_excl = excl_decay[slot, j * head_cut : (j + 1) * head_cut]
            a_total = total_decay[slot, j * head_cut : (j + 1) * head_cut]
            rows.append(spread(a_excl)[None, :] * carry + excls[j][slot])
            carry = spread(a_total)[None, :] * carry + totals[j][slot]
        entering.append(jnp.stack(rows, axis=0))
    return (entering, results)


def mamba_base_kernel(x_ref, inner_ref, cum_ref, step_ref, skip_ref, o_ref):
    rows = lax.broadcasted_iota(jnp.int32, (BLOCK, BLOCK), 0)
    cols = lax.broadcasted_iota(jnp.int32, (BLOCK, BLOCK), 1)
    causal = rows >= cols
    inner = inner_ref[0]
    for e in range(cum_ref.shape[1]):
        cum_row = cum_ref[0, e]
        cum_col = jnp.sum(jnp.where(rows == cols, cum_row, 0.0), axis=1, keepdims=True)
        log_gap = jnp.where(causal, cum_col - cum_row, -jnp.inf)
        mixing = (inner * jnp.exp(log_gap) * step_ref[0, e]).astype(jnp.bfloat16)
        x_head = x_ref[:, e * HEADDIM : (e + 1) * HEADDIM]
        intra = jnp.dot(mixing, x_head, preferred_element_type=jnp.float32)
        skip = skip_ref[:, e * HEADDIM : (e + 1) * HEADDIM] * x_head.astype(jnp.float32)
        o_ref[0, :, e * HEADDIM : (e + 1) * HEADDIM] = intra + skip


def mamba_base(x_in, steps, cum, b_blocks, c_blocks, d_skip):
    slots, heads = steps.shape[:2]
    width = x_in.shape[1]
    group = 8 if heads % 8 == 0 else 128 // HEADDIM
    inner = jnp.einsum("cin,cjn->cij", c_blocks, b_blocks, preferred_element_type=jnp.float32)
    cum_row = cum[:, :, None, :]
    step_row = steps[:, :, None, :]
    skip_row = spread(d_skip)[None, :]
    cost = pl.CostEstimate(
        flops=2 * slots * heads * BLOCK * BLOCK * (HEADDIM + 3),
        transcendentals=slots * heads * BLOCK * BLOCK,
        bytes_accessed=x_in.size * 2 + slots * BLOCK * width * 4,
    )
    carried_scale = spread(jnp.exp(cum).transpose(0, 2, 1))
    return carried_scale, pl.pallas_call(
        mamba_base_kernel,
        out_shape=jax.ShapeDtypeStruct((slots, BLOCK, width), jnp.float32),
        grid=(slots, heads // group),
        in_specs=[
            pl.BlockSpec((BLOCK, group * HEADDIM), lambda c, g: (c, g)),
            pl.BlockSpec((1, BLOCK, BLOCK), lambda c, g: (c, 0, 0)),
            pl.BlockSpec((1, group, 1, BLOCK), lambda c, g: (c, g, 0, 0)),
            pl.BlockSpec((1, group, 1, BLOCK), lambda c, g: (c, g, 0, 0)),
            pl.BlockSpec((1, group * HEADDIM), lambda c, g: (0, g)),
        ],
        out_specs=pl.BlockSpec((1, BLOCK, group * HEADDIM), lambda c, g: (c, 0, g)),
        cost_estimate=cost,
    )(x_in, inner, cum_row, step_row, skip_row)


def block_state_kernel(b_ref, f_ref, x_ref, o_ref):
    scaled = (f_ref[0] * x_ref[...].astype(jnp.float32)).astype(jnp.bfloat16)
    o_ref[0] = jnp.dot(b_ref[0], scaled, preferred_element_type=jnp.float32)


def block_states(b_blocks, factor, x_in):
    slots, tokens, state = b_blocks.shape
    width = x_in.shape[1]
    cut = 512 if width % 512 == 0 else width
    b_t = b_blocks.transpose(0, 2, 1)
    spread_factor = spread(factor)
    cost = pl.CostEstimate(
        flops=2 * slots * state * tokens * width,
        transcendentals=0,
        bytes_accessed=x_in.size * 2 + spread_factor.size * 4 + slots * state * width * 4,
    )
    return pl.pallas_call(
        block_state_kernel,
        out_shape=jax.ShapeDtypeStruct((slots, state, width), jnp.float32),
        grid=(slots, width // cut),
        in_specs=[
            pl.BlockSpec((1, state, tokens), lambda c, k: (c, 0, 0)),
            pl.BlockSpec((1, tokens, cut), lambda c, k: (c, 0, k)),
            pl.BlockSpec((tokens, cut), lambda c, k: (c, k)),
        ],
        out_specs=pl.BlockSpec((1, state, cut), lambda c, k: (c, 0, k)),
        cost_estimate=cost,
    )(b_t, spread_factor, x_in)


KEY_CHUNK = 512


def attention_kernel(q_ref, k_ref, v_ref, o_ref):
    seq_count = lax.axis_size("seq")
    me = lax.axis_index("seq")
    slot = pl.program_id(1)
    per_kv = q_ref.shape[1] // HD
    rows = per_kv * BLOCK
    held = k_ref.shape[1]
    first = (slot * seq_count + me) * BLOCK
    chunks = (first + BLOCK + KEY_CHUNK - 1) // KEY_CHUNK
    q = jnp.concatenate([q_ref[:, j * HD : (j + 1) * HD] for j in range(per_kv)], axis=0)
    query_pos = first + lax.broadcasted_iota(jnp.int32, (rows, KEY_CHUNK), 0) % BLOCK
    key_col = lax.broadcasted_iota(jnp.int32, (rows, KEY_CHUNK), 1)
    score_scale = 1.0 / HD**0.5

    def place(c):
        start = c * KEY_CHUNK
        return start, start // held, pl.multiple_of(start % held, KEY_CHUNK)

    def scores(c):
        start, at_slot, at_row = place(c)
        k = k_ref[at_slot, pl.ds(at_row, KEY_CHUNK), :]
        s = lax.dot_general(q, k, (((1,), (1,)), ((), ())), preferred_element_type=jnp.float32)
        return s * score_scale, start + key_col <= query_pos

    def top_of(c, top):
        s, visible = scores(c)
        return jnp.maximum(top, jnp.max(jnp.where(visible, s, NEG), axis=1, keepdims=True))

    top = lax.fori_loop(0, chunks, top_of, jnp.full((rows, 1), NEG, jnp.float32))

    def add_of(c, carry):
        total, acc = carry
        s, visible = scores(c)
        probs = jnp.where(visible, jnp.exp(s - top), 0.0)
        unused, at_slot, at_row = place(c)
        v = v_ref[at_slot, pl.ds(at_row, KEY_CHUNK), :]
        acc = acc + jnp.dot(probs.astype(jnp.bfloat16), v, preferred_element_type=jnp.float32)
        return (total + jnp.sum(probs, axis=1, keepdims=True), acc)

    start_carry = (jnp.zeros((rows, 1), jnp.float32), jnp.zeros((rows, HD), jnp.float32))
    total, acc = lax.fori_loop(0, chunks, add_of, start_carry)
    out = (acc / total).astype(o_ref.dtype)
    for j in range(per_kv):
        o_ref[:, j * HD : (j + 1) * HD] = out[j * BLOCK : (j + 1) * BLOCK]


def attention_core(queries, kv_piece):
    tok_rows, width = queries.shape
    slots, held, unused = kv_piece.shape
    kv_local = kv_piece.shape[2] // (2 * HD)
    group_width = width // kv_local
    keys = slots * held
    cost = pl.CostEstimate(
        flops=4 * tok_rows * width * keys,
        transcendentals=tok_rows * width * keys // HD,
        bytes_accessed=2 * (2 * queries.size + kv_piece.size),
    )
    return pl.pallas_call(
        attention_kernel,
        out_shape=jax.ShapeDtypeStruct(queries.shape, jnp.bfloat16),
        grid=(kv_local, slots),
        in_specs=[
            pl.BlockSpec((BLOCK, group_width), lambda g, s: (s, g)),
            pl.BlockSpec((slots, held, HD), lambda g, s: (0, 0, g)),
            pl.BlockSpec((slots, held, HD), lambda g, s: (0, 0, kv_local + g)),
        ],
        out_specs=pl.BlockSpec((BLOCK, group_width), lambda g, s: (s, g)),
        cost_estimate=cost,
    )(queries, kv_piece, kv_piece)


def local(x_in, step_size, a_log, d_skip, b_in, c_in, queries, key_rows, values):
    my_index = lax.axis_index("seq")
    seq_count = lax.axis_size("seq")
    tok_rows, width = x_in.shape
    slots = tok_rows // BLOCK
    heads = step_size.shape[0]
    kv_cat = jnp.concatenate(
        [key_rows.reshape(slots, BLOCK, -1), values.reshape(slots, BLOCK, -1)], axis=2
    )
    kv_piece = lax.all_gather(kv_cat, "seq", axis=1, tiled=True)
    rate = -jnp.exp(a_log)
    steps = step_size.reshape(heads, slots, BLOCK).transpose(1, 0, 2)
    cum = jnp.cumsum(steps * rate[None, :, None], axis=2)
    log_total = cum[:, :, -1]
    factor = (jnp.exp(log_total[:, :, None] - cum) * steps).transpose(0, 2, 1)
    b_blocks = b_in.reshape(slots, BLOCK, STATE)
    c_blocks = c_in.reshape(slots, BLOCK, STATE)
    block_state = block_states(b_blocks, factor, x_in)
    decay = jnp.exp(log_total)
    parts = 2 if heads % 2 == 0 else 1
    hooks = {
        (1, 0): (mamba_base, (x_in, steps, cum, b_blocks, c_blocks, d_skip)),
        (1, 1): (attention_core, (queries, kv_piece)),
    }
    incoming, results = entering_states(decay, block_state, seq_count, my_index, hooks, parts)
    c_wide = c_blocks.astype(jnp.float32)
    carried = jnp.concatenate(
        [
            jnp.einsum("ctn,cnk->ctk", c_wide, part, precision=lax.Precision.HIGHEST)
            for part in incoming
        ],
        axis=2,
    )
    carried_scale, base = results["mamba_base"]
    carried = carried * carried_scale
    mamba_out = (base + carried).astype(jnp.bfloat16).reshape(tok_rows, width)
    return (mamba_out, results["attention_core"])


def solution(mesh):
    in_specs = (
        P(("group", "seq"), "head"),
        P("head", ("group", "seq")),
        P("head"),
        P("head"),
        P(("group", "seq"), None),
        P(("group", "seq"), None),
        P(("group", "seq"), "head"),
        P(("group", "seq"), "head"),
        P(("group", "seq"), "head"),
    )
    out_specs = (P(("group", "seq"), "head"), P(("group", "seq"), "head"))
    return jax.shard_map(local, mesh=mesh, in_specs=in_specs, out_specs=out_specs, check_vma=False)
```

```python
import jax
import jax.numpy as jnp
from jax import lax
from jax.experimental import pallas as pl
from jax.experimental.pallas import tpu as pltpu
from jax.sharding import PartitionSpec as P

BLOCK = 128
HEADDIM = 64
STATE = 128
QHEADS = 16
KVHEADS = 4
HD = 128


NEG = -1e30


def spread(a):
    return jnp.repeat(a, HEADDIM, axis=-1)


def decay_scan(decay, count, mine):
    excl = jnp.ones_like(decay)
    total = decay
    steps = []
    span = 1
    while span < count:
        lower = (mine // span) % 2 == 1
        got = lax.ppermute(total, "seq", [(i, i ^ span) for i in range(count)])
        steps.append((lower, excl, total, got))
        excl = jnp.where(lower, got * excl, excl)
        total = total * got
        span *= 2
    return steps, excl, total


def entering_states(decay, block_state, count, mine, hooks, parts):
    steps, excl_decay, total_decay = decay_scan(decay, count, mine)
    heads, width = decay.shape[1], block_state.shape[2]
    head_cut, width_cut = heads // parts, width // parts
    totals = [block_state[:, :, j * width_cut : (j + 1) * width_cut] for j in range(parts)]
    excls = [jnp.zeros_like(t) for t in totals]
    results = {}
    span = 1
    for step, known_all in enumerate(steps):
        pairs = [(i, i ^ span) for i in range(count)]
        gots = []
        for j in range(parts):
            hook = hooks.get((j, step if step + 1 < len(steps) else -1))
            tie = gots[-1] if gots and step + 1 < len(steps) else ()
            totals[j], known, args, tie = lax.optimization_barrier(
                (totals[j], known_all, hook[1] if hook else (), tie)
            )
            if gots and step + 1 < len(steps):
                gots[-1] = tie
            got = lax.ppermute(totals[j].astype(jnp.bfloat16), "seq", pairs).astype(jnp.float32)
            if hook is not None:
                done = hook[0](*args)
                got, done = lax.optimization_barrier((got, done))
                results[hook[0].__name__] = done
            gots.append(got)
        lower = known_all[0]
        for j in range(parts):
            unused, excl_a, own_a, got_a = [
                v if v.ndim == 0 else v[:, j * head_cut : (j + 1) * head_cut] for v in known_all
            ]
            got = gots[j]
            excls[j] = jnp.where(lower, spread(excl_a)[:, None, :] * got + excls[j], excls[j])
            totals[j] = jnp.where(
                lower,
                spread(own_a)[:, None, :] * got + totals[j],
                spread(got_a)[:, None, :] * totals[j] + got,
            )
        span *= 2
    entering = []
    for j in range(parts):
        carry = jnp.zeros_like(totals[j][0])
        rows = []
        for slot in range(decay.shape[0]):
            a_excl = excl_decay[slot, j * head_cut : (j + 1) * head_cut]
            a_total = total_decay[slot, j * head_cut : (j + 1) * head_cut]
            rows.append(spread(a_excl)[None, :] * carry + excls[j][slot])
            carry = spread(a_total)[None, :] * carry + totals[j][slot]
        entering.append(jnp.stack(rows, axis=0))
    return (entering, results)


def mamba_base_kernel(x_ref, inner_ref, cum_ref, step_ref, skip_ref, o_ref):
    rows = lax.broadcasted_iota(jnp.int32, (BLOCK, BLOCK), 0)
    cols = lax.broadcasted_iota(jnp.int32, (BLOCK, BLOCK), 1)
    causal = rows >= cols
    inner = inner_ref[0]
    for e in range(cum_ref.shape[1]):
        cum_row = cum_ref[0, e]
        cum_col = jnp.sum(jnp.where(rows == cols, cum_row, 0.0), axis=1, keepdims=True)
        log_gap = jnp.where(causal, cum_col - cum_row, -jnp.inf)
        mixing = (inner * jnp.exp(log_gap) * step_ref[0, e]).astype(jnp.bfloat16)
        x_head = x_ref[:, e * HEADDIM : (e + 1) * HEADDIM]
        intra = jnp.dot(mixing, x_head, preferred_element_type=jnp.float32)
        skip = skip_ref[:, e * HEADDIM : (e + 1) * HEADDIM] * x_head.astype(jnp.float32)
        o_ref[0, :, e * HEADDIM : (e + 1) * HEADDIM] = intra + skip


def mamba_base(x_in, steps, cum, b_blocks, c_blocks, d_skip):
    slots, heads = steps.shape[:2]
    width = x_in.shape[1]
    group = 8 if heads % 8 == 0 else 128 // HEADDIM
    inner = jnp.einsum("cin,cjn->cij", c_blocks, b_blocks, preferred_element_type=jnp.float32)
    cum_row = cum[:, :, None, :]
    step_row = steps[:, :, None, :]
    skip_row = spread(d_skip)[None, :]
    cost = pl.CostEstimate(
        flops=2 * slots * heads * BLOCK * BLOCK * (HEADDIM + 3),
        transcendentals=slots * heads * BLOCK * BLOCK,
        bytes_accessed=x_in.size * 2 + slots * BLOCK * width * 4,
    )
    carried_scale = spread(jnp.exp(cum).transpose(0, 2, 1))
    return carried_scale, pl.pallas_call(
        mamba_base_kernel,
        out_shape=jax.ShapeDtypeStruct((slots, BLOCK, width), jnp.float32),
        grid=(slots, heads // group),
        in_specs=[
            pl.BlockSpec((BLOCK, group * HEADDIM), lambda c, g: (c, g)),
            pl.BlockSpec((1, BLOCK, BLOCK), lambda c, g: (c, 0, 0)),
            pl.BlockSpec((1, group, 1, BLOCK), lambda c, g: (c, g, 0, 0)),
            pl.BlockSpec((1, group, 1, BLOCK), lambda c, g: (c, g, 0, 0)),
            pl.BlockSpec((1, group * HEADDIM), lambda c, g: (0, g)),
        ],
        out_specs=pl.BlockSpec((1, BLOCK, group * HEADDIM), lambda c, g: (c, 0, g)),
        cost_estimate=cost,
    )(x_in, inner, cum_row, step_row, skip_row)


def block_state_kernel(b_ref, f_ref, o_ref):
    o_ref[0] = jnp.dot(b_ref[0], f_ref[0], preferred_element_type=jnp.float32)


def block_states(b_blocks, factor, x_in):
    slots, tokens, state = b_blocks.shape
    width = x_in.shape[1]
    cut = 512 if width % 512 == 0 else width
    b_t = b_blocks.transpose(0, 2, 1)
    tokens_x = x_in.reshape(slots, tokens, width).astype(jnp.float32)
    spread_factor = (spread(factor) * tokens_x).astype(jnp.bfloat16)
    cost = pl.CostEstimate(
        flops=2 * slots * state * tokens * width,
        transcendentals=0,
        bytes_accessed=spread_factor.size * 2 + slots * state * width * 4,
    )
    return pl.pallas_call(
        block_state_kernel,
        out_shape=jax.ShapeDtypeStruct((slots, state, width), jnp.float32),
        grid=(slots, width // cut),
        in_specs=[
            pl.BlockSpec((1, state, tokens), lambda c, k: (c, 0, 0)),
            pl.BlockSpec((1, tokens, cut), lambda c, k: (c, 0, k)),
        ],
        out_specs=pl.BlockSpec((1, state, cut), lambda c, k: (c, 0, k)),
        cost_estimate=cost,
    )(b_t, spread_factor)


KEY_CHUNK = 256


def attention_kernel(q_ref, k_ref, v_ref, o_ref):
    seq_count = lax.axis_size("seq")
    me = lax.axis_index("seq")
    slot = pl.program_id(1)
    per_kv = q_ref.shape[1] // HD
    rows = per_kv * BLOCK
    held = k_ref.shape[1]
    first = (slot * seq_count + me) * BLOCK
    chunks = (first + BLOCK + KEY_CHUNK - 1) // KEY_CHUNK
    q = jnp.concatenate([q_ref[:, j * HD : (j + 1) * HD] for j in range(per_kv)], axis=0)
    query_pos = first + lax.broadcasted_iota(jnp.int32, (rows, KEY_CHUNK), 0) % BLOCK
    key_col = lax.broadcasted_iota(jnp.int32, (rows, KEY_CHUNK), 1)
    score_scale = 1.0 / HD**0.5

    def place(c):
        start = c * KEY_CHUNK
        return start, start // held, pl.multiple_of(start % held, KEY_CHUNK)

    def scores(c):
        start, at_slot, at_row = place(c)
        k = k_ref[at_slot, pl.ds(at_row, KEY_CHUNK), :]
        s = lax.dot_general(q, k, (((1,), (1,)), ((), ())), preferred_element_type=jnp.float32)
        return s * score_scale, start + key_col <= query_pos

    def top_of(c, top):
        s, visible = scores(c)
        return jnp.maximum(top, jnp.max(jnp.where(visible, s, NEG), axis=1, keepdims=True))

    top = lax.fori_loop(0, chunks, top_of, jnp.full((rows, 1), NEG, jnp.float32))

    def add_of(c, carry):
        total, acc = carry
        s, visible = scores(c)
        probs = jnp.where(visible, jnp.exp(s - top), 0.0)
        unused, at_slot, at_row = place(c)
        v = v_ref[at_slot, pl.ds(at_row, KEY_CHUNK), :]
        acc = acc + jnp.dot(probs.astype(jnp.bfloat16), v, preferred_element_type=jnp.float32)
        return (total + jnp.sum(probs, axis=1, keepdims=True), acc)

    start_carry = (jnp.zeros((rows, 1), jnp.float32), jnp.zeros((rows, HD), jnp.float32))
    total, acc = lax.fori_loop(0, chunks, add_of, start_carry)
    out = (acc / total).astype(o_ref.dtype)
    for j in range(per_kv):
        o_ref[:, j * HD : (j + 1) * HD] = out[j * BLOCK : (j + 1) * BLOCK]


def attention_core(queries, kv_piece):
    tok_rows, width = queries.shape
    slots, held, unused = kv_piece.shape
    kv_local = kv_piece.shape[2] // (2 * HD)
    group_width = width // kv_local
    keys = slots * held
    cost = pl.CostEstimate(
        flops=4 * tok_rows * width * keys,
        transcendentals=tok_rows * width * keys // HD,
        bytes_accessed=2 * (2 * queries.size + kv_piece.size),
    )
    return pl.pallas_call(
        attention_kernel,
        out_shape=jax.ShapeDtypeStruct(queries.shape, jnp.bfloat16),
        grid=(kv_local, slots),
        in_specs=[
            pl.BlockSpec((BLOCK, group_width), lambda g, s: (s, g)),
            pl.BlockSpec((slots, held, HD), lambda g, s: (0, 0, g)),
            pl.BlockSpec((slots, held, HD), lambda g, s: (0, 0, kv_local + g)),
        ],
        out_specs=pl.BlockSpec((BLOCK, group_width), lambda g, s: (s, g)),
        cost_estimate=cost,
    )(queries, kv_piece, kv_piece)


def local(x_in, step_size, a_log, d_skip, b_in, c_in, queries, key_rows, values):
    my_index = lax.axis_index("seq")
    seq_count = lax.axis_size("seq")
    tok_rows, width = x_in.shape
    slots = tok_rows // BLOCK
    heads = step_size.shape[0]
    kv_cat = jnp.concatenate(
        [key_rows.reshape(slots, BLOCK, -1), values.reshape(slots, BLOCK, -1)], axis=2
    )
    kv_piece = lax.all_gather(kv_cat, "seq", axis=1, tiled=True)
    rate = -jnp.exp(a_log)
    steps = step_size.reshape(heads, slots, BLOCK).transpose(1, 0, 2)
    cum = jnp.cumsum(steps * rate[None, :, None], axis=2)
    log_total = cum[:, :, -1]
    factor = (jnp.exp(log_total[:, :, None] - cum) * steps).transpose(0, 2, 1)
    b_blocks = b_in.reshape(slots, BLOCK, STATE)
    c_blocks = c_in.reshape(slots, BLOCK, STATE)
    block_state = block_states(b_blocks, factor, x_in)
    decay = jnp.exp(log_total)
    parts = 2 if heads % 2 == 0 else 1
    hooks = {
        (1, 0): (mamba_base, (x_in, steps, cum, b_blocks, c_blocks, d_skip)),
        (1, 1): (attention_core, (queries, kv_piece)),
    }
    incoming, results = entering_states(decay, block_state, seq_count, my_index, hooks, parts)
    c_wide = c_blocks.astype(jnp.float32)
    carried = jnp.concatenate(
        [
            jnp.einsum("ctn,cnk->ctk", c_wide, part, precision=lax.Precision.HIGHEST)
            for part in incoming
        ],
        axis=2,
    )
    carried_scale, base = results["mamba_base"]
    carried = carried * carried_scale
    mamba_out = (base + carried).astype(jnp.bfloat16).reshape(tok_rows, width)
    return (mamba_out, results["attention_core"])


def solution(mesh):
    in_specs = (
        P(("group", "seq"), "head"),
        P("head", ("group", "seq")),
        P("head"),
        P("head"),
        P(("group", "seq"), None),
        P(("group", "seq"), None),
        P(("group", "seq"), "head"),
        P(("group", "seq"), "head"),
        P(("group", "seq"), "head"),
    )
    out_specs = (P(("group", "seq"), "head"), P(("group", "seq"), "head"))
    return jax.shard_map(local, mesh=mesh, in_specs=in_specs, out_specs=out_specs, check_vma=False)
```

```python
import jax
import jax.numpy as jnp
from jax import lax
from jax.experimental import pallas as pl
from jax.experimental.pallas import tpu as pltpu
from jax.sharding import PartitionSpec as P

BLOCK = 128
HEADDIM = 64
STATE = 128
QHEADS = 16
KVHEADS = 4
HD = 128


NEG = -1e30


def spread(a):
    return jnp.repeat(a, HEADDIM, axis=-1)


def decay_scan(decay, count, mine):
    excl = jnp.ones_like(decay)
    total = decay
    steps = []
    span = 1
    while span < count:
        lower = (mine // span) % 2 == 1
        got = lax.ppermute(total, "seq", [(i, i ^ span) for i in range(count)])
        steps.append((lower, excl, total, got))
        excl = jnp.where(lower, got * excl, excl)
        total = total * got
        span *= 2
    return steps, excl, total


def entering_states(decay, block_state, count, mine, hooks, parts):
    steps, excl_decay, total_decay = decay_scan(decay, count, mine)
    heads, width = decay.shape[1], block_state.shape[2]
    head_cut, width_cut = heads // parts, width // parts
    totals = [block_state[:, :, j * width_cut : (j + 1) * width_cut] for j in range(parts)]
    excls = [jnp.zeros_like(t) for t in totals]
    results = {}
    span = 1
    for step, known_all in enumerate(steps):
        pairs = [(i, i ^ span) for i in range(count)]
        gots = []
        for j in range(parts):
            hook = hooks.get((j, step if step + 1 < len(steps) else -1))
            tie = gots[-1] if gots and step + 1 < len(steps) else ()
            waited = known_all if step > 0 else ()
            totals[j], known, args, tie = lax.optimization_barrier(
                (totals[j], waited, hook[1] if hook else (), tie)
            )
            if gots and step + 1 < len(steps):
                gots[-1] = tie
            got = lax.ppermute(totals[j].astype(jnp.bfloat16), "seq", pairs).astype(jnp.float32)
            if hook is not None:
                done = hook[0](*args)
                got, done = lax.optimization_barrier((got, done))
                results[hook[0].__name__] = done
            gots.append(got)
        lower = known_all[0]
        for j in range(parts):
            unused, excl_a, own_a, got_a = [
                v if v.ndim == 0 else v[:, j * head_cut : (j + 1) * head_cut] for v in known_all
            ]
            got = gots[j]
            excls[j] = jnp.where(lower, spread(excl_a)[:, None, :] * got + excls[j], excls[j])
            totals[j] = jnp.where(
                lower,
                spread(own_a)[:, None, :] * got + totals[j],
                spread(got_a)[:, None, :] * totals[j] + got,
            )
        span *= 2
    entering = []
    for j in range(parts):
        carry = jnp.zeros_like(totals[j][0])
        rows = []
        for slot in range(decay.shape[0]):
            a_excl = excl_decay[slot, j * head_cut : (j + 1) * head_cut]
            a_total = total_decay[slot, j * head_cut : (j + 1) * head_cut]
            rows.append(spread(a_excl)[None, :] * carry + excls[j][slot])
            carry = spread(a_total)[None, :] * carry + totals[j][slot]
        entering.append(jnp.stack(rows, axis=0))
    return (entering, results)


def mamba_base_kernel(x_ref, inner_ref, cum_ref, step_ref, skip_ref, o_ref):
    rows = lax.broadcasted_iota(jnp.int32, (BLOCK, BLOCK), 0)
    cols = lax.broadcasted_iota(jnp.int32, (BLOCK, BLOCK), 1)
    causal = rows >= cols
    inner = inner_ref[0]
    for e in range(cum_ref.shape[1]):
        cum_row = cum_ref[0, e]
        cum_col = jnp.sum(jnp.where(rows == cols, cum_row, 0.0), axis=1, keepdims=True)
        log_gap = jnp.where(causal, cum_col - cum_row, -jnp.inf)
        mixing = (inner * jnp.exp(log_gap) * step_ref[0, e]).astype(jnp.bfloat16)
        x_head = x_ref[:, e * HEADDIM : (e + 1) * HEADDIM]
        intra = jnp.dot(mixing, x_head, preferred_element_type=jnp.float32)
        skip = skip_ref[:, e * HEADDIM : (e + 1) * HEADDIM] * x_head.astype(jnp.float32)
        o_ref[0, :, e * HEADDIM : (e + 1) * HEADDIM] = intra + skip


def mamba_base(x_in, steps, cum, b_blocks, c_blocks, d_skip):
    slots, heads = steps.shape[:2]
    width = x_in.shape[1]
    group = 8 if heads % 8 == 0 else 128 // HEADDIM
    inner = jnp.einsum("cin,cjn->cij", c_blocks, b_blocks, preferred_element_type=jnp.float32)
    cum_row = cum[:, :, None, :]
    step_row = steps[:, :, None, :]
    skip_row = spread(d_skip)[None, :]
    cost = pl.CostEstimate(
        flops=2 * slots * heads * BLOCK * BLOCK * (HEADDIM + 3),
        transcendentals=slots * heads * BLOCK * BLOCK,
        bytes_accessed=x_in.size * 2 + slots * BLOCK * width * 4,
    )
    carried_scale = spread(jnp.exp(cum).transpose(0, 2, 1))
    return carried_scale, pl.pallas_call(
        mamba_base_kernel,
        out_shape=jax.ShapeDtypeStruct((slots, BLOCK, width), jnp.float32),
        grid=(slots, heads // group),
        in_specs=[
            pl.BlockSpec((BLOCK, group * HEADDIM), lambda c, g: (c, g)),
            pl.BlockSpec((1, BLOCK, BLOCK), lambda c, g: (c, 0, 0)),
            pl.BlockSpec((1, group, 1, BLOCK), lambda c, g: (c, g, 0, 0)),
            pl.BlockSpec((1, group, 1, BLOCK), lambda c, g: (c, g, 0, 0)),
            pl.BlockSpec((1, group * HEADDIM), lambda c, g: (0, g)),
        ],
        out_specs=pl.BlockSpec((1, BLOCK, group * HEADDIM), lambda c, g: (c, 0, g)),
        cost_estimate=cost,
    )(x_in, inner, cum_row, step_row, skip_row)


def block_state_kernel(b_ref, f_ref, x_ref, o_ref):
    scaled = (f_ref[0] * x_ref[...].astype(jnp.float32)).astype(jnp.bfloat16)
    o_ref[0] = jnp.dot(b_ref[0], scaled, preferred_element_type=jnp.float32)


def block_states(b_blocks, factor, x_in):
    slots, tokens, state = b_blocks.shape
    width = x_in.shape[1]
    cut = 512 if width % 512 == 0 else width
    b_t = b_blocks.transpose(0, 2, 1)
    spread_factor = spread(factor)
    cost = pl.CostEstimate(
        flops=2 * slots * state * tokens * width,
        transcendentals=0,
        bytes_accessed=x_in.size * 2 + spread_factor.size * 4 + slots * state * width * 4,
    )
    return pl.pallas_call(
        block_state_kernel,
        out_shape=jax.ShapeDtypeStruct((slots, state, width), jnp.float32),
        grid=(slots, width // cut),
        in_specs=[
            pl.BlockSpec((1, state, tokens), lambda c, k: (c, 0, 0)),
            pl.BlockSpec((1, tokens, cut), lambda c, k: (c, 0, k)),
            pl.BlockSpec((tokens, cut), lambda c, k: (c, k)),
        ],
        out_specs=pl.BlockSpec((1, state, cut), lambda c, k: (c, 0, k)),
        cost_estimate=cost,
    )(b_t, spread_factor, x_in)


KEY_CHUNK = 256


def attention_kernel(q_ref, k_ref, v_ref, o_ref):
    seq_count = lax.axis_size("seq")
    me = lax.axis_index("seq")
    slot = pl.program_id(1)
    per_kv = q_ref.shape[1] // HD
    rows = per_kv * BLOCK
    held = k_ref.shape[1]
    first = (slot * seq_count + me) * BLOCK
    chunks = (first + BLOCK + KEY_CHUNK - 1) // KEY_CHUNK
    q = jnp.concatenate([q_ref[:, j * HD : (j + 1) * HD] for j in range(per_kv)], axis=0)
    query_pos = first + lax.broadcasted_iota(jnp.int32, (rows, KEY_CHUNK), 0) % BLOCK
    key_col = lax.broadcasted_iota(jnp.int32, (rows, KEY_CHUNK), 1)
    score_scale = 1.0 / HD**0.5

    def place(c):
        start = c * KEY_CHUNK
        return start, start // held, pl.multiple_of(start % held, KEY_CHUNK)

    def scores(c):
        start, at_slot, at_row = place(c)
        k = k_ref[at_slot, pl.ds(at_row, KEY_CHUNK), :]
        s = lax.dot_general(q, k, (((1,), (1,)), ((), ())), preferred_element_type=jnp.float32)
        return s * score_scale, start + key_col <= query_pos

    def top_of(c, top):
        s, visible = scores(c)
        return jnp.maximum(top, jnp.max(jnp.where(visible, s, NEG), axis=1, keepdims=True))

    top = lax.fori_loop(0, chunks, top_of, jnp.full((rows, 1), NEG, jnp.float32))

    def add_of(c, carry):
        total, acc = carry
        s, visible = scores(c)
        probs = jnp.where(visible, jnp.exp(s - top), 0.0)
        unused, at_slot, at_row = place(c)
        v = v_ref[at_slot, pl.ds(at_row, KEY_CHUNK), :]
        acc = acc + jnp.dot(probs.astype(jnp.bfloat16), v, preferred_element_type=jnp.float32)
        return (total + jnp.sum(probs, axis=1, keepdims=True), acc)

    start_carry = (jnp.zeros((rows, 1), jnp.float32), jnp.zeros((rows, HD), jnp.float32))
    total, acc = lax.fori_loop(0, chunks, add_of, start_carry)
    out = (acc / total).astype(o_ref.dtype)
    for j in range(per_kv):
        o_ref[:, j * HD : (j + 1) * HD] = out[j * BLOCK : (j + 1) * BLOCK]


def attention_core(queries, kv_piece):
    tok_rows, width = queries.shape
    slots, held, unused = kv_piece.shape
    kv_local = kv_piece.shape[2] // (2 * HD)
    group_width = width // kv_local
    keys = slots * held
    cost = pl.CostEstimate(
        flops=4 * tok_rows * width * keys,
        transcendentals=tok_rows * width * keys // HD,
        bytes_accessed=2 * (2 * queries.size + kv_piece.size),
    )
    return pl.pallas_call(
        attention_kernel,
        out_shape=jax.ShapeDtypeStruct(queries.shape, jnp.bfloat16),
        grid=(kv_local, slots),
        in_specs=[
            pl.BlockSpec((BLOCK, group_width), lambda g, s: (s, g)),
            pl.BlockSpec((slots, held, HD), lambda g, s: (0, 0, g)),
            pl.BlockSpec((slots, held, HD), lambda g, s: (0, 0, kv_local + g)),
        ],
        out_specs=pl.BlockSpec((BLOCK, group_width), lambda g, s: (s, g)),
        cost_estimate=cost,
    )(queries, kv_piece, kv_piece)


def local(x_in, step_size, a_log, d_skip, b_in, c_in, queries, key_rows, values):
    my_index = lax.axis_index("seq")
    seq_count = lax.axis_size("seq")
    tok_rows, width = x_in.shape
    slots = tok_rows // BLOCK
    heads = step_size.shape[0]
    kv_cat = jnp.concatenate(
        [key_rows.reshape(slots, BLOCK, -1), values.reshape(slots, BLOCK, -1)], axis=2
    )
    kv_piece = lax.all_gather(kv_cat, "seq", axis=1, tiled=True)
    rate = -jnp.exp(a_log)
    steps = step_size.reshape(heads, slots, BLOCK).transpose(1, 0, 2)
    cum = jnp.cumsum(steps * rate[None, :, None], axis=2)
    log_total = cum[:, :, -1]
    factor = (jnp.exp(log_total[:, :, None] - cum) * steps).transpose(0, 2, 1)
    b_blocks = b_in.reshape(slots, BLOCK, STATE)
    c_blocks = c_in.reshape(slots, BLOCK, STATE)
    block_state = block_states(b_blocks, factor, x_in)
    decay = jnp.exp(log_total)
    parts = 2 if heads % 2 == 0 else 1
    hooks = {
        (1, 0): (mamba_base, (x_in, steps, cum, b_blocks, c_blocks, d_skip)),
        (1, 1): (attention_core, (queries, kv_piece)),
    }
    incoming, results = entering_states(decay, block_state, seq_count, my_index, hooks, parts)
    c_wide = c_blocks.astype(jnp.float32)
    carried = jnp.concatenate(
        [
            jnp.einsum("ctn,cnk->ctk", c_wide, part, precision=lax.Precision.HIGHEST)
            for part in incoming
        ],
        axis=2,
    )
    carried_scale, base = results["mamba_base"]
    carried = carried * carried_scale
    mamba_out = (base + carried).astype(jnp.bfloat16).reshape(tok_rows, width)
    return (mamba_out, results["attention_core"])


def solution(mesh):
    in_specs = (
        P(("group", "seq"), "head"),
        P("head", ("group", "seq")),
        P("head"),
        P("head"),
        P(("group", "seq"), None),
        P(("group", "seq"), None),
        P(("group", "seq"), "head"),
        P(("group", "seq"), "head"),
        P(("group", "seq"), "head"),
    )
    out_specs = (P(("group", "seq"), "head"), P(("group", "seq"), "head"))
    return jax.shard_map(local, mesh=mesh, in_specs=in_specs, out_specs=out_specs, check_vma=False)
```
